256 devices in a mesh: cells: 64 (over y, z, core), freq: 4 (over x).
Axes of the slice: x: 4, y: 4, z: 8, core: 2. Of those that a mesh axis runs over, the one named last changes fastest.
Arguments:
- adj_source: float32 [4, 2, 262144], P('freq', None, 'cells'), may hold values from -6 to 6
- contrast: float32 [4, 262144], P('freq', 'cells'), may hold values from 0.2 to 0.8
- background: float32 [4, 2, 262144], P('freq', None, 'cells'), may hold values from -6 to 6
- near_blocks: float32 [4, 2, 192, 262144], P('freq', None, None, 'cells'), may hold values from -0.3125 to 0.3125
- near_list: int32 [4096, 3], P('cells'), may hold values from 0 to 4095, as said below
- proj_basis: float32 [4, 2, 16, 262144], P('freq', None, None, 'cells'), may hold values from -0.5 to 0.5
- expand_basis: float32 [4, 2, 16, 262144], P('freq', None, None, 'cells'), may hold values from -1 to 1
- coupling: float32 [4, 2, 16, 16, 65536], P('freq', None, None, None, 'cells'), may hold values from -0.25 to 0.25
- far_owner: int32 [65536, 1], P('cells'), may hold values from 0 to 63; in each aligned block of 1024 rows (0 to 1023, 1024 to 2047, ...) at most 32 rows name the same one
- far_slot: int32 [65536], P('cells'), may hold values from 0 to 63
Outputs:
- adjoint: float32 [4, 2, 262144], P('freq', None, 'cells')
- gradient: float32 [262144], P('cells')
The draws below stay inside these ranges and needn't reach their ends.
Inputs may be any that keep to these rules, and one draw needn't show every extreme that they name: near_list[c, 0] = c, and every partner of c lies on the same device: near_list[c, k] // 64 == c // 64. `far_owner`: among the far pairs of one device's targets (aligned blocks of 1024 rows) at most 32 have sources on any one device.
All inputs are finite; a program needn't handle non-finite values.
Results may differ from the reference program's by a relative error of at most 0.0001.
Values sent between devices are 32-bit elements; how exact they have to be, the bound alone decides.
No kernel may reach another device: no remote copies, remote signals or barrier semaphores. Data moves between devices by JAX's collectives and lax.ppermute only.
A program may use at most 64 MiB of HBM per device.

```python
import math
import jax
import jax.numpy as jnp
import numpy as np
from jax import lax

CLS = 64
R = 16
NEAR = 3
FAR = 16
ITERS = 2
CL_DEV = 64
CLUSTERS = 4096
NCELLS = 262144
FREQS = 4
PAIRS = 65536
CAP = 32
N_CELLS = 64


def draw_near_list(key, part):
    rows = jnp.arange(CLUSTERS, dtype=jnp.int32)
    first = rows // CL_DEV * CL_DEV
    others = jax.random.randint(key, (CLUSTERS, NEAR - 1), 0, CL_DEV, dtype=jnp.int32)
    return jnp.concatenate([rows[:, None], first[:, None] + others], axis=1).astype(jnp.int32)


def with_ends(array, key, least, top_value):
    longest = array.shape.index(max(array.shape))
    spots = []
    for shift in (0, 1):
        where = [jax.random.randint(jax.random.fold_in(key, axis), (), 0, length) for axis, length in enumerate(array.shape)]
        where[longest] = (where[longest] + shift) % array.shape[longest]
        spots.append(tuple(where))
    return array.at[spots[0]].set(least).at[spots[1]].set(top_value)


def block_scale(own_key, extent, shards, low, high):
    loudness, own = 1.0, jax.random.fold_in(own_key, 6)
    for axis_at, parts in shards:
        draws = jnp.exp(jax.random.uniform(jax.random.fold_in(own, axis_at), (parts,), jnp.float32, low / len(shards), high / len(shards)))
        loudness = loudness * jnp.repeat(draws, extent[axis_at] // parts).reshape([-1 if axis == axis_at else 1 for axis in range(len(extent))])
    return loudness


def routed_block(rng, own, number, rows, number_of, top, reach, skew):
    order = jax.random.permutation(rng, number_of)
    packed, ordinary = load_shares(number_of, rows * top, reach, skew, True), load_shares(number_of, rows * top, reach, skew, False)
    places = jnp.arange(number_of)

    def named(tallies, offset_by):
        used = int((tallies > 0).sum())
        fixed = max(1, used // 4)
        moved = fixed + (places - fixed + offset_by * (used - fixed)) % max(1, number_of - fixed)
        return jnp.zeros((number_of,), jnp.int32).at[order[jnp.where(places < fixed, places, moved)]].set(jnp.asarray(tallies, jnp.int32))

    tallies = jnp.where(number % 4 == 0, named(packed, number // 4), named(ordinary, number - number // 4 - 1))
    mixed = jax.random.permutation(jax.random.fold_in(own, 3), number_of)
    source_of, receiver = mixed[0:number_of // 2 * 2:2], mixed[1:number_of // 2 * 2:2]
    slack = jnp.minimum(tallies[source_of] - 1, reach - tallies[receiver]) // 2
    slack = jnp.where((source_of == order[0]) | (receiver == order[0]) | (tallies[receiver] == 0), 0, jnp.maximum(slack, 0))
    moved = jax.random.randint(jax.random.fold_in(own, 4), (number_of // 2,), 0, 1 << 20) % (slack + 1)
    tallies = tallies.at[source_of].add(-moved).at[receiver].add(moved)
    items = jnp.searchsorted(jnp.cumsum(tallies), jnp.arange(rows * top), side="right").astype(jnp.int32)
    grid = items.reshape(top, rows).T
    grid = grid[jax.random.permutation(jax.random.fold_in(own, 1), rows)]
    offset_by = jax.random.randint(jax.random.fold_in(own, 2), (rows, 1), 0, top)
    return jnp.take_along_axis(grid, (jnp.arange(top)[None, :] + offset_by) % top, axis=1)


def load_shares(number_of, total, most, slope, full):
    portions = [(1 << 20) // math.isqrt(standing ** slope) + 1 for standing in range(1, number_of + 1)]
    largest = most if full else min(most, max(-(-total // number_of), total * portions[0] // sum(portions)))
    least = 1 if total - largest >= number_of - 1 else 0
    counts, rest = [largest] + [least] * (number_of - 1), total - largest - least * (number_of - 1)
    while rest > 0:
        movable = [i for i in range(1, number_of) if counts[i] < largest] or [i for i in range(1, number_of) if counts[i] < most]
        whole, remaining = sum([portions[i] for i in movable]), rest
        for i in movable:
            more = min(most - counts[i], max(1, remaining * portions[i] // whole), rest)
            counts[i] = counts[i] + more
            rest = rest - more
    return np.array(counts)


def normal_values(key, shape, scale, bound, pieces=(), kind=jnp.bfloat16):
    gain = block_scale(key, shape, pieces, -0.22, 0.18) if pieces else 1.0
    result = jax.random.normal(key, shape, jnp.float32) * scale * gain
    return jnp.minimum(jnp.maximum(result, -bound), bound).astype(kind)


def setup_inputs(seed: int = 0) -> dict:
    seeds = jax.random.split(jax.random.key(seed), 11)
    adj_source = normal_values(seeds[0], (FREQS, 2, NCELLS), 1.0, 6.0, ((0, 4), (2, 64)), jnp.float32)
    contrast = jnp.clip(0.2 + 0.6 * jax.random.uniform(seeds[1], (FREQS, NCELLS), jnp.float32) ** block_scale(seeds[1], (FREQS, NCELLS), ((0, 4), (1, 64)), -0.2, 0.2), 0.2, 0.8)
    background = normal_values(seeds[2], (FREQS, 2, NCELLS), 1.0, 6.0, ((0, 4), (2, 64)), jnp.float32)
    near_blocks = normal_values(seeds[3], (FREQS, 2, NEAR * CLS, NCELLS), (2 * NEAR * CLS) ** -0.5, 0.3125, ((0, 4), (3, 64)), jnp.float32)
    near_list = draw_near_list(jax.random.fold_in(seeds[10], 71), 0)
    proj_basis = normal_values(seeds[5], (FREQS, 2, R, NCELLS), (2 * CLS) ** -0.5, 0.5, ((0, 4), (3, 64)), jnp.float32)
    expand_basis = normal_values(seeds[6], (FREQS, 2, R, NCELLS), (2 * R) ** -0.5, 1.0, ((0, 4), (3, 64)), jnp.float32)
    coupling = normal_values(seeds[7], (FREQS, 2, R, R, PAIRS), (2 * R * FAR) ** -0.5, 0.25, ((0, 4), (4, 64)), jnp.float32)
    far_owner_keys = jax.random.split(jax.random.fold_in(seeds[8], 1), PAIRS // (CL_DEV * FAR))
    far_owner_turns = jax.random.permutation(jax.random.fold_in(seeds[8], 3), PAIRS // (CL_DEV * FAR))
    far_owner = jax.vmap(lambda own, number: routed_block(jax.random.fold_in(seeds[8], 2), own, number, CL_DEV * FAR, N_CELLS, 1, CAP, 2))(far_owner_keys, far_owner_turns).reshape((PAIRS, 1))
    far_slot = with_ends(jax.random.randint(seeds[9], (PAIRS,), 0, CL_DEV), jax.random.fold_in(seeds[9], 1), 0, CL_DEV - 1).astype(jnp.int32)
    return dict(adj_source=adj_source, contrast=contrast, background=background, near_blocks=near_blocks, near_list=near_list, proj_basis=proj_basis, expand_basis=expand_basis, coupling=coupling, far_owner=far_owner, far_slot=far_slot)


def apply_green(f, field, contrast, near_blocks, near_list, proj_basis, expand_basis, coupling, source):
    highest = lax.Precision.HIGHEST
    weighted = contrast[f][None, :] * field
    grouped = weighted.reshape(2, CLUSTERS, CLS)
    partner = grouped[:, near_list, :].reshape(2, CLUSTERS, NEAR * CLS)
    blocks = near_blocks[f].reshape(2, NEAR * CLS, CLUSTERS, CLS)

    def nearprod(a, b):
        return jnp.einsum('jct,cj->ct', a, b, precision=highest)

    near_re = nearprod(blocks[0], partner[0]) - nearprod(blocks[1], partner[1])
    near_im = nearprod(blocks[0], partner[1]) + nearprod(blocks[1], partner[0])
    basis_in = proj_basis[f].reshape(2, R, CLUSTERS, CLS)

    def project(a, b):
        return jnp.einsum('rci,ci->rc', a, b, precision=highest)

    coef_re = project(basis_in[0], grouped[0]) - project(basis_in[1], grouped[1])
    coef_im = project(basis_in[0], grouped[1]) + project(basis_in[1], grouped[0])
    pair_re = coef_re[:, source]
    pair_im = coef_im[:, source]
    mats = coupling[f]

    def couple(a, b):
        return jnp.einsum('oip,ip->op', a, b, precision=highest)

    out_re = couple(mats[0], pair_re) - couple(mats[1], pair_im)
    out_im = couple(mats[0], pair_im) + couple(mats[1], pair_re)
    out_re = out_re.reshape(R, CLUSTERS, FAR).sum(axis=2)
    out_im = out_im.reshape(R, CLUSTERS, FAR).sum(axis=2)
    basis_out = expand_basis[f].reshape(2, R, CLUSTERS, CLS)

    def expand(a, b):
        return jnp.einsum('rct,rc->ct', a, b, precision=highest)

    far_re = expand(basis_out[0], out_re) - expand(basis_out[1], out_im)
    far_im = expand(basis_out[0], out_im) + expand(basis_out[1], out_re)
    return jnp.stack([near_re + far_re, near_im + far_im]).reshape(2, NCELLS)


def reference(adj_source, contrast, background, near_blocks, near_list, proj_basis, expand_basis, coupling, far_owner, far_slot):
    source = far_owner[:, 0] * CL_DEV + far_slot
    fields = []
    for f in range(FREQS):
        field = adj_source[f]
        for step in range(ITERS):
            field = adj_source[f] + apply_green(f, field, contrast, near_blocks, near_list, proj_basis, expand_basis, coupling, source)
        fields.append(field)
    adjoint = jnp.stack(fields)
    gradient = jnp.sum(background[:, 0] * adjoint[:, 0] + background[:, 1] * adjoint[:, 1], axis=0)
    return adjoint, gradient
```

```python
import jax
import jax.numpy as jnp
from jax import lax
from jax.experimental import pallas as pl
from jax.experimental.pallas import tpu as pltpu
from jax.sharding import PartitionSpec as P

ITERS = 2
F32 = jnp.float32
BF16 = jnp.bfloat16
CHUNK = 512
PAIR_CHUNK = 128
VMEM_LIMIT = 56 * 1024 * 1024


def _split3(a):
    hi = a.astype(BF16)
    r = a - hi.astype(F32)
    mid = r.astype(BF16)
    lo = (r - mid.astype(F32)).astype(BF16)
    return jnp.concatenate([hi, mid, lo], axis=0)


def _sdot(split, onehot):
    m = split.shape[0] // 3
    r = jnp.dot(split, onehot, preferred_element_type=F32)
    return r[:m] + r[m : 2 * m] + r[2 * m :]


def _xdot(a, onehot):
    return _sdot(_split3(a), onehot)


def _iota(shape, dim):
    return lax.broadcasted_iota(jnp.int32, shape, dim)


def _weighted_proj(u, c, pre, pim):
    wre = u[0:1] * c
    wim = u[1:2] * c
    return jnp.concatenate([pre * wre - pim * wim, pre * wim + pim * wre], axis=0)


def _proj_chunk(pw, off, clusters, width):
    n = pw.shape[1]
    seg = ((_iota((n, clusters), 0) + off) // width) == _iota((n, clusters), 1)
    return _xdot(pw, seg.astype(BF16))


def _send_of(q, rr_ref, clusters):
    nsend = rr_ref.shape[1]
    oh = (_iota((clusters, nsend), 0) == rr_ref[...]).astype(BF16)
    return _xdot(q, oh)


def _proj_kernel(u_ref, c_ref, p_ref, rr_ref, send_ref):
    cells = u_ref.shape[1]
    clusters = cells // 64
    rank2 = 2 * p_ref.shape[1]

    def body(ci, q):
        off = pl.multiple_of(ci * CHUNK, CHUNK)
        sl = pl.ds(off, CHUNK)
        pw = _weighted_proj(u_ref[:, sl], c_ref[:, sl], p_ref[0, :, sl], p_ref[1, :, sl])
        return q + _proj_chunk(pw, off, clusters, 64)

    q = lax.fori_loop(0, cells // CHUNK, body, jnp.zeros((rank2, clusters), F32))
    send_ref[...] = _send_of(q, rr_ref, clusters)


def _near_kernel(u_ref, c_ref, nb_ref, nlc_ref, base_ref, out_ref):
    cells = u_ref.shape[1]
    width = 64
    clusters = cells // width
    near = nlc_ref.shape[0]

    def wt_body(ci, acc):
        off = pl.multiple_of(ci * CHUNK, CHUNK)
        sl = pl.ds(off, CHUNK)
        w = u_ref[:, sl] * c_ref[:, sl]
        sel = _iota((width, CHUNK), 0) == ((_iota((width, CHUNK), 1) + off) % width)
        wm = jnp.concatenate(
            [jnp.where(sel, w[0:1], 0.0), jnp.where(sel, w[1:2], 0.0)], axis=0
        )
        seg = ((_iota((CHUNK, clusters), 0) + off) // width) == _iota((CHUNK, clusters), 1)
        return acc + _xdot(wm, seg.astype(BF16))

    wt = lax.fori_loop(0, cells // CHUNK, wt_body, jnp.zeros((2 * width, clusters), F32))
    wt_split = _split3(wt)

    def near_body(ci, carry):
        off = pl.multiple_of(ci * CHUNK, CHUNK)
        sl = pl.ds(off, CHUNK)
        crow = _iota((clusters, CHUNK), 0)
        acc_re = jnp.zeros((1, CHUNK), F32)
        acc_im = jnp.zeros((1, CHUNK), F32)
        for k in range(near):
            m = (crow == nlc_ref[k : k + 1, sl]).astype(BF16)
            wk = _sdot(wt_split, m)
            wre = wk[:width]
            wim = wk[width:]
            nre = nb_ref[0, pl.ds(k * width, width), sl]
            nim = nb_ref[1, pl.ds(k * width, width), sl]
            acc_re = acc_re + jnp.sum(nre * wre - nim * wim, axis=0, keepdims=True)
            acc_im = acc_im + jnp.sum(nre * wim + nim * wre, axis=0, keepdims=True)
        out_ref[:, sl] = base_ref[:, sl] + jnp.concatenate([acc_re, acc_im], axis=0)
        return carry

    lax.fori_loop(0, cells // CHUNK, near_body, 0)


def _far_common(part_ref, recv_ref, idx_ref, cpl_ref, e_ref, u_ref, chunk_tail):
    cells = part_ref.shape[1]
    width = 64
    clusters = cells // width
    rank = cpl_ref.shape[1]
    npairs = idx_ref.shape[1]
    far = npairs // clusters
    nrecv = recv_ref.shape[1]
    rsplit = _split3(recv_ref[...])

    def pair_body(pj, z):
        off = pl.multiple_of(pj * PAIR_CHUNK, PAIR_CHUNK)
        sl = pl.ds(off, PAIR_CHUNK)
        g = (_iota((nrecv, PAIR_CHUNK), 0) == idx_ref[:, sl]).astype(BF16)
        qs = _sdot(rsplit, g)
        qre = qs[:rank][None]
        qim = qs[rank:][None]
        cre = cpl_ref[0, :, :, sl]
        cim = cpl_ref[1, :, :, sl]
        zre = jnp.sum(cre * qre - cim * qim, axis=1)
        zim = jnp.sum(cre * qim + cim * qre, axis=1)
        seg = ((_iota((PAIR_CHUNK, clusters), 0) + off) // far) == _iota((PAIR_CHUNK, clusters), 1)
        return z + _xdot(jnp.concatenate([zre, zim], axis=0), seg.astype(BF16))

    z = lax.fori_loop(0, npairs // PAIR_CHUNK, pair_body, jnp.zeros((2 * rank, clusters), F32))
    z_split = _split3(z)

    def cell_body(ci, acc):
        off = pl.multiple_of(ci * CHUNK, CHUNK)
        sl = pl.ds(off, CHUNK)
        spread = _iota((clusters, CHUNK), 0) == ((_iota((clusters, CHUNK), 1) + off) // width)
        zz = _sdot(z_split, spread.astype(BF16))
        zre = zz[:rank]
        zim = zz[rank:]
        ere = e_ref[0, :, sl]
        eim = e_ref[1, :, sl]
        far_re = jnp.sum(ere * zre - eim * zim, axis=0, keepdims=True)
        far_im = jnp.sum(ere * zim + eim * zre, axis=0, keepdims=True)
        u = part_ref[:, sl] + jnp.concatenate([far_re, far_im], axis=0)
        u_ref[:, sl] = u
        return chunk_tail(u, off, sl, acc)

    return cell_body


def _far_proj_kernel(part_ref, recv_ref, idx_ref, cpl_ref, e_ref, c_ref, p_ref, rr_ref, u_ref, send_ref):
    cells = part_ref.shape[1]
    clusters = cells // 64
    rank2 = 2 * p_ref.shape[1]

    def tail(u, off, sl, q):
        pw = _weighted_proj(u, c_ref[:, sl], p_ref[0, :, sl], p_ref[1, :, sl])
        return q + _proj_chunk(pw, off, clusters, 64)

    body = _far_common(part_ref, recv_ref, idx_ref, cpl_ref, e_ref, u_ref, tail)
    q = lax.fori_loop(0, cells // CHUNK, body, jnp.zeros((rank2, clusters), F32))
    send_ref[...] = _send_of(q, rr_ref, clusters)


def _far_grad_kernel(part_ref, recv_ref, idx_ref, cpl_ref, e_ref, bg_ref, u_ref, t_ref):
    cells = part_ref.shape[1]

    def tail(u, off, sl, acc):
        bg = bg_ref[:, sl]
        t_ref[:, sl] = bg[0:1] * u[0:1] + bg[1:2] * u[1:2]
        return acc

    body = _far_common(part_ref, recv_ref, idx_ref, cpl_ref, e_ref, u_ref, tail)
    lax.fori_loop(0, cells // CHUNK, body, 0)


def _call(kernel, outs, args, flops, name):
    leaves = outs if isinstance(outs, tuple) else (outs,)
    nbytes = sum(a.size * a.dtype.itemsize for a in args) + sum(
        o.size * jnp.dtype(o.dtype).itemsize for o in leaves
    )
    return pl.pallas_call(
        kernel,
        out_shape=outs,
        compiler_params=pltpu.CompilerParams(vmem_limit_bytes=VMEM_LIMIT),
        cost_estimate=pl.CostEstimate(flops=flops, bytes_accessed=nbytes, transcendentals=0),
        name=name,
    )(*args)


def _exchange(send, devices):
    rows, total = send.shape
    slots = total // devices
    got = lax.all_to_all(send.reshape(rows, devices, slots), "cells", 1, 1, tiled=True)
    return got.reshape(rows, total)


def per_device(
    adj_source,
    contrast,
    background,
    near_blocks,
    near_list,
    proj_basis,
    expand_basis,
    coupling,
    far_owner,
    far_slot,
):
    devices = lax.axis_size("cells")
    clusters = near_list.shape[0]
    cells = contrast.shape[1]
    width = cells // clusters
    npairs = far_slot.shape[0]
    cap = 32

    src = adj_source[0]
    cst = contrast
    nb = near_blocks[0]
    pb = proj_basis[0]
    eb = expand_basis[0]
    cp = coupling[0]
    bg = background[0]

    me = lax.axis_index("cells")
    local_list = near_list - me * clusters
    nlc = jnp.repeat(local_list.T, width, axis=1)

    owner = far_owner[:, 0]
    slot = far_slot
    onehot = (owner[:, None] == jnp.arange(devices, dtype=jnp.int32)[None, :]).astype(jnp.int32)
    before = jnp.cumsum(onehot, axis=0) - onehot
    pos = jnp.sum(before * onehot, axis=1)
    idx = (owner * cap + pos)[None, :].astype(jnp.int32)
    req = jnp.zeros((devices, cap), jnp.int32).at[owner, pos].set(slot)
    rr = lax.all_to_all(req, "cells", 0, 0, tiled=True).reshape(1, devices * cap)

    nsend = devices * cap
    rank2 = 2 * pb.shape[1]
    send_shape = jax.ShapeDtypeStruct((rank2, nsend), F32)
    field_shape = jax.ShapeDtypeStruct((2, cells), F32)

    send = _call(_proj_kernel, send_shape, (src, cst, pb, rr), 4 * rank2 * cells, "proj")
    field = src
    for step in range(ITERS):
        recv = _exchange(send, devices)
        part = _call(
            _near_kernel, field_shape, (field, cst, nb, nlc, src), 8 * nb.shape[1] * cells, "near"
        )
        if step < ITERS - 1:
            field, send = _call(
                _far_proj_kernel,
                (field_shape, send_shape),
                (part, recv, idx, cp, eb, cst, pb, rr),
                8 * cp.size,
                "far_proj",
            )
        else:
            field, terms = _call(
                _far_grad_kernel,
                (field_shape, jax.ShapeDtypeStruct((1, cells), F32)),
                (part, recv, idx, cp, eb, bg),
                8 * cp.size,
                "far_grad",
            )
    freqs = lax.axis_size("freq")
    total = terms[0]
    hop = 1
    while hop < freqs:
        total = total + lax.ppermute(total, "freq", [(i, i ^ hop) for i in range(freqs)])
        hop *= 2
    return (field[None], total)


def solution(mesh):
    return jax.shard_map(
        per_device,
        mesh=mesh,
        in_specs=(
            P("freq", None, "cells"),
            P("freq", "cells"),
            P("freq", None, "cells"),
            P("freq", None, None, "cells"),
            P("cells", None),
            P("freq", None, None, "cells"),
            P("freq", None, None, "cells"),
            P("freq", None, None, None, "cells"),
            P("cells", None),
            P("cells"),
        ),
        out_specs=(P("freq", None, "cells"), P("cells")),
        check_vma=False,
    )
```

```python
import jax
import jax.numpy as jnp
from jax import lax
from jax.experimental import pallas as pl
from jax.experimental.pallas import tpu as pltpu
from jax.sharding import PartitionSpec as P

ITERS = 2
F32 = jnp.float32
BF16 = jnp.bfloat16
CHUNK = 512
PAIR_CHUNK = 128
VMEM_LIMIT = 56 * 1024 * 1024


def _split3(a):
    hi = a.astype(BF16)
    r = a - hi.astype(F32)
    mid = r.astype(BF16)
    lo = (r - mid.astype(F32)).astype(BF16)
    return jnp.concatenate([hi, mid, lo], axis=0)


def _sdot(split, onehot):
    m = split.shape[0] // 3
    r = jnp.dot(split, onehot, preferred_element_type=F32)
    return r[:m] + r[m : 2 * m] + r[2 * m :]


def _xdot(a, onehot):
    return _sdot(_split3(a), onehot)


def _iota(shape, dim):
    return lax.broadcasted_iota(jnp.int32, shape, dim)


def _weighted_proj(u, c, pre, pim):
    wre = u[0:1] * c
    wim = u[1:2] * c
    return jnp.concatenate([pre * wre - pim * wim, pre * wim + pim * wre], axis=0)


def _proj_chunk(pw, off, clusters, width):
    n = pw.shape[1]
    seg = ((_iota((n, clusters), 0) + off) // width) == _iota((n, clusters), 1)
    return _xdot(pw, seg.astype(BF16))


def _send_of(q, rr_ref, clusters):
    nsend = rr_ref.shape[1]
    oh = (_iota((clusters, nsend), 0).astype(F32) == rr_ref[...]).astype(BF16)
    return _xdot(q, oh)


def _proj_kernel(u_ref, c_ref, p_ref, rr_ref, send_ref):
    cells = u_ref.shape[1]
    clusters = cells // 64
    rank2 = 2 * p_ref.shape[1]

    def body(ci, q):
        off = pl.multiple_of(ci * CHUNK, CHUNK)
        sl = pl.ds(off, CHUNK)
        pw = _weighted_proj(u_ref[:, sl], c_ref[:, sl], p_ref[0, :, sl], p_ref[1, :, sl])
        return q + _proj_chunk(pw, off, clusters, 64)

    q = lax.fori_loop(0, cells // CHUNK, body, jnp.zeros((rank2, clusters), F32))
    send_ref[...] = _send_of(q, rr_ref, clusters)


def _near_kernel(u_ref, c_ref, nb_ref, nlc_ref, base_ref, out_ref):
    cells = u_ref.shape[1]
    width = 64
    clusters = cells // width
    near = nlc_ref.shape[0]

    def wt_body(ci, acc):
        off = pl.multiple_of(ci * CHUNK, CHUNK)
        sl = pl.ds(off, CHUNK)
        w = u_ref[:, sl] * c_ref[:, sl]
        sel = _iota((width, CHUNK), 0) == ((_iota((width, CHUNK), 1) + off) % width)
        wm = jnp.concatenate(
            [jnp.where(sel, w[0:1], 0.0), jnp.where(sel, w[1:2], 0.0)], axis=0
        )
        seg = ((_iota((CHUNK, clusters), 0) + off) // width) == _iota((CHUNK, clusters), 1)
        return acc + _xdot(wm, seg.astype(BF16))

    wt = lax.fori_loop(0, cells // CHUNK, wt_body, jnp.zeros((2 * width, clusters), F32))
    wt_split = _split3(wt)

    def near_body(ci, carry):
        off = pl.multiple_of(ci * CHUNK, CHUNK)
        sl = pl.ds(off, CHUNK)
        crow = _iota((clusters, CHUNK), 0)
        acc_re = jnp.zeros((1, CHUNK), F32)
        acc_im = jnp.zeros((1, CHUNK), F32)
        for k in range(near):
            m = (crow == nlc_ref[k : k + 1, sl]).astype(BF16)
            wk = _sdot(wt_split, m)
            wre = wk[:width]
            wim = wk[width:]
            nre = nb_ref[0, pl.ds(k * width, width), sl]
            nim = nb_ref[1, pl.ds(k * width, width), sl]
            acc_re = acc_re + jnp.sum(nre * wre - nim * wim, axis=0, keepdims=True)
            acc_im = acc_im + jnp.sum(nre * wim + nim * wre, axis=0, keepdims=True)
        out_ref[:, sl] = base_ref[:, sl] + jnp.concatenate([acc_re, acc_im], axis=0)
        return carry

    lax.fori_loop(0, cells // CHUNK, near_body, 0)


def _far_common(part_ref, recv_ref, idx_ref, cpl_ref, e_ref, u_ref, chunk_tail):
    cells = part_ref.shape[1]
    width = 64
    clusters = cells // width
    rank = cpl_ref.shape[1]
    npairs = idx_ref.shape[1]
    far = npairs // clusters
    nrecv = recv_ref.shape[1]
    rsplit = _split3(recv_ref[...])

    def pair_body(pj, z):
        off = pl.multiple_of(pj * PAIR_CHUNK, PAIR_CHUNK)
        sl = pl.ds(off, PAIR_CHUNK)
        g = (_iota((nrecv, PAIR_CHUNK), 0) == idx_ref[:, sl]).astype(BF16)
        qs = _sdot(rsplit, g)
        qre = qs[:rank][None]
        qim = qs[rank:][None]
        cre = cpl_ref[0, :, :, sl]
        cim = cpl_ref[1, :, :, sl]
        zre = jnp.sum(cre * qre - cim * qim, axis=1)
        zim = jnp.sum(cre * qim + cim * qre, axis=1)
        seg = ((_iota((PAIR_CHUNK, clusters), 0) + off) // far) == _iota((PAIR_CHUNK, clusters), 1)
        return z + _xdot(jnp.concatenate([zre, zim], axis=0), seg.astype(BF16))

    z = lax.fori_loop(0, npairs // PAIR_CHUNK, pair_body, jnp.zeros((2 * rank, clusters), F32))
    z_split = _split3(z)

    def cell_body(ci, acc):
        off = pl.multiple_of(ci * CHUNK, CHUNK)
        sl = pl.ds(off, CHUNK)
        spread = _iota((clusters, CHUNK), 0) == ((_iota((clusters, CHUNK), 1) + off) // width)
        zz = _sdot(z_split, spread.astype(BF16))
        zre = zz[:rank]
        zim = zz[rank:]
        ere = e_ref[0, :, sl]
        eim = e_ref[1, :, sl]
        far_re = jnp.sum(ere * zre - eim * zim, axis=0, keepdims=True)
        far_im = jnp.sum(ere * zim + eim * zre, axis=0, keepdims=True)
        u = part_ref[:, sl] + jnp.concatenate([far_re, far_im], axis=0)
        u_ref[:, sl] = u
        return chunk_tail(u, off, sl, acc)

    return cell_body


def _far_proj_kernel(part_ref, recv_ref, idx_ref, cpl_ref, e_ref, c_ref, p_ref, rr_ref, u_ref, send_ref):
    cells = part_ref.shape[1]
    clusters = cells // 64
    rank2 = 2 * p_ref.shape[1]

    def tail(u, off, sl, q):
        pw = _weighted_proj(u, c_ref[:, sl], p_ref[0, :, sl], p_ref[1, :, sl])
        return q + _proj_chunk(pw, off, clusters, 64)

    body = _far_common(part_ref, recv_ref, idx_ref, cpl_ref, e_ref, u_ref, tail)
    q = lax.fori_loop(0, cells // CHUNK, body, jnp.zeros((rank2, clusters), F32))
    send_ref[...] = _send_of(q, rr_ref, clusters)


def _far_grad_kernel(part_ref, recv_ref, idx_ref, cpl_ref, e_ref, bg_ref, u_ref, t_ref):
    cells = part_ref.shape[1]

    def tail(u, off, sl, acc):
        bg = bg_ref[:, sl]
        t_ref[:, sl] = bg[0:1] * u[0:1] + bg[1:2] * u[1:2]
        return acc

    body = _far_common(part_ref, recv_ref, idx_ref, cpl_ref, e_ref, u_ref, tail)
    lax.fori_loop(0, cells // CHUNK, body, 0)


def _prep_kernel(or_ref, sr_ref, idx_ref, req_ref):
    n = or_ref.shape[1]
    devices, cap = req_ref.shape
    oht = _iota((devices, n), 0) == or_ref[...]
    upper = (_iota((n, n), 0) < _iota((n, n), 1)).astype(BF16)
    counts = jnp.dot(oht.astype(BF16), upper, preferred_element_type=F32)
    pos = jnp.sum(jnp.where(oht, counts, 0.0), axis=0, keepdims=True).astype(jnp.int32)
    idx_ref[...] = or_ref[...] * cap + pos
    pkt = (_iota((cap, n), 0) == pos).astype(BF16)
    ohs = jnp.where(oht, sr_ref[...].astype(F32), 0.0).astype(BF16)
    req_ref[...] = lax.dot_general(
        ohs, pkt, (((1,), (1,)), ((), ())), preferred_element_type=F32
    )


def _call(kernel, outs, args, flops, name):
    leaves = outs if isinstance(outs, tuple) else (outs,)
    nbytes = sum(a.size * a.dtype.itemsize for a in args) + sum(
        o.size * jnp.dtype(o.dtype).itemsize for o in leaves
    )
    return pl.pallas_call(
        kernel,
        out_shape=outs,
        compiler_params=pltpu.CompilerParams(vmem_limit_bytes=VMEM_LIMIT),
        cost_estimate=pl.CostEstimate(flops=flops, bytes_accessed=nbytes, transcendentals=0),
        name=name,
    )(*args)


def _exchange(send, devices):
    rows, total = send.shape
    slots = total // devices
    got = lax.all_to_all(send.reshape(rows, devices, slots), "cells", 1, 1, tiled=True)
    return got.reshape(rows, total)


def per_device(
    adj_source,
    contrast,
    background,
    near_blocks,
    near_list,
    proj_basis,
    expand_basis,
    coupling,
    far_owner,
    far_slot,
):
    devices = lax.axis_size("cells")
    clusters = near_list.shape[0]
    cells = contrast.shape[1]
    width = cells // clusters
    npairs = far_slot.shape[0]
    cap = 32

    src = adj_source[0]
    cst = contrast
    nb = near_blocks[0]
    pb = proj_basis[0]
    eb = expand_basis[0]
    cp = coupling[0]
    bg = background[0]

    me = lax.axis_index("cells")
    local_list = near_list - me * clusters
    nlc = jnp.repeat(local_list.T, width, axis=1)

    idx, req = _call(
        _prep_kernel,
        (
            jax.ShapeDtypeStruct((1, npairs), jnp.int32),
            jax.ShapeDtypeStruct((devices, cap), F32),
        ),
        (far_owner.reshape(1, npairs), far_slot.reshape(1, npairs)),
        2 * devices * npairs * npairs,
        "prep",
    )
    rr = lax.all_to_all(req, "cells", 0, 0, tiled=True).reshape(1, devices * cap)

    nsend = devices * cap
    rank2 = 2 * pb.shape[1]
    send_shape = jax.ShapeDtypeStruct((rank2, nsend), F32)
    field_shape = jax.ShapeDtypeStruct((2, cells), F32)

    send = _call(_proj_kernel, send_shape, (src, cst, pb, rr), 4 * rank2 * cells, "proj")
    field = src
    for step in range(ITERS):
        recv = _exchange(send, devices)
        part = _call(
            _near_kernel, field_shape, (field, cst, nb, nlc, src), 8 * nb.shape[1] * cells, "near"
        )
        if step < ITERS - 1:
            field, send = _call(
                _far_proj_kernel,
                (field_shape, send_shape),
                (part, recv, idx, cp, eb, cst, pb, rr),
                8 * cp.size,
                "far_proj",
            )
        else:
            field, terms = _call(
                _far_grad_kernel,
                (field_shape, jax.ShapeDtypeStruct((1, cells), F32)),
                (part, recv, idx, cp, eb, bg),
                8 * cp.size,
                "far_grad",
            )
    freqs = lax.axis_size("freq")
    total = terms[0]
    hop = 1
    while hop < freqs:
        total = total + lax.ppermute(total, "freq", [(i, i ^ hop) for i in range(freqs)])
        hop *= 2
    return (field[None], total)


def solution(mesh):
    return jax.shard_map(
        per_device,
        mesh=mesh,
        in_specs=(
            P("freq", None, "cells"),
            P("freq", "cells"),
            P("freq", None, "cells"),
            P("freq", None, None, "cells"),
            P("cells", None),
            P("freq", None, None, "cells"),
            P("freq", None, None, "cells"),
            P("freq", None, None, None, "cells"),
            P("cells", None),
            P("cells"),
        ),
        out_specs=(P("freq", None, "cells"), P("cells")),
        check_vma=False,
    )
```

```python
import jax
import jax.numpy as jnp
from jax import lax
from jax.experimental import pallas as pl
from jax.experimental.pallas import tpu as pltpu
from jax.sharding import PartitionSpec as P

ITERS = 2
F32 = jnp.float32
BF16 = jnp.bfloat16
CHUNK = 512
PAIR_CHUNK = 128
VMEM_LIMIT = 56 * 1024 * 1024


def _split3(a):
    hi = a.astype(BF16)
    r = a - hi.astype(F32)
    mid = r.astype(BF16)
    lo = (r - mid.astype(F32)).astype(BF16)
    return jnp.concatenate([hi, mid, lo], axis=0)


def _sdot(split, onehot):
    m = split.shape[0] // 3
    r = jnp.dot(split, onehot, preferred_element_type=F32)
    return r[:m] + r[m : 2 * m] + r[2 * m :]


def _xdot(a, onehot):
    return _sdot(_split3(a), onehot)


def _iota(shape, dim):
    return lax.broadcasted_iota(jnp.int32, shape, dim)


def _weighted_proj(u, c, pre, pim):
    wre = u[0:1] * c
    wim = u[1:2] * c
    return jnp.concatenate([pre * wre - pim * wim, pre * wim + pim * wre], axis=0)


def _proj_chunk(pw, off, clusters, width):
    n = pw.shape[1]
    seg = ((_iota((n, clusters), 0) + off) // width) == _iota((n, clusters), 1)
    return _xdot(pw, seg.astype(BF16))


def _send_of(q, rr_ref, clusters):
    nsend = rr_ref.shape[1]
    oh = (_iota((clusters, nsend), 0).astype(F32) == rr_ref[...]).astype(BF16)
    return _xdot(q, oh)


def _proj_kernel(u_ref, c_ref, p_ref, q_ref):
    cells = u_ref.shape[1]
    clusters = cells // 64
    rank2 = 2 * p_ref.shape[1]

    def body(ci, q):
        off = pl.multiple_of(ci * CHUNK, CHUNK)
        sl = pl.ds(off, CHUNK)
        pw = _weighted_proj(u_ref[:, sl], c_ref[:, sl], p_ref[0, :, sl], p_ref[1, :, sl])
        return q + _proj_chunk(pw, off, clusters, 64)

    q_ref[...] = lax.fori_loop(0, cells // CHUNK, body, jnp.zeros((rank2, clusters), F32))


def _near_kernel(u_ref, c_ref, nb_ref, nlc_ref, base_ref, out_ref):
    cells = u_ref.shape[1]
    width = 64
    clusters = cells // width
    near = nlc_ref.shape[0]

    def wt_body(ci, acc):
        off = pl.multiple_of(ci * CHUNK, CHUNK)
        sl = pl.ds(off, CHUNK)
        w = u_ref[:, sl] * c_ref[:, sl]
        sel = _iota((width, CHUNK), 0) == ((_iota((width, CHUNK), 1) + off) % width)
        wm = jnp.concatenate(
            [jnp.where(sel, w[0:1], 0.0), jnp.where(sel, w[1:2], 0.0)], axis=0
        )
        seg = ((_iota((CHUNK, clusters), 0) + off) // width) == _iota((CHUNK, clusters), 1)
        return acc + _xdot(wm, seg.astype(BF16))

    wt = lax.fori_loop(0, cells // CHUNK, wt_body, jnp.zeros((2 * width, clusters), F32))
    wt_split = _split3(wt)

    def near_body(ci, carry):
        off = pl.multiple_of(ci * CHUNK, CHUNK)
        sl = pl.ds(off, CHUNK)
        crow = _iota((clusters, CHUNK), 0)
        acc_re = jnp.zeros((1, CHUNK), F32)
        acc_im = jnp.zeros((1, CHUNK), F32)
        for k in range(near):
            m = (crow == nlc_ref[k : k + 1, sl]).astype(BF16)
            wk = _sdot(wt_split, m)
            wre = wk[:width]
            wim = wk[width:]
            nre = nb_ref[0, pl.ds(k * width, width), sl]
            nim = nb_ref[1, pl.ds(k * width, width), sl]
            acc_re = acc_re + jnp.sum(nre * wre - nim * wim, axis=0, keepdims=True)
            acc_im = acc_im + jnp.sum(nre * wim + nim * wre, axis=0, keepdims=True)
        out_ref[:, sl] = base_ref[:, sl] + jnp.concatenate([acc_re, acc_im], axis=0)
        return carry

    lax.fori_loop(0, cells // CHUNK, near_body, 0)


def _far_common(part_ref, qs_ref, cpl_ref, e_ref, u_ref, chunk_tail):
    cells = part_ref.shape[1]
    width = 64
    clusters = cells // width
    rank = cpl_ref.shape[1]
    npairs = qs_ref.shape[1]
    far = npairs // clusters

    def pair_body(pj, z):
        off = pl.multiple_of(pj * PAIR_CHUNK, PAIR_CHUNK)
        sl = pl.ds(off, PAIR_CHUNK)
        qs = qs_ref[:, sl]
        qre = qs[:rank][None]
        qim = qs[rank:][None]
        cre = cpl_ref[0, :, :, sl]
        cim = cpl_ref[1, :, :, sl]
        zre = jnp.sum(cre * qre - cim * qim, axis=1)
        zim = jnp.sum(cre * qim + cim * qre, axis=1)
        seg = ((_iota((PAIR_CHUNK, clusters), 0) + off) // far) == _iota((PAIR_CHUNK, clusters), 1)
        return z + _xdot(jnp.concatenate([zre, zim], axis=0), seg.astype(BF16))

    z = lax.fori_loop(0, npairs // PAIR_CHUNK, pair_body, jnp.zeros((2 * rank, clusters), F32))
    z_split = _split3(z)

    def cell_body(ci, acc):
        off = pl.multiple_of(ci * CHUNK, CHUNK)
        sl = pl.ds(off, CHUNK)
        spread = _iota((clusters, CHUNK), 0) == ((_iota((clusters, CHUNK), 1) + off) // width)
        zz = _sdot(z_split, spread.astype(BF16))
        zre = zz[:rank]
        zim = zz[rank:]
        ere = e_ref[0, :, sl]
        eim = e_ref[1, :, sl]
        far_re = jnp.sum(ere * zre - eim * zim, axis=0, keepdims=True)
        far_im = jnp.sum(ere * zim + eim * zre, axis=0, keepdims=True)
        u = part_ref[:, sl] + jnp.concatenate([far_re, far_im], axis=0)
        u_ref[:, sl] = u
        return chunk_tail(u, off, sl, acc)

    return cell_body


def _far_proj_kernel(part_ref, qs_ref, cpl_ref, e_ref, c_ref, p_ref, u_ref, q_ref):
    cells = part_ref.shape[1]
    clusters = cells // 64
    rank2 = 2 * p_ref.shape[1]

    def tail(u, off, sl, q):
        pw = _weighted_proj(u, c_ref[:, sl], p_ref[0, :, sl], p_ref[1, :, sl])
        return q + _proj_chunk(pw, off, clusters, 64)

    body = _far_common(part_ref, qs_ref, cpl_ref, e_ref, u_ref, tail)
    q_ref[...] = lax.fori_loop(0, cells // CHUNK, body, jnp.zeros((rank2, clusters), F32))


def _far_grad_kernel(part_ref, qs_ref, cpl_ref, e_ref, bg_ref, u_ref, t_ref):
    cells = part_ref.shape[1]

    def tail(u, off, sl, acc):
        bg = bg_ref[:, sl]
        t_ref[:, sl] = bg[0:1] * u[0:1] + bg[1:2] * u[1:2]
        return acc

    body = _far_common(part_ref, qs_ref, cpl_ref, e_ref, u_ref, tail)
    lax.fori_loop(0, cells // CHUNK, body, 0)


def _prep_kernel(or_ref, sr_ref, idx_ref, req_ref):
    n = or_ref.shape[1]
    devices, cap = req_ref.shape
    oht = _iota((devices, n), 0) == or_ref[...]
    upper = (_iota((n, n), 0) < _iota((n, n), 1)).astype(BF16)
    counts = jnp.dot(oht.astype(BF16), upper, preferred_element_type=F32)
    pos = jnp.sum(jnp.where(oht, counts, 0.0), axis=0, keepdims=True).astype(jnp.int32)
    idx_ref[...] = or_ref[...] * cap + pos
    pkt = (_iota((cap, n), 0) == pos).astype(BF16)
    ohs = jnp.where(oht, sr_ref[...].astype(F32), 0.0).astype(BF16)
    req_ref[...] = lax.dot_general(
        ohs, pkt, (((1,), (1,)), ((), ())), preferred_element_type=F32
    )


def _call(kernel, outs, args, flops, name):
    leaves = outs if isinstance(outs, tuple) else (outs,)
    nbytes = sum(a.size * a.dtype.itemsize for a in args) + sum(
        o.size * jnp.dtype(o.dtype).itemsize for o in leaves
    )
    return pl.pallas_call(
        kernel,
        out_shape=outs,
        compiler_params=pltpu.CompilerParams(vmem_limit_bytes=VMEM_LIMIT),
        cost_estimate=pl.CostEstimate(flops=flops, bytes_accessed=nbytes, transcendentals=0),
        name=name,
    )(*args)


def _exchange(q, rr, idx, devices):
    send = q[:, rr]
    rows, total = send.shape
    slots = total // devices
    got = lax.all_to_all(send.reshape(rows, devices, slots), "cells", 1, 1, tiled=True)
    return got.reshape(rows, total)[:, idx]


def per_device(
    adj_source,
    contrast,
    background,
    near_blocks,
    near_list,
    proj_basis,
    expand_basis,
    coupling,
    far_owner,
    far_slot,
):
    devices = lax.axis_size("cells")
    clusters = near_list.shape[0]
    cells = contrast.shape[1]
    width = cells // clusters
    npairs = far_slot.shape[0]
    cap = 32

    src = adj_source[0]
    cst = contrast
    nb = near_blocks[0]
    pb = proj_basis[0]
    eb = expand_basis[0]
    cp = coupling[0]
    bg = background[0]

    me = lax.axis_index("cells")
    local_list = near_list - me * clusters
    nlc = jnp.repeat(local_list.T, width, axis=1)

    idx, req = _call(
        _prep_kernel,
        (
            jax.ShapeDtypeStruct((1, npairs), jnp.int32),
            jax.ShapeDtypeStruct((devices, cap), F32),
        ),
        (far_owner.reshape(1, npairs), far_slot.reshape(1, npairs)),
        2 * devices * npairs * npairs,
        "prep",
    )
    rr = lax.all_to_all(req, "cells", 0, 0, tiled=True).reshape(devices * cap).astype(jnp.int32)
    idx = idx.reshape(npairs)

    nsend = devices * cap
    rank2 = 2 * pb.shape[1]
    q_shape = jax.ShapeDtypeStruct((rank2, clusters), F32)
    field_shape = jax.ShapeDtypeStruct((2, cells), F32)

    q = _call(_proj_kernel, q_shape, (src, cst, pb), 4 * rank2 * cells, "proj")
    field = src
    for step in range(ITERS):
        qs = _exchange(q, rr, idx, devices)
        part = _call(
            _near_kernel, field_shape, (field, cst, nb, nlc, src), 8 * nb.shape[1] * cells, "near"
        )
        if step < ITERS - 1:
            field, q = _call(
                _far_proj_kernel,
                (field_shape, q_shape),
                (part, qs, cp, eb, cst, pb),
                8 * cp.size,
                "far_proj",
            )
        else:
            field, terms = _call(
                _far_grad_kernel,
                (field_shape, jax.ShapeDtypeStruct((1, cells), F32)),
                (part, qs, cp, eb, bg),
                8 * cp.size,
                "far_grad",
            )
    freqs = lax.axis_size("freq")
    total = terms[0]
    hop = 1
    while hop < freqs:
        total = total + lax.ppermute(total, "freq", [(i, i ^ hop) for i in range(freqs)])
        hop *= 2
    return (field[None], total)


def solution(mesh):
    return jax.shard_map(
        per_device,
        mesh=mesh,
        in_specs=(
            P("freq", None, "cells"),
            P("freq", "cells"),
            P("freq", None, "cells"),
            P("freq", None, None, "cells"),
            P("cells", None),
            P("freq", None, None, "cells"),
            P("freq", None, None, "cells"),
            P("freq", None, None, None, "cells"),
            P("cells", None),
            P("cells"),
        ),
        out_specs=(P("freq", None, "cells"), P("cells")),
        check_vma=False,
    )
```

```python
import jax
import jax.numpy as jnp
from jax import lax
from jax.experimental import pallas as pl
from jax.experimental.pallas import tpu as pltpu
from jax.sharding import PartitionSpec as P

ITERS = 2
F32 = jnp.float32
BF16 = jnp.bfloat16
CHUNK = 512
PAIR_CHUNK = 128
VMEM_LIMIT = 56 * 1024 * 1024


def _split3(a):
    hi = a.astype(BF16)
    r = a - hi.astype(F32)
    mid = r.astype(BF16)
    lo = (r - mid.astype(F32)).astype(BF16)
    return jnp.concatenate([hi, mid, lo], axis=0)


def _sdot(split, onehot):
    m = split.shape[0] // 3
    r = jnp.dot(split, onehot, preferred_element_type=F32)
    return r[:m] + r[m : 2 * m] + r[2 * m :]


def _xdot(a, onehot):
    return _sdot(_split3(a), onehot)


def _iota(shape, dim):
    return lax.broadcasted_iota(jnp.int32, shape, dim)


def _weighted_proj(u, c, pre, pim):
    wre = u[0:1] * c
    wim = u[1:2] * c
    return jnp.concatenate([pre * wre - pim * wim, pre * wim + pim * wre], axis=0)


def _proj_chunk(pw, off, clusters, width):
    n = pw.shape[1]
    seg = ((_iota((n, clusters), 0) + off) // width) == _iota((n, clusters), 1)
    return _xdot(pw, seg.astype(BF16))


def _pack(q, rr_ref):
    rank2, clusters = q.shape
    rows, groups = rr_ref.shape
    wide = groups * clusters
    lane = _iota((rows, wide), 1)
    grp = lane // clusters
    rr = rr_ref[...]
    want = rr[:, 0:1]
    for g in range(1, groups):
        want = jnp.where(grp == g, rr[:, g : g + 1], want)
    oh = ((lane % clusters).astype(F32) == want).astype(BF16)
    tile = (_iota((clusters, wide), 0) == _iota((clusters, wide), 1) % clusters).astype(BF16)
    qw = _xdot(q, tile)
    qw = jnp.concatenate([qw] * groups, axis=0)
    keep = (_iota((groups * rank2, wide), 0) // rank2) == (_iota((groups * rank2, wide), 1) // clusters)
    qw = jnp.where(keep, qw, 0.0)
    r = lax.dot_general(oh, _split3(qw), (((1,), (1,)), ((), ())), preferred_element_type=F32)
    n = groups * rank2
    return r[:, :n] + r[:, n : 2 * n] + r[:, 2 * n :]


def _pack_kernel(q_ref, rr_ref, send_ref):
    send_ref[...] = _pack(q_ref[...], rr_ref)


def _proj_kernel(u_ref, c_ref, p_ref, q_ref):
    cells = u_ref.shape[1]
    clusters = cells // 64
    rank2 = 2 * p_ref.shape[1]

    def body(ci, q):
        off = pl.multiple_of(ci * CHUNK, CHUNK)
        sl = pl.ds(off, CHUNK)
        pw = _weighted_proj(u_ref[:, sl], c_ref[:, sl], p_ref[0, :, sl], p_ref[1, :, sl])
        return q + _proj_chunk(pw, off, clusters, 64)

    q_ref[...] = lax.fori_loop(0, cells // CHUNK, body, jnp.zeros((rank2, clusters), F32))


def _near_kernel(u_ref, c_ref, nb_ref, nlc_ref, base_ref, out_ref):
    cells = u_ref.shape[1]
    width = 64
    clusters = cells // width
    near = nlc_ref.shape[0]

    def wt_body(ci, acc):
        off = pl.multiple_of(ci * CHUNK, CHUNK)
        sl = pl.ds(off, CHUNK)
        w = u_ref[:, sl] * c_ref[:, sl]
        sel = _iota((width, CHUNK), 0) == ((_iota((width, CHUNK), 1) + off) % width)
        wm = jnp.concatenate(
            [jnp.where(sel, w[0:1], 0.0), jnp.where(sel, w[1:2], 0.0)], axis=0
        )
        seg = ((_iota((CHUNK, clusters), 0) + off) // width) == _iota((CHUNK, clusters), 1)
        return acc + _xdot(wm, seg.astype(BF16))

    wt = lax.fori_loop(0, cells // CHUNK, wt_body, jnp.zeros((2 * width, clusters), F32))
    wt_split = _split3(wt)

    def near_body(ci, carry):
        off = pl.multiple_of(ci * CHUNK, CHUNK)
        sl = pl.ds(off, CHUNK)
        crow = _iota((clusters, CHUNK), 0)
        acc_re = jnp.zeros((1, CHUNK), F32)
        acc_im = jnp.zeros((1, CHUNK), F32)
        for k in range(near):
            m = (crow == nlc_ref[k : k + 1, sl]).astype(BF16)
            wk = _sdot(wt_split, m)
            wre = wk[:width]
            wim = wk[width:]
            nre = nb_ref[0, pl.ds(k * width, width), sl]
            nim = nb_ref[1, pl.ds(k * width, width), sl]
            acc_re = acc_re + jnp.sum(nre * wre - nim * wim, axis=0, keepdims=True)
            acc_im = acc_im + jnp.sum(nre * wim + nim * wre, axis=0, keepdims=True)
        out_ref[:, sl] = base_ref[:, sl] + jnp.concatenate([acc_re, acc_im], axis=0)
        return carry

    lax.fori_loop(0, cells // CHUNK, near_body, 0)


def _far_common(part_ref, qs_ref, cpl_ref, e_ref, u_ref, chunk_tail):
    cells = part_ref.shape[1]
    width = 64
    clusters = cells // width
    rank = cpl_ref.shape[1]
    npairs = qs_ref.shape[1]
    far = npairs // clusters

    def pair_body(pj, z):
        off = pl.multiple_of(pj * PAIR_CHUNK, PAIR_CHUNK)
        sl = pl.ds(off, PAIR_CHUNK)
        qs = qs_ref[:, sl]
        qre = qs[:rank][None]
        qim = qs[rank:][None]
        cre = cpl_ref[0, :, :, sl]
        cim = cpl_ref[1, :, :, sl]
        zre = jnp.sum(cre * qre - cim * qim, axis=1)
        zim = jnp.sum(cre * qim + cim * qre, axis=1)
        seg = ((_iota((PAIR_CHUNK, clusters), 0) + off) // far) == _iota((PAIR_CHUNK, clusters), 1)
        return z + _xdot(jnp.concatenate([zre, zim], axis=0), seg.astype(BF16))

    z = lax.fori_loop(0, npairs // PAIR_CHUNK, pair_body, jnp.zeros((2 * rank, clusters), F32))
    z_split = _split3(z)

    def cell_body(ci, acc):
        off = pl.multiple_of(ci * CHUNK, CHUNK)
        sl = pl.ds(off, CHUNK)
        spread = _iota((clusters, CHUNK), 0) == ((_iota((clusters, CHUNK), 1) + off) // width)
        zz = _sdot(z_split, spread.astype(BF16))
        zre = zz[:rank]
        zim = zz[rank:]
        ere = e_ref[0, :, sl]
        eim = e_ref[1, :, sl]
        far_re = jnp.sum(ere * zre - eim * zim, axis=0, keepdims=True)
        far_im = jnp.sum(ere * zim + eim * zre, axis=0, keepdims=True)
        u = part_ref[:, sl] + jnp.concatenate([far_re, far_im], axis=0)
        u_ref[:, sl] = u
        return chunk_tail(u, off, sl, acc)

    return cell_body


def _far_proj_kernel(part_ref, qs_ref, cpl_ref, e_ref, c_ref, p_ref, rr_ref, u_ref, send_ref):
    cells = part_ref.shape[1]
    clusters = cells // 64
    rank2 = 2 * p_ref.shape[1]

    def tail(u, off, sl, q):
        pw = _weighted_proj(u, c_ref[:, sl], p_ref[0, :, sl], p_ref[1, :, sl])
        return q + _proj_chunk(pw, off, clusters, 64)

    body = _far_common(part_ref, qs_ref, cpl_ref, e_ref, u_ref, tail)
    q = lax.fori_loop(0, cells // CHUNK, body, jnp.zeros((rank2, clusters), F32))
    send_ref[...] = _pack(q, rr_ref)


def _far_grad_kernel(part_ref, qs_ref, cpl_ref, e_ref, bg_ref, u_ref, t_ref):
    cells = part_ref.shape[1]

    def tail(u, off, sl, acc):
        bg = bg_ref[:, sl]
        t_ref[:, sl] = bg[0:1] * u[0:1] + bg[1:2] * u[1:2]
        return acc

    body = _far_common(part_ref, qs_ref, cpl_ref, e_ref, u_ref, tail)
    lax.fori_loop(0, cells // CHUNK, body, 0)


def _prep_kernel(or_ref, sr_ref, idx_ref, req_ref):
    n = or_ref.shape[1]
    devices, cap = req_ref.shape
    oht = _iota((devices, n), 0) == or_ref[...]
    upper = (_iota((n, n), 0) < _iota((n, n), 1)).astype(BF16)
    counts = jnp.dot(oht.astype(BF16), upper, preferred_element_type=F32)
    pos = jnp.sum(jnp.where(oht, counts, 0.0), axis=0, keepdims=True).astype(jnp.int32)
    idx_ref[...] = or_ref[...] * cap + pos
    pkt = (_iota((cap, n), 0) == pos).astype(BF16)
    ohs = jnp.where(oht, sr_ref[...].astype(F32), 0.0).astype(BF16)
    req_ref[...] = lax.dot_general(
        ohs, pkt, (((1,), (1,)), ((), ())), preferred_element_type=F32
    )


def _call(kernel, outs, args, flops, name):
    leaves = outs if isinstance(outs, tuple) else (outs,)
    nbytes = sum(a.size * a.dtype.itemsize for a in args) + sum(
        o.size * jnp.dtype(o.dtype).itemsize for o in leaves
    )
    return pl.pallas_call(
        kernel,
        out_shape=outs,
        compiler_params=pltpu.CompilerParams(vmem_limit_bytes=VMEM_LIMIT),
        cost_estimate=pl.CostEstimate(flops=flops, bytes_accessed=nbytes, transcendentals=0),
        name=name,
    )(*args)


def _exchange(send, idx, devices, cap):
    total = send.size
    got = lax.all_to_all(send.reshape(devices, total // devices), "cells", 0, 0)
    got = got.reshape(devices * cap, total // (devices * cap))
    return got[idx].T


def per_device(
    adj_source,
    contrast,
    background,
    near_blocks,
    near_list,
    proj_basis,
    expand_basis,
    coupling,
    far_owner,
    far_slot,
):
    devices = lax.axis_size("cells")
    clusters = near_list.shape[0]
    cells = contrast.shape[1]
    width = cells // clusters
    npairs = far_slot.shape[0]
    cap = 32

    src = adj_source[0]
    cst = contrast
    nb = near_blocks[0]
    pb = proj_basis[0]
    eb = expand_basis[0]
    cp = coupling[0]
    bg = background[0]

    me = lax.axis_index("cells")
    local_list = near_list - me * clusters
    nlc = jnp.repeat(local_list.T, width, axis=1)

    idx, req = _call(
        _prep_kernel,
        (
            jax.ShapeDtypeStruct((1, npairs), jnp.int32),
            jax.ShapeDtypeStruct((devices, cap), F32),
        ),
        (far_owner.reshape(1, npairs), far_slot.reshape(1, npairs)),
        2 * devices * npairs * npairs,
        "prep",
    )
    groups = 4
    rr = lax.all_to_all(req, "cells", 0, 0, tiled=True).reshape(devices * cap // groups, groups)
    idx = idx.reshape(npairs)

    nsend = devices * cap
    rank2 = 2 * pb.shape[1]
    q_shape = jax.ShapeDtypeStruct((rank2, clusters), F32)
    field_shape = jax.ShapeDtypeStruct((2, cells), F32)

    q = _call(_proj_kernel, q_shape, (src, cst, pb), 4 * rank2 * cells, "proj")
    send_shape = jax.ShapeDtypeStruct((devices * cap // groups, groups * rank2), F32)
    send = _call(_pack_kernel, send_shape, (q, rr), 2 * send_shape.size * clusters, "pack")
    field = src
    for step in range(ITERS):
        qs = _exchange(send, idx, devices, cap)
        part = _call(
            _near_kernel, field_shape, (field, cst, nb, nlc, src), 8 * nb.shape[1] * cells, "near"
        )
        if step < ITERS - 1:
            field, send = _call(
                _far_proj_kernel,
                (field_shape, send_shape),
                (part, qs, cp, eb, cst, pb, rr),
                8 * cp.size,
                "far_proj",
            )
        else:
            field, terms = _call(
                _far_grad_kernel,
                (field_shape, jax.ShapeDtypeStruct((1, cells), F32)),
                (part, qs, cp, eb, bg),
                8 * cp.size,
                "far_grad",
            )
    freqs = lax.axis_size("freq")
    total = terms[0]
    hop = 1
    while hop < freqs:
        total = total + lax.ppermute(total, "freq", [(i, i ^ hop) for i in range(freqs)])
        hop *= 2
    return (field[None], total)


def solution(mesh):
    return jax.shard_map(
        per_device,
        mesh=mesh,
        in_specs=(
            P("freq", None, "cells"),
            P("freq", "cells"),
            P("freq", None, "cells"),
            P("freq", None, None, "cells"),
            P("cells", None),
            P("freq", None, None, "cells"),
            P("freq", None, None, "cells"),
            P("freq", None, None, None, "cells"),
            P("cells", None),
            P("cells"),
        ),
        out_specs=(P("freq", None, "cells"), P("cells")),
        check_vma=False,
    )
```

```python
import jax
import jax.numpy as jnp
from jax import lax
from jax.experimental import pallas as pl
from jax.experimental.pallas import tpu as pltpu
from jax.sharding import PartitionSpec as P

ITERS = 2
F32 = jnp.float32
BF16 = jnp.bfloat16
CHUNK = 512
PAIR_CHUNK = 128
VMEM_LIMIT = 56 * 1024 * 1024


def _split3(a):
    hi = a.astype(BF16)
    r = a - hi.astype(F32)
    mid = r.astype(BF16)
    lo = (r - mid.astype(F32)).astype(BF16)
    return jnp.concatenate([hi, mid, lo], axis=0)


def _sdot(split, onehot):
    m = split.shape[0] // 3
    r = jnp.dot(split, onehot, preferred_element_type=F32)
    return r[:m] + r[m : 2 * m] + r[2 * m :]


def _xdot(a, onehot):
    return _sdot(_split3(a), onehot)


def _iota(shape, dim):
    return lax.broadcasted_iota(jnp.int32, shape, dim)


def _weighted_proj(u, c, pre, pim):
    wre = u[0:1] * c
    wim = u[1:2] * c
    return jnp.concatenate([pre * wre - pim * wim, pre * wim + pim * wre], axis=0)


def _proj_chunk(pw, off, clusters, width):
    n = pw.shape[1]
    seg = ((_iota((n, clusters), 0) + off) // width) == _iota((n, clusters), 1)
    return _xdot(pw, seg.astype(BF16))


def _pack(q, rr):
    rank2, clusters = q.shape
    rows, groups = rr.shape
    wide = groups * clusters
    lane = _iota((rows, wide), 1)
    grp = lane // clusters
    want = rr[:, 0:1]
    for g in range(1, groups):
        want = jnp.where(grp == g, rr[:, g : g + 1], want)
    oh = ((lane % clusters).astype(F32) == want).astype(BF16)
    tile = (_iota((clusters, wide), 0) == _iota((clusters, wide), 1) % clusters).astype(BF16)
    qw = _xdot(q, tile)
    qw = jnp.concatenate([qw] * groups, axis=0)
    keep = (_iota((groups * rank2, wide), 0) // rank2) == (_iota((groups * rank2, wide), 1) // clusters)
    qw = jnp.where(keep, qw, 0.0)
    r = lax.dot_general(oh, _split3(qw), (((1,), (1,)), ((), ())), preferred_element_type=F32)
    n = groups * rank2
    return r[:, :n] + r[:, n : 2 * n] + r[:, 2 * n :]


def _proj_pack_kernel(u_ref, c_ref, p_ref, req_ref, send_ref):
    cells = u_ref.shape[1]
    clusters = cells // 64
    rank2 = 2 * p_ref.shape[1]
    devices, cap = req_ref.shape
    groups = 4
    lanes = groups * rank2

    def body(ci, q):
        off = pl.multiple_of(ci * CHUNK, CHUNK)
        sl = pl.ds(off, CHUNK)
        pw = _weighted_proj(u_ref[:, sl], c_ref[:, sl], p_ref[0, :, sl], p_ref[1, :, sl])
        return q + _proj_chunk(pw, off, clusters, 64)

    q = lax.fori_loop(0, cells // CHUNK, body, jnp.zeros((rank2, clusters), F32))
    nrow = clusters // groups
    order = (_iota((nrow, groups), 0) * groups + _iota((nrow, groups), 1)).astype(F32)
    flat = _pack(q, order)
    place = (_iota((cap, lanes), 0) == _iota((cap, lanes), 1)).astype(BF16)
    reqrow = jnp.dot(req_ref[...].astype(BF16), place, preferred_element_type=F32)
    block = nrow + 1
    for e in range(devices):
        send_ref[pl.ds(e * block, nrow), :] = flat
        send_ref[pl.ds(e * block + nrow, 1), :] = reqrow[e : e + 1]


def _proj_kernel(u_ref, c_ref, p_ref, q_ref):
    cells = u_ref.shape[1]
    clusters = cells // 64
    rank2 = 2 * p_ref.shape[1]

    def body(ci, q):
        off = pl.multiple_of(ci * CHUNK, CHUNK)
        sl = pl.ds(off, CHUNK)
        pw = _weighted_proj(u_ref[:, sl], c_ref[:, sl], p_ref[0, :, sl], p_ref[1, :, sl])
        return q + _proj_chunk(pw, off, clusters, 64)

    q_ref[...] = lax.fori_loop(0, cells // CHUNK, body, jnp.zeros((rank2, clusters), F32))


def _near_kernel(u_ref, c_ref, nb_ref, nlc_ref, base_ref, out_ref):
    cells = u_ref.shape[1]
    width = 64
    clusters = cells // width
    near = nlc_ref.shape[0]

    def wt_body(ci, acc):
        off = pl.multiple_of(ci * CHUNK, CHUNK)
        sl = pl.ds(off, CHUNK)
        w = u_ref[:, sl] * c_ref[:, sl]
        sel = _iota((width, CHUNK), 0) == ((_iota((width, CHUNK), 1) + off) % width)
        wm = jnp.concatenate(
            [jnp.where(sel, w[0:1], 0.0), jnp.where(sel, w[1:2], 0.0)], axis=0
        )
        seg = ((_iota((CHUNK, clusters), 0) + off) // width) == _iota((CHUNK, clusters), 1)
        return acc + _xdot(wm, seg.astype(BF16))

    wt = lax.fori_loop(0, cells // CHUNK, wt_body, jnp.zeros((2 * width, clusters), F32))
    wt_split = _split3(wt)

    def near_body(ci, carry):
        off = pl.multiple_of(ci * CHUNK, CHUNK)
        sl = pl.ds(off, CHUNK)
        crow = _iota((clusters, CHUNK), 0)
        acc_re = jnp.zeros((1, CHUNK), F32)
        acc_im = jnp.zeros((1, CHUNK), F32)
        for k in range(near):
            m = (crow == nlc_ref[k : k + 1, sl]).astype(BF16)
            wk = _sdot(wt_split, m)
            wre = wk[:width]
            wim = wk[width:]
            nre = nb_ref[0, pl.ds(k * width, width), sl]
            nim = nb_ref[1, pl.ds(k * width, width), sl]
            acc_re = acc_re + jnp.sum(nre * wre - nim * wim, axis=0, keepdims=True)
            acc_im = acc_im + jnp.sum(nre * wim + nim * wre, axis=0, keepdims=True)
        out_ref[:, sl] = base_ref[:, sl] + jnp.concatenate([acc_re, acc_im], axis=0)
        return carry

    lax.fori_loop(0, cells // CHUNK, near_body, 0)


def _far_common(part_ref, qs_ref, cpl_ref, e_ref, u_ref, chunk_tail):
    cells = part_ref.shape[1]
    width = 64
    clusters = cells // width
    rank = cpl_ref.shape[1]
    npairs = qs_ref.shape[1]
    far = npairs // clusters

    def pair_body(pj, z):
        off = pl.multiple_of(pj * PAIR_CHUNK, PAIR_CHUNK)
        sl = pl.ds(off, PAIR_CHUNK)
        qs = qs_ref[:, sl]
        qre = qs[:rank][None]
        qim = qs[rank:][None]
        cre = cpl_ref[0, :, :, sl]
        cim = cpl_ref[1, :, :, sl]
        zre = jnp.sum(cre * qre - cim * qim, axis=1)
        zim = jnp.sum(cre * qim + cim * qre, axis=1)
        seg = ((_iota((PAIR_CHUNK, clusters), 0) + off) // far) == _iota((PAIR_CHUNK, clusters), 1)
        return z + _xdot(jnp.concatenate([zre, zim], axis=0), seg.astype(BF16))

    z = lax.fori_loop(0, npairs // PAIR_CHUNK, pair_body, jnp.zeros((2 * rank, clusters), F32))
    z_split = _split3(z)

    def cell_body(ci, acc):
        off = pl.multiple_of(ci * CHUNK, CHUNK)
        sl = pl.ds(off, CHUNK)
        spread = _iota((clusters, CHUNK), 0) == ((_iota((clusters, CHUNK), 1) + off) // width)
        zz = _sdot(z_split, spread.astype(BF16))
        zre = zz[:rank]
        zim = zz[rank:]
        ere = e_ref[0, :, sl]
        eim = e_ref[1, :, sl]
        far_re = jnp.sum(ere * zre - eim * zim, axis=0, keepdims=True)
        far_im = jnp.sum(ere * zim + eim * zre, axis=0, keepdims=True)
        u = part_ref[:, sl] + jnp.concatenate([far_re, far_im], axis=0)
        u_ref[:, sl] = u
        return chunk_tail(u, off, sl, acc)

    return cell_body


def _far_proj_kernel(part_ref, qs_ref, cpl_ref, e_ref, c_ref, p_ref, rr_ref, u_ref, send_ref):
    cells = part_ref.shape[1]
    clusters = cells // 64
    rank2 = 2 * p_ref.shape[1]

    def tail(u, off, sl, q):
        pw = _weighted_proj(u, c_ref[:, sl], p_ref[0, :, sl], p_ref[1, :, sl])
        return q + _proj_chunk(pw, off, clusters, 64)

    body = _far_common(part_ref, qs_ref, cpl_ref, e_ref, u_ref, tail)
    q = lax.fori_loop(0, cells // CHUNK, body, jnp.zeros((rank2, clusters), F32))
    send_ref[...] = _pack(q, rr_ref[...])


def _far_grad_kernel(part_ref, qs_ref, cpl_ref, e_ref, bg_ref, u_ref, t_ref):
    cells = part_ref.shape[1]

    def tail(u, off, sl, acc):
        bg = bg_ref[:, sl]
        t_ref[:, sl] = bg[0:1] * u[0:1] + bg[1:2] * u[1:2]
        return acc

    body = _far_common(part_ref, qs_ref, cpl_ref, e_ref, u_ref, tail)
    lax.fori_loop(0, cells // CHUNK, body, 0)


def _prep_kernel(or_ref, sr_ref, idx_ref, req_ref):
    n = or_ref.shape[1]
    devices, cap = req_ref.shape
    oht = _iota((devices, n), 0) == or_ref[...]
    upper = (_iota((n, n), 0) < _iota((n, n), 1)).astype(BF16)
    counts = jnp.dot(oht.astype(BF16), upper, preferred_element_type=F32)
    pos = jnp.sum(jnp.where(oht, counts, 0.0), axis=0, keepdims=True).astype(jnp.int32)
    idx_ref[...] = or_ref[...] * cap + pos
    pkt = (_iota((cap, n), 0) == pos).astype(BF16)
    ohs = jnp.where(oht, sr_ref[...].astype(F32), 0.0).astype(BF16)
    req_ref[...] = lax.dot_general(
        ohs, pkt, (((1,), (1,)), ((), ())), preferred_element_type=F32
    )


def _call(kernel, outs, args, flops, name):
    leaves = outs if isinstance(outs, tuple) else (outs,)
    nbytes = sum(a.size * a.dtype.itemsize for a in args) + sum(
        o.size * jnp.dtype(o.dtype).itemsize for o in leaves
    )
    return pl.pallas_call(
        kernel,
        out_shape=outs,
        compiler_params=pltpu.CompilerParams(vmem_limit_bytes=VMEM_LIMIT),
        cost_estimate=pl.CostEstimate(flops=flops, bytes_accessed=nbytes, transcendentals=0),
        name=name,
    )(*args)


def _exchange(send, idx, devices, cap):
    total = send.size
    got = lax.all_to_all(send.reshape(devices, total // devices), "cells", 0, 0)
    got = got.reshape(devices * cap, total // (devices * cap))
    return got[idx].T


def _exchange_all(send, devices, clusters, rank2, cap, groups, src_index):
    total = send.size
    got = lax.all_to_all(send.reshape(devices, total // devices), "cells", 0, 0)
    lanes = send.shape[1]
    got = got.reshape(devices, total // (devices * lanes), lanes)
    rr = got[:, -1, :cap].reshape(devices * cap // groups, groups)
    table = got[:, :-1, :].reshape(devices * clusters, rank2)
    return table[src_index].T, rr


def per_device(
    adj_source,
    contrast,
    background,
    near_blocks,
    near_list,
    proj_basis,
    expand_basis,
    coupling,
    far_owner,
    far_slot,
):
    devices = lax.axis_size("cells")
    clusters = near_list.shape[0]
    cells = contrast.shape[1]
    width = cells // clusters
    npairs = far_slot.shape[0]
    cap = 32

    src = adj_source[0]
    cst = contrast
    nb = near_blocks[0]
    pb = proj_basis[0]
    eb = expand_basis[0]
    cp = coupling[0]
    bg = background[0]

    me = lax.axis_index("cells")
    local_list = near_list - me * clusters
    nlc = jnp.repeat(local_list.T, width, axis=1)

    idx, req = _call(
        _prep_kernel,
        (
            jax.ShapeDtypeStruct((1, npairs), jnp.int32),
            jax.ShapeDtypeStruct((devices, cap), F32),
        ),
        (far_owner.reshape(1, npairs), far_slot.reshape(1, npairs)),
        2 * devices * npairs * npairs,
        "prep",
    )
    groups = 4
    idx = idx.reshape(npairs)
    src_index = far_owner[:, 0] * clusters + far_slot

    nsend = devices * cap
    rank2 = 2 * pb.shape[1]
    q_shape = jax.ShapeDtypeStruct((rank2, clusters), F32)
    field_shape = jax.ShapeDtypeStruct((2, cells), F32)

    first_shape = jax.ShapeDtypeStruct((devices * (clusters // groups + 1), groups * rank2), F32)
    send = _call(_proj_pack_kernel, first_shape, (src, cst, pb, req), 4 * rank2 * cells, "proj_pack")
    send_shape = jax.ShapeDtypeStruct((devices * cap // groups, groups * rank2), F32)
    field = src
    for step in range(ITERS):
        if step == 0:
            qs, rr = _exchange_all(send, devices, clusters, rank2, cap, groups, src_index)
        else:
            qs = _exchange(send, idx, devices, cap)
        part = _call(
            _near_kernel, field_shape, (field, cst, nb, nlc, src), 8 * nb.shape[1] * cells, "near"
        )
        if step < ITERS - 1:
            field, send = _call(
                _far_proj_kernel,
                (field_shape, send_shape),
                (part, qs, cp, eb, cst, pb, rr),
                8 * cp.size,
                "far_proj",
            )
        else:
            field, terms = _call(
                _far_grad_kernel,
                (field_shape, jax.ShapeDtypeStruct((1, cells), F32)),
                (part, qs, cp, eb, bg),
                8 * cp.size,
                "far_grad",
            )
    freqs = lax.axis_size("freq")
    total = terms[0]
    hop = 1
    while hop < freqs:
        total = total + lax.ppermute(total, "freq", [(i, i ^ hop) for i in range(freqs)])
        hop *= 2
    return (field[None], total)


def solution(mesh):
    return jax.shard_map(
        per_device,
        mesh=mesh,
        in_specs=(
            P("freq", None, "cells"),
            P("freq", "cells"),
            P("freq", None, "cells"),
            P("freq", None, None, "cells"),
            P("cells", None),
            P("freq", None, None, "cells"),
            P("freq", None, None, "cells"),
            P("freq", None, None, None, "cells"),
            P("cells", None),
            P("cells"),
        ),
        out_specs=(P("freq", None, "cells"), P("cells")),
        check_vma=False,
    )
```

```python
import jax
import jax.numpy as jnp
from jax import lax
from jax.experimental import pallas as pl
from jax.experimental.pallas import tpu as pltpu
from jax.sharding import PartitionSpec as P

ITERS = 2
F32 = jnp.float32
BF16 = jnp.bfloat16
CHUNK = 512
PAIR_CHUNK = 128
VMEM_LIMIT = 56 * 1024 * 1024


def _split3(a):
    hi = a.astype(BF16)
    r = a - hi.astype(F32)
    mid = r.astype(BF16)
    lo = (r - mid.astype(F32)).astype(BF16)
    return jnp.concatenate([hi, mid, lo], axis=0)


def _sdot(split, onehot):
    m = split.shape[0] // 3
    r = jnp.dot(split, onehot, preferred_element_type=F32)
    return r[:m] + r[m : 2 * m] + r[2 * m :]


def _xdot(a, onehot):
    return _sdot(_split3(a), onehot)


def _iota(shape, dim):
    return lax.broadcasted_iota(jnp.int32, shape, dim)


def _weighted_proj(u, c, pre, pim):
    wre = u[0:1] * c
    wim = u[1:2] * c
    return jnp.concatenate([pre * wre - pim * wim, pre * wim + pim * wre], axis=0)


def _proj_chunk(pw, off, clusters, width):
    n = pw.shape[1]
    seg = ((_iota((n, clusters), 0) + off) // width) == _iota((n, clusters), 1)
    return _xdot(pw, seg.astype(BF16))


def _pack(q, rr):
    rank2, clusters = q.shape
    rows, groups = rr.shape
    wide = groups * clusters
    lane = _iota((rows, wide), 1)
    grp = lane // clusters
    want = rr[:, 0:1]
    for g in range(1, groups):
        want = jnp.where(grp == g, rr[:, g : g + 1], want)
    oh = ((lane % clusters).astype(F32) == want).astype(BF16)
    tile = (_iota((clusters, wide), 0) == _iota((clusters, wide), 1) % clusters).astype(BF16)
    qw = _xdot(q, tile)
    qw = jnp.concatenate([qw] * groups, axis=0)
    keep = (_iota((groups * rank2, wide), 0) // rank2) == (_iota((groups * rank2, wide), 1) // clusters)
    qw = jnp.where(keep, qw, 0.0)
    r = lax.dot_general(oh, _split3(qw), (((1,), (1,)), ((), ())), preferred_element_type=F32)
    n = groups * rank2
    return r[:, :n] + r[:, n : 2 * n] + r[:, 2 * n :]


def _proj_pack_kernel(u_ref, c_ref, p_ref, req_ref, send_ref):
    cells = u_ref.shape[1]
    clusters = cells // 64
    rank2 = 2 * p_ref.shape[1]
    devices, cap = req_ref.shape
    groups = 4
    lanes = groups * rank2

    def body(ci, q):
        off = pl.multiple_of(ci * CHUNK, CHUNK)
        sl = pl.ds(off, CHUNK)
        pw = _weighted_proj(u_ref[:, sl], c_ref[:, sl], p_ref[0, :, sl], p_ref[1, :, sl])
        return q + _proj_chunk(pw, off, clusters, 64)

    q = lax.fori_loop(0, cells // CHUNK, body, jnp.zeros((rank2, clusters), F32))
    nrow = clusters // groups
    order = (_iota((nrow, groups), 0) * groups + _iota((nrow, groups), 1)).astype(F32)
    flat = _pack(q, order)
    place = (_iota((cap, lanes), 0) == _iota((cap, lanes), 1)).astype(BF16)
    reqrow = jnp.dot(req_ref[...].astype(BF16), place, preferred_element_type=F32)
    block = nrow + 1
    for e in range(devices):
        send_ref[pl.ds(e * block, nrow), :] = flat
        send_ref[pl.ds(e * block + nrow, 1), :] = reqrow[e : e + 1]


def _proj_kernel(u_ref, c_ref, p_ref, q_ref):
    cells = u_ref.shape[1]
    clusters = cells // 64
    rank2 = 2 * p_ref.shape[1]

    def body(ci, q):
        off = pl.multiple_of(ci * CHUNK, CHUNK)
        sl = pl.ds(off, CHUNK)
        pw = _weighted_proj(u_ref[:, sl], c_ref[:, sl], p_ref[0, :, sl], p_ref[1, :, sl])
        return q + _proj_chunk(pw, off, clusters, 64)

    q_ref[...] = lax.fori_loop(0, cells // CHUNK, body, jnp.zeros((rank2, clusters), F32))


def _near_kernel(u_ref, c_ref, nb_ref, nlc_ref, base_ref, out_ref):
    cells = u_ref.shape[1]
    width = 64
    clusters = cells // width
    near = nlc_ref.shape[0]

    def wt_body(ci, acc):
        off = pl.multiple_of(ci * CHUNK, CHUNK)
        sl = pl.ds(off, CHUNK)
        w = u_ref[:, sl] * c_ref[:, sl]
        sel = _iota((width, CHUNK), 0) == ((_iota((width, CHUNK), 1) + off) % width)
        wm = jnp.concatenate(
            [jnp.where(sel, w[0:1], 0.0), jnp.where(sel, w[1:2], 0.0)], axis=0
        )
        seg = ((_iota((CHUNK, clusters), 0) + off) // width) == _iota((CHUNK, clusters), 1)
        return acc + _xdot(wm, seg.astype(BF16))

    wt = lax.fori_loop(0, cells // CHUNK, wt_body, jnp.zeros((2 * width, clusters), F32))
    wt_split = _split3(wt)

    def near_body(ci, carry):
        off = pl.multiple_of(ci * CHUNK, CHUNK)
        sl = pl.ds(off, CHUNK)
        crow = _iota((clusters, CHUNK), 0)
        acc_re = jnp.zeros((1, CHUNK), F32)
        acc_im = jnp.zeros((1, CHUNK), F32)
        for k in range(near):
            m = (crow == nlc_ref[k : k + 1, sl]).astype(BF16)
            wk = _sdot(wt_split, m)
            wre = wk[:width]
            wim = wk[width:]
            nre = nb_ref[0, pl.ds(k * width, width), sl]
            nim = nb_ref[1, pl.ds(k * width, width), sl]
            acc_re = acc_re + jnp.sum(nre * wre - nim * wim, axis=0, keepdims=True)
            acc_im = acc_im + jnp.sum(nre * wim + nim * wre, axis=0, keepdims=True)
        out_ref[:, sl] = base_ref[:, sl] + jnp.concatenate([acc_re, acc_im], axis=0)
        return carry

    lax.fori_loop(0, cells // CHUNK, near_body, 0)


def _far_common(part_ref, qs_ref, cpl_ref, e_ref, u_ref, chunk_tail):
    cells = part_ref.shape[1]
    width = 64
    clusters = cells // width
    rank = cpl_ref.shape[1]
    npairs = qs_ref.shape[1]
    far = npairs // clusters

    def pair_body(pj, z):
        off = pl.multiple_of(pj * PAIR_CHUNK, PAIR_CHUNK)
        sl = pl.ds(off, PAIR_CHUNK)
        qs = qs_ref[:, sl]
        qre = qs[:rank][None]
        qim = qs[rank:][None]
        cre = cpl_ref[0, :, :, sl]
        cim = cpl_ref[1, :, :, sl]
        zre = jnp.sum(cre * qre - cim * qim, axis=1)
        zim = jnp.sum(cre * qim + cim * qre, axis=1)
        seg = ((_iota((PAIR_CHUNK, clusters), 0) + off) // far) == _iota((PAIR_CHUNK, clusters), 1)
        return z + _xdot(jnp.concatenate([zre, zim], axis=0), seg.astype(BF16))

    z = lax.fori_loop(0, npairs // PAIR_CHUNK, pair_body, jnp.zeros((2 * rank, clusters), F32))
    z_split = _split3(z)

    def cell_body(ci, acc):
        off = pl.multiple_of(ci * CHUNK, CHUNK)
        sl = pl.ds(off, CHUNK)
        spread = _iota((clusters, CHUNK), 0) == ((_iota((clusters, CHUNK), 1) + off) // width)
        zz = _sdot(z_split, spread.astype(BF16))
        zre = zz[:rank]
        zim = zz[rank:]
        ere = e_ref[0, :, sl]
        eim = e_ref[1, :, sl]
        far_re = jnp.sum(ere * zre - eim * zim, axis=0, keepdims=True)
        far_im = jnp.sum(ere * zim + eim * zre, axis=0, keepdims=True)
        u = part_ref[:, sl] + jnp.concatenate([far_re, far_im], axis=0)
        u_ref[:, sl] = u
        return chunk_tail(u, off, sl, acc)

    return cell_body


def _far_proj_kernel(part_ref, qs_ref, cpl_ref, e_ref, c_ref, p_ref, rr_ref, u_ref, send_ref):
    cells = part_ref.shape[1]
    clusters = cells // 64
    rank2 = 2 * p_ref.shape[1]

    def tail(u, off, sl, q):
        pw = _weighted_proj(u, c_ref[:, sl], p_ref[0, :, sl], p_ref[1, :, sl])
        return q + _proj_chunk(pw, off, clusters, 64)

    body = _far_common(part_ref, qs_ref, cpl_ref, e_ref, u_ref, tail)
    q = lax.fori_loop(0, cells // CHUNK, body, jnp.zeros((rank2, clusters), F32))
    send_ref[...] = _pack(q, rr_ref[...])


def _far_grad_kernel(part_ref, qs_ref, cpl_ref, e_ref, bg_ref, u_ref, t_ref):
    cells = part_ref.shape[1]

    def tail(u, off, sl, acc):
        bg = bg_ref[:, sl]
        t_ref[:, sl] = bg[0:1] * u[0:1] + bg[1:2] * u[1:2]
        return acc

    body = _far_common(part_ref, qs_ref, cpl_ref, e_ref, u_ref, tail)
    lax.fori_loop(0, cells // CHUNK, body, 0)


def _prep_kernel(or_ref, sr_ref, idx_ref, req_ref):
    n = or_ref.shape[1]
    devices, cap = req_ref.shape
    oht = _iota((devices, n), 0) == or_ref[...]
    upper = (_iota((n, n), 0) < _iota((n, n), 1)).astype(BF16)
    counts = jnp.dot(oht.astype(BF16), upper, preferred_element_type=F32)
    pos = jnp.sum(jnp.where(oht, counts, 0.0), axis=0, keepdims=True).astype(jnp.int32)
    idx_ref[...] = or_ref[...] * cap + pos
    pkt = (_iota((cap, n), 0) == pos).astype(BF16)
    ohs = jnp.where(oht, sr_ref[...].astype(F32), 0.0).astype(BF16)
    req_ref[...] = lax.dot_general(
        ohs, pkt, (((1,), (1,)), ((), ())), preferred_element_type=F32
    )


def _call(kernel, outs, args, flops, name):
    leaves = outs if isinstance(outs, tuple) else (outs,)
    nbytes = sum(a.size * a.dtype.itemsize for a in args) + sum(
        o.size * jnp.dtype(o.dtype).itemsize for o in leaves
    )
    return pl.pallas_call(
        kernel,
        out_shape=outs,
        compiler_params=pltpu.CompilerParams(vmem_limit_bytes=VMEM_LIMIT),
        cost_estimate=pl.CostEstimate(flops=flops, bytes_accessed=nbytes, transcendentals=0),
        name=name,
    )(*args)


def _exchange(send, idx, devices, cap):
    total = send.size
    got = lax.all_to_all(send.reshape(devices, total // devices), "cells", 0, 0)
    got = got.reshape(devices * cap, total // (devices * cap))
    return got[idx].T


def _exchange_all(send, devices, clusters, rank2, cap, groups, src_index):
    total = send.size
    got = lax.all_to_all(send.reshape(devices, total // devices), "cells", 0, 0)
    lanes = send.shape[1]
    got = got.reshape(devices, total // (devices * lanes), lanes)
    rr = got[:, -1, :cap].reshape(devices * cap // groups, groups)
    table = got[:, :-1, :].reshape(devices * clusters, rank2)
    return table[src_index].T, rr


def per_device(
    adj_source,
    contrast,
    background,
    near_blocks,
    near_list,
    proj_basis,
    expand_basis,
    coupling,
    far_owner,
    far_slot,
):
    devices = lax.axis_size("cells")
    clusters = near_list.shape[0]
    cells = contrast.shape[1]
    width = cells // clusters
    npairs = far_slot.shape[0]
    cap = 32

    src = adj_source[0]
    cst = contrast
    nb = near_blocks[0]
    pb = proj_basis[0]
    eb = expand_basis[0]
    cp = coupling[0]
    bg = background[0]

    me = lax.axis_index("cells")
    local_list = near_list - me * clusters
    nlc = jnp.repeat(local_list.T, width, axis=1)

    idx, req = _call(
        _prep_kernel,
        (
            jax.ShapeDtypeStruct((1, npairs), jnp.int32),
            jax.ShapeDtypeStruct((devices, cap), F32),
        ),
        (far_owner.reshape(1, npairs), far_slot.reshape(1, npairs)),
        2 * devices * npairs * npairs,
        "prep",
    )
    groups = 4
    idx = idx.reshape(npairs)
    src_index = far_owner[:, 0] * clusters + far_slot

    nsend = devices * cap
    rank2 = 2 * pb.shape[1]
    q_shape = jax.ShapeDtypeStruct((rank2, clusters), F32)
    field_shape = jax.ShapeDtypeStruct((2, cells), F32)

    first_shape = jax.ShapeDtypeStruct((devices * (clusters // groups + 1), groups * rank2), F32)
    send = _call(_proj_pack_kernel, first_shape, (src, cst, pb, req), 4 * rank2 * cells, "proj_pack")
    send_shape = jax.ShapeDtypeStruct((devices * cap // groups, groups * rank2), F32)
    field = src
    for step in range(ITERS):
        if step == 0:
            qs, rr = _exchange_all(send, devices, clusters, rank2, cap, groups, src_index)
        else:
            qs = _exchange(send, idx, devices, cap)
        part = _call(
            _near_kernel, field_shape, (field, cst, nb, nlc, src), 8 * nb.shape[1] * cells, "near"
        )
        if step < ITERS - 1:
            field, send = _call(
                _far_proj_kernel,
                (field_shape, send_shape),
                (part, qs, cp, eb, cst, pb, rr),
                8 * cp.size,
                "far_proj",
            )
        else:
            field, terms = _call(
                _far_grad_kernel,
                (field_shape, jax.ShapeDtypeStruct((1, cells), F32)),
                (part, qs, cp, eb, bg),
                8 * cp.size,
                "far_grad",
            )
    freqs = lax.axis_size("freq")
    mine = terms[0]
    got = [mine] + [
        lax.ppermute(mine, "freq", [(i, (i + k) % freqs) for i in range(freqs)])
        for k in range(1, freqs)
    ]
    stacked = jnp.stack(got)
    f = lax.axis_index("freq")
    total = stacked[(f - 0) % freqs]
    for src in range(1, freqs):
        total = total + stacked[(f - src) % freqs]
    return (field[None], total)


def solution(mesh):
    return jax.shard_map(
        per_device,
        mesh=mesh,
        in_specs=(
            P("freq", None, "cells"),
            P("freq", "cells"),
            P("freq", None, "cells"),
            P("freq", None, None, "cells"),
            P("cells", None),
            P("freq", None, None, "cells"),
            P("freq", None, None, "cells"),
            P("freq", None, None, None, "cells"),
            P("cells", None),
            P("cells"),
        ),
        out_specs=(P("freq", None, "cells"), P("cells")),
        check_vma=False,
    )
```

```python
import jax
import jax.numpy as jnp
from jax import lax
from jax.experimental import pallas as pl
from jax.experimental.pallas import tpu as pltpu
from jax.sharding import PartitionSpec as P

ITERS = 2
F32 = jnp.float32
BF16 = jnp.bfloat16
CHUNK = 512
PAIR_CHUNK = 128
VMEM_LIMIT = 56 * 1024 * 1024


def _split3(a):
    hi = a.astype(BF16)
    r = a - hi.astype(F32)
    mid = r.astype(BF16)
    lo = (r - mid.astype(F32)).astype(BF16)
    return jnp.concatenate([hi, mid, lo], axis=0)


def _sdot(split, onehot):
    m = split.shape[0] // 3
    r = jnp.dot(split, onehot, preferred_element_type=F32)
    return r[:m] + r[m : 2 * m] + r[2 * m :]


def _xdot(a, onehot):
    return _sdot(_split3(a), onehot)


def _iota(shape, dim):
    return lax.broadcasted_iota(jnp.int32, shape, dim)


def _weighted_proj(u, c, pre, pim):
    wre = u[0:1] * c
    wim = u[1:2] * c
    return jnp.concatenate([pre * wre - pim * wim, pre * wim + pim * wre], axis=0)


def _proj_chunk(pw, off, clusters, width):
    n = pw.shape[1]
    seg = ((_iota((n, clusters), 0) + off) // width) == _iota((n, clusters), 1)
    return _xdot(pw, seg.astype(BF16))


def _pack(q, rr):
    rank2, clusters = q.shape
    rows, groups = rr.shape
    wide = groups * clusters
    lane = _iota((rows, wide), 1)
    grp = lane // clusters
    want = rr[:, 0:1]
    for g in range(1, groups):
        want = jnp.where(grp == g, rr[:, g : g + 1], want)
    oh = ((lane % clusters).astype(F32) == want).astype(BF16)
    tile = (_iota((clusters, wide), 0) == _iota((clusters, wide), 1) % clusters).astype(BF16)
    qw = _xdot(q, tile)
    qw = jnp.concatenate([qw] * groups, axis=0)
    keep = (_iota((groups * rank2, wide), 0) // rank2) == (_iota((groups * rank2, wide), 1) // clusters)
    qw = jnp.where(keep, qw, 0.0)
    r = lax.dot_general(oh, _split3(qw), (((1,), (1,)), ((), ())), preferred_element_type=F32)
    n = groups * rank2
    return r[:, :n] + r[:, n : 2 * n] + r[:, 2 * n :]


def _prep(or_ref, sr_ref, idx_ref, devices, cap):
    n = or_ref.shape[1]
    oht = _iota((devices, n), 0) == or_ref[...]
    upper = (_iota((n, n), 0) < _iota((n, n), 1)).astype(BF16)
    counts = jnp.dot(oht.astype(BF16), upper, preferred_element_type=F32)
    pos = jnp.sum(jnp.where(oht, counts, 0.0), axis=0, keepdims=True).astype(jnp.int32)
    idx_ref[...] = or_ref[...] * cap + pos
    pkt = (_iota((cap, n), 0) == pos).astype(BF16)
    ohs = jnp.where(oht, sr_ref[...].astype(F32), 0.0).astype(BF16)
    return lax.dot_general(ohs, pkt, (((1,), (1,)), ((), ())), preferred_element_type=F32)


def _proj_pack_kernel(u_ref, c_ref, p_ref, or_ref, sr_ref, idx_ref, send_ref):
    cells = u_ref.shape[1]
    clusters = cells // 64
    rank2 = 2 * p_ref.shape[1]
    lanes = send_ref.shape[1]
    nrow = rank2 * clusters // lanes
    block = nrow + 1
    devices = send_ref.shape[0] // block
    cap = 32
    req = _prep(or_ref, sr_ref, idx_ref, devices, cap)

    def body(ci, q):
        off = pl.multiple_of(ci * CHUNK, CHUNK)
        sl = pl.ds(off, CHUNK)
        pw = _weighted_proj(u_ref[:, sl], c_ref[:, sl], p_ref[0, :, sl], p_ref[1, :, sl])
        return q + _proj_chunk(pw, off, clusters, 64)

    q = lax.fori_loop(0, cells // CHUNK, body, jnp.zeros((rank2, clusters), F32))
    per = lanes // clusters
    hi = q.astype(BF16)
    r1 = q - hi.astype(F32)
    mid = r1.astype(BF16)
    lo = (r1 - mid.astype(F32)).astype(BF16)
    flat = jnp.zeros((nrow, lanes), F32)
    for h in range(per):
        sel = (_iota((nrow, rank2), 1) == _iota((nrow, rank2), 0) * per + h).astype(BF16)
        part = sum(jnp.dot(sel, x, preferred_element_type=F32) for x in (hi, mid, lo))
        place = (_iota((clusters, lanes), 1) == _iota((clusters, lanes), 0) + h * clusters)
        flat = flat + _xdot(part, place.astype(BF16))
    place = (_iota((cap, lanes), 0) == _iota((cap, lanes), 1)).astype(BF16)
    reqrow = jnp.dot(req.astype(BF16), place, preferred_element_type=F32)
    for e in range(devices):
        send_ref[pl.ds(e * block, nrow), :] = flat
        send_ref[pl.ds(e * block + nrow, 1), :] = reqrow[e : e + 1]


def _rr_groups(rr, groups):
    devices, cap = rr.shape
    per = cap // groups
    rows = devices * per
    rep = ((_iota((rows, devices), 0) // per) == _iota((rows, devices), 1)).astype(BF16)
    wide = jnp.dot(rep, rr.astype(BF16), preferred_element_type=F32)
    keep = (_iota((rows, cap), 1) // groups) == (_iota((rows, cap), 0) % per)
    fold = ((_iota((cap, groups), 0) % groups) == _iota((cap, groups), 1)).astype(BF16)
    return jnp.dot(jnp.where(keep, wide, 0.0).astype(BF16), fold, preferred_element_type=F32)


def _near_kernel(u_ref, c_ref, nb_ref, nlc_ref, base_ref, out_ref):
    cells = u_ref.shape[1]
    width = 64
    clusters = cells // width
    near = nlc_ref.shape[0]

    def wt_body(ci, acc):
        off = pl.multiple_of(ci * CHUNK, CHUNK)
        sl = pl.ds(off, CHUNK)
        w = u_ref[:, sl] * c_ref[:, sl]
        sel = _iota((width, CHUNK), 0) == ((_iota((width, CHUNK), 1) + off) % width)
        wm = jnp.concatenate(
            [jnp.where(sel, w[0:1], 0.0), jnp.where(sel, w[1:2], 0.0)], axis=0
        )
        seg = ((_iota((CHUNK, clusters), 0) + off) // width) == _iota((CHUNK, clusters), 1)
        return acc + _xdot(wm, seg.astype(BF16))

    wt = lax.fori_loop(0, cells // CHUNK, wt_body, jnp.zeros((2 * width, clusters), F32))
    wt_split = _split3(wt)

    def near_body(ci, carry):
        off = pl.multiple_of(ci * CHUNK, CHUNK)
        sl = pl.ds(off, CHUNK)
        crow = _iota((clusters, CHUNK), 0)
        acc_re = jnp.zeros((1, CHUNK), F32)
        acc_im = jnp.zeros((1, CHUNK), F32)
        for k in range(near):
            m = (crow == nlc_ref[k : k + 1, sl]).astype(BF16)
            wk = _sdot(wt_split, m)
            wre = wk[:width]
            wim = wk[width:]
            nre = nb_ref[0, pl.ds(k * width, width), sl]
            nim = nb_ref[1, pl.ds(k * width, width), sl]
            acc_re = acc_re + jnp.sum(nre * wre - nim * wim, axis=0, keepdims=True)
            acc_im = acc_im + jnp.sum(nre * wim + nim * wre, axis=0, keepdims=True)
        out_ref[:, sl] = base_ref[:, sl] + jnp.concatenate([acc_re, acc_im], axis=0)
        return carry

    lax.fori_loop(0, cells // CHUNK, near_body, 0)


def _far_common(part_ref, qs_ref, cpl_ref, e_ref, u_ref, chunk_tail):
    cells = part_ref.shape[1]
    width = 64
    clusters = cells // width
    rank = cpl_ref.shape[1]
    npairs = qs_ref.shape[1]
    far = npairs // clusters

    def pair_body(pj, z):
        off = pl.multiple_of(pj * PAIR_CHUNK, PAIR_CHUNK)
        sl = pl.ds(off, PAIR_CHUNK)
        qs = qs_ref[:, sl]
        qre = qs[:rank][None]
        qim = qs[rank:][None]
        cre = cpl_ref[0, :, :, sl]
        cim = cpl_ref[1, :, :, sl]
        zre = jnp.sum(cre * qre - cim * qim, axis=1)
        zim = jnp.sum(cre * qim + cim * qre, axis=1)
        seg = ((_iota((PAIR_CHUNK, clusters), 0) + off) // far) == _iota((PAIR_CHUNK, clusters), 1)
        return z + _xdot(jnp.concatenate([zre, zim], axis=0), seg.astype(BF16))

    z = lax.fori_loop(0, npairs // PAIR_CHUNK, pair_body, jnp.zeros((2 * rank, clusters), F32))
    z_split = _split3(z)

    def cell_body(ci, acc):
        off = pl.multiple_of(ci * CHUNK, CHUNK)
        sl = pl.ds(off, CHUNK)
        spread = _iota((clusters, CHUNK), 0) == ((_iota((clusters, CHUNK), 1) + off) // width)
        zz = _sdot(z_split, spread.astype(BF16))
        zre = zz[:rank]
        zim = zz[rank:]
        ere = e_ref[0, :, sl]
        eim = e_ref[1, :, sl]
        far_re = jnp.sum(ere * zre - eim * zim, axis=0, keepdims=True)
        far_im = jnp.sum(ere * zim + eim * zre, axis=0, keepdims=True)
        u = part_ref[:, sl] + jnp.concatenate([far_re, far_im], axis=0)
        u_ref[:, sl] = u
        return chunk_tail(u, off, sl, acc)

    return cell_body


def _far_proj_kernel(part_ref, qs_ref, cpl_ref, e_ref, c_ref, p_ref, rr_ref, u_ref, send_ref):
    cells = part_ref.shape[1]
    clusters = cells // 64
    rank2 = 2 * p_ref.shape[1]

    def tail(u, off, sl, q):
        pw = _weighted_proj(u, c_ref[:, sl], p_ref[0, :, sl], p_ref[1, :, sl])
        return q + _proj_chunk(pw, off, clusters, 64)

    body = _far_common(part_ref, qs_ref, cpl_ref, e_ref, u_ref, tail)
    q = lax.fori_loop(0, cells // CHUNK, body, jnp.zeros((rank2, clusters), F32))
    send_ref[...] = _pack(q, _rr_groups(rr_ref[...], send_ref.shape[1] // rank2))


def _far_grad_kernel(part_ref, qs_ref, cpl_ref, e_ref, bg_ref, u_ref, t_ref):
    cells = part_ref.shape[1]

    def tail(u, off, sl, acc):
        bg = bg_ref[:, sl]
        t_ref[:, sl] = bg[0:1] * u[0:1] + bg[1:2] * u[1:2]
        return acc

    body = _far_common(part_ref, qs_ref, cpl_ref, e_ref, u_ref, tail)
    lax.fori_loop(0, cells // CHUNK, body, 0)


def _call(kernel, outs, args, flops, name):
    leaves = outs if isinstance(outs, tuple) else (outs,)
    nbytes = sum(a.size * a.dtype.itemsize for a in args) + sum(
        o.size * jnp.dtype(o.dtype).itemsize for o in leaves
    )
    return pl.pallas_call(
        kernel,
        out_shape=outs,
        compiler_params=pltpu.CompilerParams(vmem_limit_bytes=VMEM_LIMIT),
        cost_estimate=pl.CostEstimate(flops=flops, bytes_accessed=nbytes, transcendentals=0),
        name=name,
    )(*args)


def _exchange(send, idx, devices, cap):
    total = send.size
    got = lax.all_to_all(send.reshape(devices, total // devices), "cells", 0, 0)
    got = got.reshape(devices * cap, total // (devices * cap))
    return got[idx].T


def _exchange_all(send, devices, clusters, rank2, cap, groups, src_index):
    total = send.size
    got = lax.all_to_all(send.reshape(devices, total // devices), "cells", 0, 0)
    lanes = send.shape[1]
    got = got.reshape(devices, total // (devices * lanes), lanes)
    rr = got[:, -1, :cap]
    table = got[:, :-1, :].reshape(devices, rank2, clusters).transpose(1, 0, 2)
    return table.reshape(rank2, devices * clusters)[:, src_index], rr


def per_device(
    adj_source,
    contrast,
    background,
    near_blocks,
    near_list,
    proj_basis,
    expand_basis,
    coupling,
    far_owner,
    far_slot,
):
    devices = lax.axis_size("cells")
    clusters = near_list.shape[0]
    cells = contrast.shape[1]
    width = cells // clusters
    npairs = far_slot.shape[0]
    cap = 32

    src = adj_source[0]
    cst = contrast
    nb = near_blocks[0]
    pb = proj_basis[0]
    eb = expand_basis[0]
    cp = coupling[0]
    bg = background[0]

    me = lax.axis_index("cells")
    local_list = near_list - me * clusters
    nlc = jnp.repeat(local_list.T, width, axis=1)

    groups = 4
    src_index = far_owner[:, 0] * clusters + far_slot

    nsend = devices * cap
    rank2 = 2 * pb.shape[1]
    q_shape = jax.ShapeDtypeStruct((rank2, clusters), F32)
    field_shape = jax.ShapeDtypeStruct((2, cells), F32)

    first_shape = jax.ShapeDtypeStruct((devices * (clusters // groups + 1), groups * rank2), F32)
    idx, send = _call(
        _proj_pack_kernel,
        (jax.ShapeDtypeStruct((1, npairs), jnp.int32), first_shape),
        (src, cst, pb, far_owner.reshape(1, npairs), far_slot.reshape(1, npairs)),
        4 * rank2 * cells + 2 * devices * npairs * npairs,
        "proj_pack",
    )
    idx = idx.reshape(npairs)
    send_shape = jax.ShapeDtypeStruct((devices * cap // groups, groups * rank2), F32)
    field = src
    for step in range(ITERS):
        if step == 0:
            qs, rr = _exchange_all(send, devices, clusters, rank2, cap, groups, src_index)
        else:
            qs = _exchange(send, idx, devices, cap)
        part = _call(
            _near_kernel, field_shape, (field, cst, nb, nlc, src), 8 * nb.shape[1] * cells, "near"
        )
        if step < ITERS - 1:
            field, send = _call(
                _far_proj_kernel,
                (field_shape, send_shape),
                (part, qs, cp, eb, cst, pb, rr),
                8 * cp.size,
                "far_proj",
            )
        else:
            field, terms = _call(
                _far_grad_kernel,
                (field_shape, jax.ShapeDtypeStruct((1, cells), F32)),
                (part, qs, cp, eb, bg),
                8 * cp.size,
                "far_grad",
            )
    freqs = lax.axis_size("freq")
    mine = terms[0]
    got = [mine] + [
        lax.ppermute(mine, "freq", [(i, (i + k) % freqs) for i in range(freqs)])
        for k in range(1, freqs)
    ]
    stacked = jnp.stack(got)
    f = lax.axis_index("freq")
    total = stacked[(f - 0) % freqs]
    for src in range(1, freqs):
        total = total + stacked[(f - src) % freqs]
    return (field[None], total)


def solution(mesh):
    return jax.shard_map(
        per_device,
        mesh=mesh,
        in_specs=(
            P("freq", None, "cells"),
            P("freq", "cells"),
            P("freq", None, "cells"),
            P("freq", None, None, "cells"),
            P("cells", None),
            P("freq", None, None, "cells"),
            P("freq", None, None, "cells"),
            P("freq", None, None, None, "cells"),
            P("cells", None),
            P("cells"),
        ),
        out_specs=(P("freq", None, "cells"), P("cells")),
        check_vma=False,
    )
```

```python
import jax
import jax.numpy as jnp
from jax import lax
from jax.experimental import pallas as pl
from jax.experimental.pallas import tpu as pltpu
from jax.sharding import PartitionSpec as P

ITERS = 2
F32 = jnp.float32
BF16 = jnp.bfloat16
CHUNK = 512
PAIR_CHUNK = 128
VMEM_LIMIT = 56 * 1024 * 1024


def _split3(a):
    hi = a.astype(BF16)
    r = a - hi.astype(F32)
    mid = r.astype(BF16)
    lo = (r - mid.astype(F32)).astype(BF16)
    return jnp.concatenate([hi, mid, lo], axis=0)


def _sdot(split, onehot):
    m = split.shape[0] // 3
    r = jnp.dot(split, onehot, preferred_element_type=F32)
    return r[:m] + r[m : 2 * m] + r[2 * m :]


def _xdot(a, onehot):
    return _sdot(_split3(a), onehot)


def _iota(shape, dim):
    return lax.broadcasted_iota(jnp.int32, shape, dim)


def _weighted_proj(u, c, pre, pim):
    wre = u[0:1] * c
    wim = u[1:2] * c
    return jnp.concatenate([pre * wre - pim * wim, pre * wim + pim * wre], axis=0)


def _proj_chunk(pw, off, clusters, width):
    n = pw.shape[1]
    seg = ((_iota((n, clusters), 0) + off) // width) == _iota((n, clusters), 1)
    return _xdot(pw, seg.astype(BF16))


def _pack(q, rr):
    rank2, clusters = q.shape
    rows, groups = rr.shape
    wide = groups * clusters
    lane = _iota((rows, wide), 1)
    grp = lane // clusters
    want = rr[:, 0:1]
    for g in range(1, groups):
        want = jnp.where(grp == g, rr[:, g : g + 1], want)
    oh = ((lane % clusters).astype(F32) == want).astype(BF16)
    tile = (_iota((clusters, wide), 0) == _iota((clusters, wide), 1) % clusters).astype(BF16)
    qw = _xdot(q, tile)
    qw = jnp.concatenate([qw] * groups, axis=0)
    keep = (_iota((groups * rank2, wide), 0) // rank2) == (_iota((groups * rank2, wide), 1) // clusters)
    qw = jnp.where(keep, qw, 0.0)
    r = lax.dot_general(oh, _split3(qw), (((1,), (1,)), ((), ())), preferred_element_type=F32)
    n = groups * rank2
    return r[:, :n] + r[:, n : 2 * n] + r[:, 2 * n :]


def _prep(or_ref, sr_ref, idx_ref, devices, cap):
    n = or_ref.shape[1]
    oht = _iota((devices, n), 0) == or_ref[...]
    upper = (_iota((n, n), 0) < _iota((n, n), 1)).astype(BF16)
    counts = jnp.dot(oht.astype(BF16), upper, preferred_element_type=F32)
    pos = jnp.sum(jnp.where(oht, counts, 0.0), axis=0, keepdims=True).astype(jnp.int32)
    idx_ref[...] = or_ref[...] * cap + pos
    pkt = (_iota((cap, n), 0) == pos).astype(BF16)
    ohs = jnp.where(oht, sr_ref[...].astype(F32), 0.0).astype(BF16)
    return lax.dot_general(ohs, pkt, (((1,), (1,)), ((), ())), preferred_element_type=F32)


def _proj_pack_kernel(u_ref, c_ref, p_ref, or_ref, sr_ref, idx_ref, send_ref):
    cells = u_ref.shape[1]
    clusters = cells // 64
    rank2 = 2 * p_ref.shape[1]
    lanes = send_ref.shape[1]
    nrow = rank2 * clusters // lanes
    block = nrow + 1
    devices = send_ref.shape[0] // block
    cap = 32
    req = _prep(or_ref, sr_ref, idx_ref, devices, cap)

    def body(ci, q):
        off = pl.multiple_of(ci * CHUNK, CHUNK)
        sl = pl.ds(off, CHUNK)
        pw = _weighted_proj(u_ref[:, sl], c_ref[:, sl], p_ref[0, :, sl], p_ref[1, :, sl])
        return q + _proj_chunk(pw, off, clusters, 64)

    q = lax.fori_loop(0, cells // CHUNK, body, jnp.zeros((rank2, clusters), F32))
    per = lanes // clusters
    hi = q.astype(BF16)
    r1 = q - hi.astype(F32)
    mid = r1.astype(BF16)
    lo = (r1 - mid.astype(F32)).astype(BF16)
    flat = jnp.zeros((nrow, lanes), F32)
    for h in range(per):
        sel = (_iota((nrow, rank2), 1) == _iota((nrow, rank2), 0) * per + h).astype(BF16)
        part = sum(jnp.dot(sel, x, preferred_element_type=F32) for x in (hi, mid, lo))
        place = (_iota((clusters, lanes), 1) == _iota((clusters, lanes), 0) + h * clusters)
        flat = flat + _xdot(part, place.astype(BF16))
    place = (_iota((cap, lanes), 0) == _iota((cap, lanes), 1)).astype(BF16)
    reqrow = jnp.dot(req.astype(BF16), place, preferred_element_type=F32)
    for e in range(devices):
        send_ref[pl.ds(e * block, nrow), :] = flat
        send_ref[pl.ds(e * block + nrow, 1), :] = reqrow[e : e + 1]


def _rr_groups(rr, groups):
    devices, cap = rr.shape
    per = cap // groups
    rows = devices * per
    rep = ((_iota((rows, devices), 0) // per) == _iota((rows, devices), 1)).astype(BF16)
    wide = jnp.dot(rep, rr.astype(BF16), preferred_element_type=F32)
    keep = (_iota((rows, cap), 1) // groups) == (_iota((rows, cap), 0) % per)
    fold = ((_iota((cap, groups), 0) % groups) == _iota((cap, groups), 1)).astype(BF16)
    return jnp.dot(jnp.where(keep, wide, 0.0).astype(BF16), fold, preferred_element_type=F32)


def _near_kernel(u_ref, c_ref, nb_ref, nlc_ref, base_ref, out_ref):
    cells = u_ref.shape[1]
    width = 64
    clusters = cells // width
    near = nlc_ref.shape[0]

    def wt_body(ci, acc):
        off = pl.multiple_of(ci * CHUNK, CHUNK)
        sl = pl.ds(off, CHUNK)
        w = u_ref[:, sl] * c_ref[:, sl]
        sel = _iota((width, CHUNK), 0) == ((_iota((width, CHUNK), 1) + off) % width)
        wm = jnp.concatenate(
            [jnp.where(sel, w[0:1], 0.0), jnp.where(sel, w[1:2], 0.0)], axis=0
        )
        seg = ((_iota((CHUNK, clusters), 0) + off) // width) == _iota((CHUNK, clusters), 1)
        return acc + _xdot(wm, seg.astype(BF16))

    wt = lax.fori_loop(0, cells // CHUNK, wt_body, jnp.zeros((2 * width, clusters), F32))
    wt_split = _split3(wt)

    def near_body(ci, carry):
        off = pl.multiple_of(ci * CHUNK, CHUNK)
        sl = pl.ds(off, CHUNK)
        crow = _iota((clusters, CHUNK), 0)
        acc_re = jnp.zeros((1, CHUNK), F32)
        acc_im = jnp.zeros((1, CHUNK), F32)
        for k in range(near):
            m = (crow == nlc_ref[k : k + 1, sl]).astype(BF16)
            wk = _sdot(wt_split, m)
            wre = wk[:width]
            wim = wk[width:]
            nre = nb_ref[0, pl.ds(k * width, width), sl]
            nim = nb_ref[1, pl.ds(k * width, width), sl]
            acc_re = acc_re + jnp.sum(nre * wre - nim * wim, axis=0, keepdims=True)
            acc_im = acc_im + jnp.sum(nre * wim + nim * wre, axis=0, keepdims=True)
        out_ref[:, sl] = base_ref[:, sl] + jnp.concatenate([acc_re, acc_im], axis=0)
        return carry

    lax.fori_loop(0, cells // CHUNK, near_body, 0)


def _far_common(part_ref, qs_ref, cpl_ref, e_ref, u_ref, chunk_tail):
    cells = part_ref.shape[1]
    width = 64
    clusters = cells // width
    rank = cpl_ref.shape[1]
    npairs = qs_ref.shape[1]
    far = npairs // clusters

    def pair_body(pj, z):
        off = pl.multiple_of(pj * PAIR_CHUNK, PAIR_CHUNK)
        sl = pl.ds(off, PAIR_CHUNK)
        qs = qs_ref[:, sl]
        zre = jnp.zeros((rank, PAIR_CHUNK), F32)
        zim = jnp.zeros((rank, PAIR_CHUNK), F32)
        for i in range(rank):
            cre = cpl_ref[0, i, :, sl]
            cim = cpl_ref[1, i, :, sl]
            qre = qs[i : i + 1]
            qim = qs[rank + i : rank + i + 1]
            zre = zre + (cre * qre - cim * qim)
            zim = zim + (cre * qim + cim * qre)
        seg = ((_iota((PAIR_CHUNK, clusters), 0) + off) // far) == _iota((PAIR_CHUNK, clusters), 1)
        return z + _xdot(jnp.concatenate([zre, zim], axis=0), seg.astype(BF16))

    z = lax.fori_loop(0, npairs // PAIR_CHUNK, pair_body, jnp.zeros((2 * rank, clusters), F32))
    z_split = _split3(z)

    def cell_body(ci, acc):
        off = pl.multiple_of(ci * CHUNK, CHUNK)
        sl = pl.ds(off, CHUNK)
        spread = _iota((clusters, CHUNK), 0) == ((_iota((clusters, CHUNK), 1) + off) // width)
        zz = _sdot(z_split, spread.astype(BF16))
        zre = zz[:rank]
        zim = zz[rank:]
        ere = e_ref[0, :, sl]
        eim = e_ref[1, :, sl]
        far_re = jnp.sum(ere * zre - eim * zim, axis=0, keepdims=True)
        far_im = jnp.sum(ere * zim + eim * zre, axis=0, keepdims=True)
        u = part_ref[:, sl] + jnp.concatenate([far_re, far_im], axis=0)
        u_ref[:, sl] = u
        return chunk_tail(u, off, sl, acc)

    return cell_body


def _far_proj_kernel(part_ref, qs_ref, cpl_ref, e_ref, c_ref, p_ref, rr_ref, u_ref, send_ref):
    cells = part_ref.shape[1]
    clusters = cells // 64
    rank2 = 2 * p_ref.shape[1]

    def tail(u, off, sl, q):
        pw = _weighted_proj(u, c_ref[:, sl], p_ref[0, :, sl], p_ref[1, :, sl])
        return q + _proj_chunk(pw, off, clusters, 64)

    body = _far_common(part_ref, qs_ref, cpl_ref, e_ref, u_ref, tail)
    q = lax.fori_loop(0, cells // CHUNK, body, jnp.zeros((rank2, clusters), F32))
    send_ref[...] = _pack(q, _rr_groups(rr_ref[...], send_ref.shape[1] // rank2))


def _far_grad_kernel(part_ref, qs_ref, cpl_ref, e_ref, bg_ref, u_ref, t_ref):
    cells = part_ref.shape[1]

    def tail(u, off, sl, acc):
        bg = bg_ref[:, sl]
        t_ref[:, sl] = bg[0:1] * u[0:1] + bg[1:2] * u[1:2]
        return acc

    body = _far_common(part_ref, qs_ref, cpl_ref, e_ref, u_ref, tail)
    lax.fori_loop(0, cells // CHUNK, body, 0)


def _call(kernel, outs, args, flops, name):
    leaves = outs if isinstance(outs, tuple) else (outs,)
    nbytes = sum(a.size * a.dtype.itemsize for a in args) + sum(
        o.size * jnp.dtype(o.dtype).itemsize for o in leaves
    )
    return pl.pallas_call(
        kernel,
        out_shape=outs,
        compiler_params=pltpu.CompilerParams(vmem_limit_bytes=VMEM_LIMIT),
        cost_estimate=pl.CostEstimate(flops=flops, bytes_accessed=nbytes, transcendentals=0),
        name=name,
    )(*args)


def _exchange(send, idx, devices, cap):
    total = send.size
    got = lax.all_to_all(send.reshape(devices, total // devices), "cells", 0, 0)
    got = got.reshape(devices * cap, total // (devices * cap))
    return got[idx].T


def _exchange_all(send, devices, clusters, rank2, cap, groups, src_index):
    total = send.size
    got = lax.all_to_all(send.reshape(devices, total // devices), "cells", 0, 0)
    lanes = send.shape[1]
    got = got.reshape(devices, total // (devices * lanes), lanes)
    rr = got[:, -1, :cap]
    table = got[:, :-1, :].reshape(devices, rank2, clusters).transpose(1, 0, 2)
    return table.reshape(rank2, devices * clusters)[:, src_index], rr


def per_device(
    adj_source,
    contrast,
    background,
    near_blocks,
    near_list,
    proj_basis,
    expand_basis,
    coupling,
    far_owner,
    far_slot,
):
    devices = lax.axis_size("cells")
    clusters = near_list.shape[0]
    cells = contrast.shape[1]
    width = cells // clusters
    npairs = far_slot.shape[0]
    cap = 32

    src = adj_source[0]
    cst = contrast
    nb = near_blocks[0]
    pb = proj_basis[0]
    eb = expand_basis[0]
    cp = jnp.transpose(coupling[0], (0, 2, 1, 3))
    bg = background[0]

    me = lax.axis_index("cells")
    local_list = near_list - me * clusters
    nlc = jnp.repeat(local_list.T, width, axis=1)

    groups = 4
    src_index = far_owner[:, 0] * clusters + far_slot

    nsend = devices * cap
    rank2 = 2 * pb.shape[1]
    q_shape = jax.ShapeDtypeStruct((rank2, clusters), F32)
    field_shape = jax.ShapeDtypeStruct((2, cells), F32)

    first_shape = jax.ShapeDtypeStruct((devices * (clusters // groups + 1), groups * rank2), F32)
    idx, send = _call(
        _proj_pack_kernel,
        (jax.ShapeDtypeStruct((1, npairs), jnp.int32), first_shape),
        (src, cst, pb, far_owner.reshape(1, npairs), far_slot.reshape(1, npairs)),
        4 * rank2 * cells + 2 * devices * npairs * npairs,
        "proj_pack",
    )
    idx = idx.reshape(npairs)
    send_shape = jax.ShapeDtypeStruct((devices * cap // groups, groups * rank2), F32)
    field = src
    for step in range(ITERS):
        if step == 0:
            qs, rr = _exchange_all(send, devices, clusters, rank2, cap, groups, src_index)
        else:
            qs = _exchange(send, idx, devices, cap)
        part = _call(
            _near_kernel, field_shape, (field, cst, nb, nlc, src), 8 * nb.shape[1] * cells, "near"
        )
        if step < ITERS - 1:
            field, send = _call(
                _far_proj_kernel,
                (field_shape, send_shape),
                (part, qs, cp, eb, cst, pb, rr),
                8 * cp.size,
                "far_proj",
            )
        else:
            field, terms = _call(
                _far_grad_kernel,
                (field_shape, jax.ShapeDtypeStruct((1, cells), F32)),
                (part, qs, cp, eb, bg),
                8 * cp.size,
                "far_grad",
            )
    freqs = lax.axis_size("freq")
    mine = terms[0]
    got = [mine] + [
        lax.ppermute(mine, "freq", [(i, (i + k) % freqs) for i in range(freqs)])
        for k in range(1, freqs)
    ]
    stacked = jnp.stack(got)
    f = lax.axis_index("freq")
    total = stacked[(f - 0) % freqs]
    for src in range(1, freqs):
        total = total + stacked[(f - src) % freqs]
    return (field[None], total)


def solution(mesh):
    return jax.shard_map(
        per_device,
        mesh=mesh,
        in_specs=(
            P("freq", None, "cells"),
            P("freq", "cells"),
            P("freq", None, "cells"),
            P("freq", None, None, "cells"),
            P("cells", None),
            P("freq", None, None, "cells"),
            P("freq", None, None, "cells"),
            P("freq", None, None, None, "cells"),
            P("cells", None),
            P("cells"),
        ),
        out_specs=(P("freq", None, "cells"), P("cells")),
        check_vma=False,
    )
```

```python
import jax
import jax.numpy as jnp
from jax import lax
from jax.experimental import pallas as pl
from jax.experimental.pallas import tpu as pltpu
from jax.sharding import PartitionSpec as P

ITERS = 2
F32 = jnp.float32
BF16 = jnp.bfloat16
CHUNK = 512
PAIR_CHUNK = 128
VMEM_LIMIT = 56 * 1024 * 1024


def _split3(a):
    hi = a.astype(BF16)
    r = a - hi.astype(F32)
    mid = r.astype(BF16)
    lo = (r - mid.astype(F32)).astype(BF16)
    return jnp.concatenate([hi, mid, lo], axis=0)


def _sdot(split, onehot):
    m = split.shape[0] // 3
    r = jnp.dot(split, onehot, preferred_element_type=F32)
    return r[:m] + r[m : 2 * m] + r[2 * m :]


def _xdot(a, onehot):
    return _sdot(_split3(a), onehot)


def _iota(shape, dim):
    return lax.broadcasted_iota(jnp.int32, shape, dim)


def _weighted_proj(u, c, pre, pim):
    wre = u[0:1] * c
    wim = u[1:2] * c
    return jnp.concatenate([pre * wre - pim * wim, pre * wim + pim * wre], axis=0)


def _proj_chunk(pw, off, clusters, width):
    n = pw.shape[1]
    seg = ((_iota((n, clusters), 0) + off) // width) == _iota((n, clusters), 1)
    return _xdot(pw, seg.astype(BF16))


def _pack(q, rr):
    rank2, clusters = q.shape
    rows, groups = rr.shape
    wide = groups * clusters
    lane = _iota((rows, wide), 1)
    grp = lane // clusters
    want = rr[:, 0:1]
    for g in range(1, groups):
        want = jnp.where(grp == g, rr[:, g : g + 1], want)
    oh = ((lane % clusters).astype(F32) == want).astype(BF16)
    tile = (_iota((clusters, wide), 0) == _iota((clusters, wide), 1) % clusters).astype(BF16)
    qw = _xdot(q, tile)
    qw = jnp.concatenate([qw] * groups, axis=0)
    keep = (_iota((groups * rank2, wide), 0) // rank2) == (_iota((groups * rank2, wide), 1) // clusters)
    qw = jnp.where(keep, qw, 0.0)
    r = lax.dot_general(oh, _split3(qw), (((1,), (1,)), ((), ())), preferred_element_type=F32)
    n = groups * rank2
    return r[:, :n] + r[:, n : 2 * n] + r[:, 2 * n :]


def _prep(or_ref, sr_ref, idx_ref, devices, cap):
    n = or_ref.shape[1]
    oht = _iota((devices, n), 0) == or_ref[...]
    upper = (_iota((n, n), 0) < _iota((n, n), 1)).astype(BF16)
    counts = jnp.dot(oht.astype(BF16), upper, preferred_element_type=F32)
    pos = jnp.sum(jnp.where(oht, counts, 0.0), axis=0, keepdims=True).astype(jnp.int32)
    idx_ref[...] = or_ref[...] * cap + pos
    pkt = (_iota((cap, n), 0) == pos).astype(BF16)
    ohs = jnp.where(oht, sr_ref[...].astype(F32), 0.0).astype(BF16)
    return lax.dot_general(ohs, pkt, (((1,), (1,)), ((), ())), preferred_element_type=F32)


def _proj_pack_kernel(u_ref, c_ref, p_ref, or_ref, sr_ref, idx_ref, send_ref):
    cells = u_ref.shape[1]
    clusters = cells // 64
    rank2 = 2 * p_ref.shape[1]
    lanes = send_ref.shape[1]
    nrow = rank2 * clusters // lanes
    block = nrow + 1
    devices = send_ref.shape[0] // block
    cap = 32
    req = _prep(or_ref, sr_ref, idx_ref, devices, cap)

    def body(ci, q):
        off = pl.multiple_of(ci * CHUNK, CHUNK)
        sl = pl.ds(off, CHUNK)
        pw = _weighted_proj(u_ref[:, sl], c_ref[:, sl], p_ref[0, :, sl], p_ref[1, :, sl])
        return q + _proj_chunk(pw, off, clusters, 64)

    q = lax.fori_loop(0, cells // CHUNK, body, jnp.zeros((rank2, clusters), F32))
    per = lanes // clusters
    hi = q.astype(BF16)
    r1 = q - hi.astype(F32)
    mid = r1.astype(BF16)
    lo = (r1 - mid.astype(F32)).astype(BF16)
    flat = jnp.zeros((nrow, lanes), F32)
    for h in range(per):
        sel = (_iota((nrow, rank2), 1) == _iota((nrow, rank2), 0) * per + h).astype(BF16)
        part = sum(jnp.dot(sel, x, preferred_element_type=F32) for x in (hi, mid, lo))
        place = (_iota((clusters, lanes), 1) == _iota((clusters, lanes), 0) + h * clusters)
        flat = flat + _xdot(part, place.astype(BF16))
    place = (_iota((cap, lanes), 0) == _iota((cap, lanes), 1)).astype(BF16)
    reqrow = jnp.dot(req.astype(BF16), place, preferred_element_type=F32)
    for e in range(devices):
        send_ref[pl.ds(e * block, nrow), :] = flat
        send_ref[pl.ds(e * block + nrow, 1), :] = reqrow[e : e + 1]


def _rr_groups(rr, groups):
    devices, cap = rr.shape
    per = cap // groups
    rows = devices * per
    rep = ((_iota((rows, devices), 0) // per) == _iota((rows, devices), 1)).astype(BF16)
    wide = jnp.dot(rep, rr.astype(BF16), preferred_element_type=F32)
    keep = (_iota((rows, cap), 1) // groups) == (_iota((rows, cap), 0) % per)
    fold = ((_iota((cap, groups), 0) % groups) == _iota((cap, groups), 1)).astype(BF16)
    return jnp.dot(jnp.where(keep, wide, 0.0).astype(BF16), fold, preferred_element_type=F32)


def _near_kernel(u_ref, c_ref, nb_ref, nlc_ref, base_ref, out_ref):
    cells = u_ref.shape[1]
    width = 64
    clusters = cells // width
    near = nlc_ref.shape[0]

    def wt_body(ci, acc):
        off = pl.multiple_of(ci * CHUNK, CHUNK)
        sl = pl.ds(off, CHUNK)
        w = u_ref[:, sl] * c_ref[:, sl]
        sel = _iota((width, CHUNK), 0) == ((_iota((width, CHUNK), 1) + off) % width)
        wm = jnp.concatenate(
            [jnp.where(sel, w[0:1], 0.0), jnp.where(sel, w[1:2], 0.0)], axis=0
        )
        seg = ((_iota((CHUNK, clusters), 0) + off) // width) == _iota((CHUNK, clusters), 1)
        return acc + _xdot(wm, seg.astype(BF16))

    wt = lax.fori_loop(0, cells // CHUNK, wt_body, jnp.zeros((2 * width, clusters), F32))
    wt_split = _split3(wt)

    def near_body(ci, carry):
        off = pl.multiple_of(ci * CHUNK, CHUNK)
        sl = pl.ds(off, CHUNK)
        crow = _iota((clusters, CHUNK), 0)
        acc_re = jnp.zeros((1, CHUNK), F32)
        acc_im = jnp.zeros((1, CHUNK), F32)
        for k in range(near):
            m = (crow == nlc_ref[k : k + 1, sl]).astype(BF16)
            wk = _sdot(wt_split, m)
            wre = wk[:width]
            wim = wk[width:]
            nre = nb_ref[0, pl.ds(k * width, width), sl]
            nim = nb_ref[1, pl.ds(k * width, width), sl]
            acc_re = acc_re + jnp.sum(nre * wre - nim * wim, axis=0, keepdims=True)
            acc_im = acc_im + jnp.sum(nre * wim + nim * wre, axis=0, keepdims=True)
        out_ref[:, sl] = base_ref[:, sl] + jnp.concatenate([acc_re, acc_im], axis=0)
        return carry

    lax.fori_loop(0, cells // CHUNK, near_body, 0)


def _far_common(part_ref, qs_ref, cpl_ref, e_ref, u_ref, chunk_tail):
    cells = part_ref.shape[1]
    width = 64
    clusters = cells // width
    rank = cpl_ref.shape[1]
    npairs = qs_ref.shape[1]
    far = npairs // clusters

    def pair_body(pj, z):
        off = pl.multiple_of(pj * PAIR_CHUNK, PAIR_CHUNK)
        sl = pl.ds(off, PAIR_CHUNK)
        qs = qs_ref[:, sl]
        qre = qs[:rank][None]
        qim = qs[rank:][None]
        cre = cpl_ref[0, :, :, sl]
        cim = cpl_ref[1, :, :, sl]
        zre = jnp.sum(cre * qre - cim * qim, axis=1)
        zim = jnp.sum(cre * qim + cim * qre, axis=1)
        seg = ((_iota((PAIR_CHUNK, clusters), 0) + off) // far) == _iota((PAIR_CHUNK, clusters), 1)
        return z + _xdot(jnp.concatenate([zre, zim], axis=0), seg.astype(BF16))

    z = lax.fori_loop(0, npairs // PAIR_CHUNK, pair_body, jnp.zeros((2 * rank, clusters), F32))
    z_split = _split3(z)

    def cell_body(ci, acc):
        off = pl.multiple_of(ci * CHUNK, CHUNK)
        sl = pl.ds(off, CHUNK)
        spread = _iota((clusters, CHUNK), 0) == ((_iota((clusters, CHUNK), 1) + off) // width)
        zz = _sdot(z_split, spread.astype(BF16))
        zre = zz[:rank]
        zim = zz[rank:]
        ere = e_ref[0, :, sl]
        eim = e_ref[1, :, sl]
        far_re = jnp.sum(ere * zre - eim * zim, axis=0, keepdims=True)
        far_im = jnp.sum(ere * zim + eim * zre, axis=0, keepdims=True)
        u = part_ref[:, sl] + jnp.concatenate([far_re, far_im], axis=0)
        u_ref[:, sl] = u
        return chunk_tail(u, off, sl, acc)

    return cell_body


def _far_proj_kernel(part_ref, qs_ref, cpl_ref, e_ref, c_ref, p_ref, rr_ref, u_ref, send_ref):
    cells = part_ref.shape[1]
    clusters = cells // 64
    rank2 = 2 * p_ref.shape[1]

    def tail(u, off, sl, q):
        pw = _weighted_proj(u, c_ref[:, sl], p_ref[0, :, sl], p_ref[1, :, sl])
        return q + _proj_chunk(pw, off, clusters, 64)

    body = _far_common(part_ref, qs_ref, cpl_ref, e_ref, u_ref, tail)
    q = lax.fori_loop(0, cells // CHUNK, body, jnp.zeros((rank2, clusters), F32))
    send_ref[...] = _pack(q, _rr_groups(rr_ref[...], send_ref.shape[1] // rank2))


def _far_grad_kernel(part_ref, qs_ref, cpl_ref, e_ref, bg_ref, u_ref, t_ref):
    cells = part_ref.shape[1]

    def tail(u, off, sl, acc):
        bg = bg_ref[:, sl]
        t_ref[:, sl] = bg[0:1] * u[0:1] + bg[1:2] * u[1:2]
        return acc

    body = _far_common(part_ref, qs_ref, cpl_ref, e_ref, u_ref, tail)
    lax.fori_loop(0, cells // CHUNK, body, 0)


def _call(kernel, outs, args, flops, name, resident=False):
    leaves = outs if isinstance(outs, tuple) else (outs,)
    nbytes = sum(a.size * a.dtype.itemsize for a in args) + sum(
        o.size * jnp.dtype(o.dtype).itemsize for o in leaves
    )
    extra = {}
    limit = VMEM_LIMIT
    if resident:
        extra["in_specs"] = [pl.BlockSpec(memory_space=pltpu.VMEM)] * len(args)
        limit = 24 * 1024 * 1024
    return pl.pallas_call(
        kernel,
        out_shape=outs,
        **extra,
        compiler_params=pltpu.CompilerParams(vmem_limit_bytes=limit),
        cost_estimate=pl.CostEstimate(flops=flops, bytes_accessed=nbytes, transcendentals=0),
        name=name,
    )(*args)


def _exchange(send, idx, devices, cap):
    total = send.size
    got = lax.all_to_all(send.reshape(devices, total // devices), "cells", 0, 0)
    got = got.reshape(devices * cap, total // (devices * cap))
    return got[idx].T


def _exchange_all(send, devices, clusters, rank2, cap, groups, src_index):
    total = send.size
    got = lax.all_to_all(send.reshape(devices, total // devices), "cells", 0, 0)
    lanes = send.shape[1]
    got = got.reshape(devices, total // (devices * lanes), lanes)
    rr = got[:, -1, :cap]
    table = got[:, :-1, :].reshape(devices, rank2, clusters).transpose(1, 0, 2)
    return table.reshape(rank2, devices * clusters)[:, src_index], rr


def per_device(
    adj_source,
    contrast,
    background,
    near_blocks,
    near_list,
    proj_basis,
    expand_basis,
    coupling,
    far_owner,
    far_slot,
):
    devices = lax.axis_size("cells")
    clusters = near_list.shape[0]
    cells = contrast.shape[1]
    width = cells // clusters
    npairs = far_slot.shape[0]
    cap = 32

    src = adj_source[0]
    cst = contrast
    nb = near_blocks[0]
    pb = proj_basis[0]
    eb = expand_basis[0]
    cp = coupling[0]
    bg = background[0]

    me = lax.axis_index("cells")
    local_list = near_list - me * clusters
    nlc = jnp.repeat(local_list.T, width, axis=1)

    groups = 4
    src_index = far_owner[:, 0] * clusters + far_slot

    nsend = devices * cap
    rank2 = 2 * pb.shape[1]
    q_shape = jax.ShapeDtypeStruct((rank2, clusters), F32)
    field_shape = jax.ShapeDtypeStruct((2, cells), F32)

    first_shape = jax.ShapeDtypeStruct((devices * (clusters // groups + 1), groups * rank2), F32)
    idx, send = _call(
        _proj_pack_kernel,
        (jax.ShapeDtypeStruct((1, npairs), jnp.int32), first_shape),
        (src, cst, pb, far_owner.reshape(1, npairs), far_slot.reshape(1, npairs)),
        4 * rank2 * cells + 2 * devices * npairs * npairs,
        "proj_pack",
    )
    idx = idx.reshape(npairs)
    send_shape = jax.ShapeDtypeStruct((devices * cap // groups, groups * rank2), F32)
    field = src
    for step in range(ITERS):
        if step == 0:
            qs, rr = _exchange_all(send, devices, clusters, rank2, cap, groups, src_index)
        else:
            qs = _exchange(send, idx, devices, cap)
        part = _call(
            _near_kernel, field_shape, (field, cst, nb, nlc, src), 8 * nb.shape[1] * cells, "near"
        )
        if step < ITERS - 1:
            field, send = _call(
                _far_proj_kernel,
                (field_shape, send_shape),
                (part, qs, cp, eb, cst, pb, rr),
                8 * cp.size,
                "far_proj",
                resident=True,
            )
        else:
            field, terms = _call(
                _far_grad_kernel,
                (field_shape, jax.ShapeDtypeStruct((1, cells), F32)),
                (part, qs, cp, eb, bg),
                8 * cp.size,
                "far_grad",
                resident=True,
            )
    freqs = lax.axis_size("freq")
    mine = terms[0]
    got = [mine] + [
        lax.ppermute(mine, "freq", [(i, (i + k) % freqs) for i in range(freqs)])
        for k in range(1, freqs)
    ]
    stacked = jnp.stack(got)
    f = lax.axis_index("freq")
    total = stacked[(f - 0) % freqs]
    for src in range(1, freqs):
        total = total + stacked[(f - src) % freqs]
    return (field[None], total)


def solution(mesh):
    return jax.shard_map(
        per_device,
        mesh=mesh,
        in_specs=(
            P("freq", None, "cells"),
            P("freq", "cells"),
            P("freq", None, "cells"),
            P("freq", None, None, "cells"),
            P("cells", None),
            P("freq", None, None, "cells"),
            P("freq", None, None, "cells"),
            P("freq", None, None, None, "cells"),
            P("cells", None),
            P("cells"),
        ),
        out_specs=(P("freq", None, "cells"), P("cells")),
        check_vma=False,
    )
```

```python
import jax
import jax.numpy as jnp
from jax import lax
from jax.experimental import pallas as pl
from jax.experimental.pallas import tpu as pltpu
from jax.sharding import PartitionSpec as P

ITERS = 2
F32 = jnp.float32
BF16 = jnp.bfloat16
CHUNK = 512
PAIR_CHUNK = 128
VMEM_LIMIT = 56 * 1024 * 1024


def _split3(a):
    hi = a.astype(BF16)
    r = a - hi.astype(F32)
    mid = r.astype(BF16)
    lo = (r - mid.astype(F32)).astype(BF16)
    return jnp.concatenate([hi, mid, lo], axis=0)


def _sdot(split, onehot):
    m = split.shape[0] // 3
    r = jnp.dot(split, onehot, preferred_element_type=F32)
    return r[:m] + r[m : 2 * m] + r[2 * m :]


def _xdot(a, onehot):
    return _sdot(_split3(a), onehot)


def _iota(shape, dim):
    return lax.broadcasted_iota(jnp.int32, shape, dim)


def _div(x, d):
    return x >> (d.bit_length() - 1) if d & (d - 1) == 0 else x // d


def _mod(x, d):
    return x & (d - 1) if d & (d - 1) == 0 else x % d


def _weighted_proj(u, c, pre, pim):
    wre = u[0:1] * c
    wim = u[1:2] * c
    return jnp.concatenate([pre * wre - pim * wim, pre * wim + pim * wre], axis=0)


def _proj_chunk(pw, off, clusters, width):
    n = pw.shape[1]
    seg = _div(_iota((n, clusters), 0) + off, width) == _iota((n, clusters), 1)
    return _xdot(pw, seg.astype(BF16))


def _pack(q, rr):
    rank2, clusters = q.shape
    rows, groups = rr.shape
    wide = groups * clusters
    lane = _iota((rows, wide), 1)
    grp = _div(lane, clusters)
    want = rr[:, 0:1]
    for g in range(1, groups):
        want = jnp.where(grp == g, rr[:, g : g + 1], want)
    oh = (_mod(lane, clusters).astype(F32) == want).astype(BF16)
    tile = (_iota((clusters, wide), 0) == _mod(_iota((clusters, wide), 1), clusters)).astype(BF16)
    qw = _xdot(q, tile)
    qw = jnp.concatenate([qw] * groups, axis=0)
    keep = _div(_iota((groups * rank2, wide), 0), rank2) == _div(_iota((groups * rank2, wide), 1), clusters)
    qw = jnp.where(keep, qw, 0.0)
    r = lax.dot_general(oh, _split3(qw), (((1,), (1,)), ((), ())), preferred_element_type=F32)
    n = groups * rank2
    return r[:, :n] + r[:, n : 2 * n] + r[:, 2 * n :]


def _prep(or_ref, sr_ref, idx_ref, devices, cap):
    n = or_ref.shape[1]
    oht = _iota((devices, n), 0) == or_ref[...]
    upper = (_iota((n, n), 0) < _iota((n, n), 1)).astype(BF16)
    counts = jnp.dot(oht.astype(BF16), upper, preferred_element_type=F32)
    pos = jnp.sum(jnp.where(oht, counts, 0.0), axis=0, keepdims=True).astype(jnp.int32)
    idx_ref[...] = or_ref[...] * cap + pos
    pkt = (_iota((cap, n), 0) == pos).astype(BF16)
    ohs = jnp.where(oht, sr_ref[...].astype(F32), 0.0).astype(BF16)
    return lax.dot_general(ohs, pkt, (((1,), (1,)), ((), ())), preferred_element_type=F32)


def _proj_pack_kernel(u_ref, c_ref, p_ref, or_ref, sr_ref, idx_ref, send_ref):
    cells = u_ref.shape[1]
    clusters = cells // 64
    rank2 = 2 * p_ref.shape[1]
    lanes = send_ref.shape[1]
    nrow = rank2 * clusters // lanes
    block = nrow + 1
    devices = send_ref.shape[0] // block
    cap = 32
    req = _prep(or_ref, sr_ref, idx_ref, devices, cap)

    def body(ci, q):
        off = pl.multiple_of(ci * CHUNK, CHUNK)
        sl = pl.ds(off, CHUNK)
        pw = _weighted_proj(u_ref[:, sl], c_ref[:, sl], p_ref[0, :, sl], p_ref[1, :, sl])
        return q + _proj_chunk(pw, off, clusters, 64)

    q = lax.fori_loop(0, cells // CHUNK, body, jnp.zeros((rank2, clusters), F32))
    per = lanes // clusters
    hi = q.astype(BF16)
    r1 = q - hi.astype(F32)
    mid = r1.astype(BF16)
    lo = (r1 - mid.astype(F32)).astype(BF16)
    flat = jnp.zeros((nrow, lanes), F32)
    for h in range(per):
        sel = (_iota((nrow, rank2), 1) == _iota((nrow, rank2), 0) * per + h).astype(BF16)
        part = sum(jnp.dot(sel, x, preferred_element_type=F32) for x in (hi, mid, lo))
        place = (_iota((clusters, lanes), 1) == _iota((clusters, lanes), 0) + h * clusters)
        flat = flat + _xdot(part, place.astype(BF16))
    place = (_iota((cap, lanes), 0) == _iota((cap, lanes), 1)).astype(BF16)
    reqrow = jnp.dot(req.astype(BF16), place, preferred_element_type=F32)
    for e in range(devices):
        send_ref[pl.ds(e * block, nrow), :] = flat
        send_ref[pl.ds(e * block + nrow, 1), :] = reqrow[e : e + 1]


def _rr_groups(rr, groups):
    devices, cap = rr.shape
    per = cap // groups
    rows = devices * per
    rep = (_div(_iota((rows, devices), 0), per) == _iota((rows, devices), 1)).astype(BF16)
    wide = jnp.dot(rep, rr.astype(BF16), preferred_element_type=F32)
    keep = _div(_iota((rows, cap), 1), groups) == _mod(_iota((rows, cap), 0), per)
    fold = (_mod(_iota((cap, groups), 0), groups) == _iota((cap, groups), 1)).astype(BF16)
    return jnp.dot(jnp.where(keep, wide, 0.0).astype(BF16), fold, preferred_element_type=F32)


def _near_kernel(u_ref, c_ref, nb_ref, nlc_ref, base_ref, out_ref):
    cells = u_ref.shape[1]
    width = 64
    clusters = cells // width
    near = nlc_ref.shape[0]

    def wt_body(ci, acc):
        off = pl.multiple_of(ci * CHUNK, CHUNK)
        sl = pl.ds(off, CHUNK)
        w = u_ref[:, sl] * c_ref[:, sl]
        sel = _iota((width, CHUNK), 0) == _mod(_iota((width, CHUNK), 1) + off, width)
        wm = jnp.concatenate(
            [jnp.where(sel, w[0:1], 0.0), jnp.where(sel, w[1:2], 0.0)], axis=0
        )
        seg = _div(_iota((CHUNK, clusters), 0) + off, width) == _iota((CHUNK, clusters), 1)
        return acc + _xdot(wm, seg.astype(BF16))

    wt = lax.fori_loop(0, cells // CHUNK, wt_body, jnp.zeros((2 * width, clusters), F32))
    wt_split = _split3(wt)

    def near_body(ci, carry):
        off = pl.multiple_of(ci * CHUNK, CHUNK)
        sl = pl.ds(off, CHUNK)
        crow = _iota((clusters, CHUNK), 0)
        acc_re = jnp.zeros((1, CHUNK), F32)
        acc_im = jnp.zeros((1, CHUNK), F32)
        for k in range(near):
            m = (crow == nlc_ref[k : k + 1, sl]).astype(BF16)
            wk = _sdot(wt_split, m)
            wre = wk[:width]
            wim = wk[width:]
            nre = nb_ref[0, pl.ds(k * width, width), sl]
            nim = nb_ref[1, pl.ds(k * width, width), sl]
            acc_re = acc_re + jnp.sum(nre * wre - nim * wim, axis=0, keepdims=True)
            acc_im = acc_im + jnp.sum(nre * wim + nim * wre, axis=0, keepdims=True)
        out_ref[:, sl] = base_ref[:, sl] + jnp.concatenate([acc_re, acc_im], axis=0)
        return carry

    lax.fori_loop(0, cells // CHUNK, near_body, 0)


def _far_common(part_ref, qs_ref, cpl_ref, e_ref, u_ref, chunk_tail):
    cells = part_ref.shape[1]
    width = 64
    clusters = cells // width
    rank = cpl_ref.shape[1]
    npairs = qs_ref.shape[1]
    far = npairs // clusters

    def pair_body(pj, z):
        off = pl.multiple_of(pj * PAIR_CHUNK, PAIR_CHUNK)
        sl = pl.ds(off, PAIR_CHUNK)
        qs = qs_ref[:, sl]
        qre = qs[:rank][None]
        qim = qs[rank:][None]
        cre = cpl_ref[0, :, :, sl]
        cim = cpl_ref[1, :, :, sl]
        zre = jnp.sum(cre * qre - cim * qim, axis=1)
        zim = jnp.sum(cre * qim + cim * qre, axis=1)
        seg = _div(_iota((PAIR_CHUNK, clusters), 0) + off, far) == _iota((PAIR_CHUNK, clusters), 1)
        return z + _xdot(jnp.concatenate([zre, zim], axis=0), seg.astype(BF16))

    z = lax.fori_loop(0, npairs // PAIR_CHUNK, pair_body, jnp.zeros((2 * rank, clusters), F32))
    z_split = _split3(z)

    def cell_body(ci, acc):
        off = pl.multiple_of(ci * CHUNK, CHUNK)
        sl = pl.ds(off, CHUNK)
        spread = _iota((clusters, CHUNK), 0) == _div(_iota((clusters, CHUNK), 1) + off, width)
        zz = _sdot(z_split, spread.astype(BF16))
        zre = zz[:rank]
        zim = zz[rank:]
        ere = e_ref[0, :, sl]
        eim = e_ref[1, :, sl]
        far_re = jnp.sum(ere * zre - eim * zim, axis=0, keepdims=True)
        far_im = jnp.sum(ere * zim + eim * zre, axis=0, keepdims=True)
        u = part_ref[:, sl] + jnp.concatenate([far_re, far_im], axis=0)
        u_ref[:, sl] = u
        return chunk_tail(u, off, sl, acc)

    return cell_body


def _far_proj_kernel(part_ref, qs_ref, cpl_ref, e_ref, c_ref, p_ref, rr_ref, u_ref, send_ref):
    cells = part_ref.shape[1]
    clusters = cells // 64
    rank2 = 2 * p_ref.shape[1]

    def tail(u, off, sl, q):
        pw = _weighted_proj(u, c_ref[:, sl], p_ref[0, :, sl], p_ref[1, :, sl])
        return q + _proj_chunk(pw, off, clusters, 64)

    body = _far_common(part_ref, qs_ref, cpl_ref, e_ref, u_ref, tail)
    q = lax.fori_loop(0, cells // CHUNK, body, jnp.zeros((rank2, clusters), F32))
    send_ref[...] = _pack(q, _rr_groups(rr_ref[...], send_ref.shape[1] // rank2))


def _far_grad_kernel(part_ref, qs_ref, cpl_ref, e_ref, bg_ref, u_ref, t_ref):
    cells = part_ref.shape[1]

    def tail(u, off, sl, acc):
        bg = bg_ref[:, sl]
        t_ref[:, sl] = bg[0:1] * u[0:1] + bg[1:2] * u[1:2]
        return acc

    body = _far_common(part_ref, qs_ref, cpl_ref, e_ref, u_ref, tail)
    lax.fori_loop(0, cells // CHUNK, body, 0)


def _call(kernel, outs, args, flops, name):
    leaves = outs if isinstance(outs, tuple) else (outs,)
    nbytes = sum(a.size * a.dtype.itemsize for a in args) + sum(
        o.size * jnp.dtype(o.dtype).itemsize for o in leaves
    )
    return pl.pallas_call(
        kernel,
        out_shape=outs,
        compiler_params=pltpu.CompilerParams(vmem_limit_bytes=VMEM_LIMIT),
        cost_estimate=pl.CostEstimate(flops=flops, bytes_accessed=nbytes, transcendentals=0),
        name=name,
    )(*args)


def _exchange(send, idx, devices, cap):
    total = send.size
    got = lax.all_to_all(send.reshape(devices, total // devices), "cells", 0, 0)
    got = got.reshape(devices * cap, total // (devices * cap))
    return got[idx].T


def _exchange_all(send, devices, clusters, rank2, cap, groups, src_index):
    total = send.size
    got = lax.all_to_all(send.reshape(devices, total // devices), "cells", 0, 0)
    lanes = send.shape[1]
    got = got.reshape(devices, total // (devices * lanes), lanes)
    rr = got[:, -1, :cap]
    table = got[:, :-1, :].reshape(devices, rank2, clusters).transpose(1, 0, 2)
    return table.reshape(rank2, devices * clusters)[:, src_index], rr


def per_device(
    adj_source,
    contrast,
    background,
    near_blocks,
    near_list,
    proj_basis,
    expand_basis,
    coupling,
    far_owner,
    far_slot,
):
    devices = lax.axis_size("cells")
    clusters = near_list.shape[0]
    cells = contrast.shape[1]
    width = cells // clusters
    npairs = far_slot.shape[0]
    cap = 32

    src = adj_source[0]
    cst = contrast
    nb = near_blocks[0]
    pb = proj_basis[0]
    eb = expand_basis[0]
    cp = coupling[0]
    bg = background[0]

    me = lax.axis_index("cells")
    local_list = near_list - me * clusters
    nlc = jnp.repeat(local_list.T, width, axis=1)

    groups = 4
    src_index = far_owner[:, 0] * clusters + far_slot

    nsend = devices * cap
    rank2 = 2 * pb.shape[1]
    q_shape = jax.ShapeDtypeStruct((rank2, clusters), F32)
    field_shape = jax.ShapeDtypeStruct((2, cells), F32)

    first_shape = jax.ShapeDtypeStruct((devices * (clusters // groups + 1), groups * rank2), F32)
    idx, send = _call(
        _proj_pack_kernel,
        (jax.ShapeDtypeStruct((1, npairs), jnp.int32), first_shape),
        (src, cst, pb, far_owner.reshape(1, npairs), far_slot.reshape(1, npairs)),
        4 * rank2 * cells + 2 * devices * npairs * npairs,
        "proj_pack",
    )
    idx = idx.reshape(npairs)
    send_shape = jax.ShapeDtypeStruct((devices * cap // groups, groups * rank2), F32)
    field = src
    for step in range(ITERS):
        if step == 0:
            qs, rr = _exchange_all(send, devices, clusters, rank2, cap, groups, src_index)
        else:
            qs = _exchange(send, idx, devices, cap)
        part = _call(
            _near_kernel, field_shape, (field, cst, nb, nlc, src), 8 * nb.shape[1] * cells, "near"
        )
        if step < ITERS - 1:
            field, send = _call(
                _far_proj_kernel,
                (field_shape, send_shape),
                (part, qs, cp, eb, cst, pb, rr),
                8 * cp.size,
                "far_proj",
            )
        else:
            field, terms = _call(
                _far_grad_kernel,
                (field_shape, jax.ShapeDtypeStruct((1, cells), F32)),
                (part, qs, cp, eb, bg),
                8 * cp.size,
                "far_grad",
            )
    freqs = lax.axis_size("freq")
    mine = terms[0]
    got = [mine] + [
        lax.ppermute(mine, "freq", [(i, (i + k) % freqs) for i in range(freqs)])
        for k in range(1, freqs)
    ]
    stacked = jnp.stack(got)
    f = lax.axis_index("freq")
    total = stacked[(f - 0) % freqs]
    for src in range(1, freqs):
        total = total + stacked[(f - src) % freqs]
    return (field[None], total)


def solution(mesh):
    return jax.shard_map(
        per_device,
        mesh=mesh,
        in_specs=(
            P("freq", None, "cells"),
            P("freq", "cells"),
            P("freq", None, "cells"),
            P("freq", None, None, "cells"),
            P("cells", None),
            P("freq", None, None, "cells"),
            P("freq", None, None, "cells"),
            P("freq", None, None, None, "cells"),
            P("cells", None),
            P("cells"),
        ),
        out_specs=(P("freq", None, "cells"), P("cells")),
        check_vma=False,
    )
```

```python
import jax
import jax.numpy as jnp
from jax import lax
from jax.experimental import pallas as pl
from jax.experimental.pallas import tpu as pltpu
from jax.sharding import PartitionSpec as P

ITERS = 2
F32 = jnp.float32
BF16 = jnp.bfloat16
CHUNK = 1024
PAIR_CHUNK = 256
VMEM_LIMIT = 56 * 1024 * 1024


def _split3(a):
    hi = a.astype(BF16)
    r = a - hi.astype(F32)
    mid = r.astype(BF16)
    lo = (r - mid.astype(F32)).astype(BF16)
    return jnp.concatenate([hi, mid, lo], axis=0)


def _sdot(split, onehot):
    m = split.shape[0] // 3
    r = jnp.dot(split, onehot, preferred_element_type=F32)
    return r[:m] + r[m : 2 * m] + r[2 * m :]


def _xdot(a, onehot):
    return _sdot(_split3(a), onehot)


def _iota(shape, dim):
    return lax.broadcasted_iota(jnp.int32, shape, dim)


def _div(x, d):
    return x >> (d.bit_length() - 1) if d & (d - 1) == 0 else x // d


def _mod(x, d):
    return x & (d - 1) if d & (d - 1) == 0 else x % d


def _weighted_proj(u, c, pre, pim):
    wre = u[0:1] * c
    wim = u[1:2] * c
    return jnp.concatenate([pre * wre - pim * wim, pre * wim + pim * wre], axis=0)


def _proj_chunk(pw, off, clusters, width):
    n = pw.shape[1]
    seg = _div(_iota((n, clusters), 0) + off, width) == _iota((n, clusters), 1)
    return _xdot(pw, seg.astype(BF16))


def _pack(q, rr):
    rank2, clusters = q.shape
    rows, groups = rr.shape
    wide = groups * clusters
    lane = _iota((rows, wide), 1)
    grp = _div(lane, clusters)
    want = rr[:, 0:1]
    for g in range(1, groups):
        want = jnp.where(grp == g, rr[:, g : g + 1], want)
    oh = (_mod(lane, clusters).astype(F32) == want).astype(BF16)
    tile = (_iota((clusters, wide), 0) == _mod(_iota((clusters, wide), 1), clusters)).astype(BF16)
    qw = _xdot(q, tile)
    qw = jnp.concatenate([qw] * groups, axis=0)
    keep = _div(_iota((groups * rank2, wide), 0), rank2) == _div(_iota((groups * rank2, wide), 1), clusters)
    qw = jnp.where(keep, qw, 0.0)
    r = lax.dot_general(oh, _split3(qw), (((1,), (1,)), ((), ())), preferred_element_type=F32)
    n = groups * rank2
    return r[:, :n] + r[:, n : 2 * n] + r[:, 2 * n :]


def _prep(or_ref, sr_ref, idx_ref, devices, cap):
    n = or_ref.shape[1]
    oht = _iota((devices, n), 0) == or_ref[...]
    upper = (_iota((n, n), 0) < _iota((n, n), 1)).astype(BF16)
    counts = jnp.dot(oht.astype(BF16), upper, preferred_element_type=F32)
    pos = jnp.sum(jnp.where(oht, counts, 0.0), axis=0, keepdims=True).astype(jnp.int32)
    idx_ref[...] = or_ref[...] * cap + pos
    pkt = (_iota((cap, n), 0) == pos).astype(BF16)
    ohs = jnp.where(oht, sr_ref[...].astype(F32), 0.0).astype(BF16)
    return lax.dot_general(ohs, pkt, (((1,), (1,)), ((), ())), preferred_element_type=F32)


def _proj_pack_kernel(u_ref, c_ref, p_ref, or_ref, sr_ref, idx_ref, send_ref):
    cells = u_ref.shape[1]
    clusters = cells // 64
    rank2 = 2 * p_ref.shape[1]
    lanes = send_ref.shape[1]
    nrow = rank2 * clusters // lanes
    block = nrow + 1
    devices = send_ref.shape[0] // block
    cap = 32
    req = _prep(or_ref, sr_ref, idx_ref, devices, cap)

    def body(ci, q):
        off = pl.multiple_of(ci * CHUNK, CHUNK)
        sl = pl.ds(off, CHUNK)
        pw = _weighted_proj(u_ref[:, sl], c_ref[:, sl], p_ref[0, :, sl], p_ref[1, :, sl])
        return q + _proj_chunk(pw, off, clusters, 64)

    q = lax.fori_loop(0, cells // CHUNK, body, jnp.zeros((rank2, clusters), F32))
    per = lanes // clusters
    hi = q.astype(BF16)
    r1 = q - hi.astype(F32)
    mid = r1.astype(BF16)
    lo = (r1 - mid.astype(F32)).astype(BF16)
    flat = jnp.zeros((nrow, lanes), F32)
    for h in range(per):
        sel = (_iota((nrow, rank2), 1) == _iota((nrow, rank2), 0) * per + h).astype(BF16)
        part = sum(jnp.dot(sel, x, preferred_element_type=F32) for x in (hi, mid, lo))
        place = (_iota((clusters, lanes), 1) == _iota((clusters, lanes), 0) + h * clusters)
        flat = flat + _xdot(part, place.astype(BF16))
    place = (_iota((cap, lanes), 0) == _iota((cap, lanes), 1)).astype(BF16)
    reqrow = jnp.dot(req.astype(BF16), place, preferred_element_type=F32)
    for e in range(devices):
        send_ref[pl.ds(e * block, nrow), :] = flat
        send_ref[pl.ds(e * block + nrow, 1), :] = reqrow[e : e + 1]


def _rr_groups(rr, groups):
    devices, cap = rr.shape
    per = cap // groups
    rows = devices * per
    rep = (_div(_iota((rows, devices), 0), per) == _iota((rows, devices), 1)).astype(BF16)
    wide = jnp.dot(rep, rr.astype(BF16), preferred_element_type=F32)
    keep = _div(_iota((rows, cap), 1), groups) == _mod(_iota((rows, cap), 0), per)
    fold = (_mod(_iota((cap, groups), 0), groups) == _iota((cap, groups), 1)).astype(BF16)
    return jnp.dot(jnp.where(keep, wide, 0.0).astype(BF16), fold, preferred_element_type=F32)


def _near_kernel(u_ref, c_ref, nb_ref, nlc_ref, base_ref, out_ref):
    cells = u_ref.shape[1]
    width = 64
    clusters = cells // width
    near = nlc_ref.shape[0]

    def wt_body(ci, acc):
        off = pl.multiple_of(ci * CHUNK, CHUNK)
        sl = pl.ds(off, CHUNK)
        w = u_ref[:, sl] * c_ref[:, sl]
        sel = _iota((width, CHUNK), 0) == _mod(_iota((width, CHUNK), 1) + off, width)
        wm = jnp.concatenate(
            [jnp.where(sel, w[0:1], 0.0), jnp.where(sel, w[1:2], 0.0)], axis=0
        )
        seg = _div(_iota((CHUNK, clusters), 0) + off, width) == _iota((CHUNK, clusters), 1)
        return acc + _xdot(wm, seg.astype(BF16))

    wt = lax.fori_loop(0, cells // CHUNK, wt_body, jnp.zeros((2 * width, clusters), F32))
    wt_split = _split3(wt)

    def near_body(ci, carry):
        off = pl.multiple_of(ci * CHUNK, CHUNK)
        sl = pl.ds(off, CHUNK)
        crow = _iota((clusters, CHUNK), 0)
        acc_re = jnp.zeros((1, CHUNK), F32)
        acc_im = jnp.zeros((1, CHUNK), F32)
        for k in range(near):
            m = (crow == nlc_ref[k : k + 1, sl]).astype(BF16)
            wk = _sdot(wt_split, m)
            wre = wk[:width]
            wim = wk[width:]
            nre = nb_ref[0, pl.ds(k * width, width), sl]
            nim = nb_ref[1, pl.ds(k * width, width), sl]
            acc_re = acc_re + jnp.sum(nre * wre - nim * wim, axis=0, keepdims=True)
            acc_im = acc_im + jnp.sum(nre * wim + nim * wre, axis=0, keepdims=True)
        out_ref[:, sl] = base_ref[:, sl] + jnp.concatenate([acc_re, acc_im], axis=0)
        return carry

    lax.fori_loop(0, cells // CHUNK, near_body, 0)


def _far_common(part_ref, qs_ref, cpl_ref, e_ref, u_ref, chunk_tail):
    cells = part_ref.shape[1]
    width = 64
    clusters = cells // width
    rank = cpl_ref.shape[1]
    npairs = qs_ref.shape[1]
    far = npairs // clusters

    def pair_body(pj, z):
        off = pl.multiple_of(pj * PAIR_CHUNK, PAIR_CHUNK)
        sl = pl.ds(off, PAIR_CHUNK)
        qs = qs_ref[:, sl]
        qre = qs[:rank][None]
        qim = qs[rank:][None]
        cre = cpl_ref[0, :, :, sl]
        cim = cpl_ref[1, :, :, sl]
        zre = jnp.sum(cre * qre - cim * qim, axis=1)
        zim = jnp.sum(cre * qim + cim * qre, axis=1)
        seg = _div(_iota((PAIR_CHUNK, clusters), 0) + off, far) == _iota((PAIR_CHUNK, clusters), 1)
        return z + _xdot(jnp.concatenate([zre, zim], axis=0), seg.astype(BF16))

    z = lax.fori_loop(0, npairs // PAIR_CHUNK, pair_body, jnp.zeros((2 * rank, clusters), F32))
    z_split = _split3(z)

    def cell_body(ci, acc):
        off = pl.multiple_of(ci * CHUNK, CHUNK)
        sl = pl.ds(off, CHUNK)
        spread = _iota((clusters, CHUNK), 0) == _div(_iota((clusters, CHUNK), 1) + off, width)
        zz = _sdot(z_split, spread.astype(BF16))
        zre = zz[:rank]
        zim = zz[rank:]
        ere = e_ref[0, :, sl]
        eim = e_ref[1, :, sl]
        far_re = jnp.sum(ere * zre - eim * zim, axis=0, keepdims=True)
        far_im = jnp.sum(ere * zim + eim * zre, axis=0, keepdims=True)
        u = part_ref[:, sl] + jnp.concatenate([far_re, far_im], axis=0)
        u_ref[:, sl] = u
        return chunk_tail(u, off, sl, acc)

    return cell_body


def _far_proj_kernel(part_ref, qs_ref, cpl_ref, e_ref, c_ref, p_ref, rr_ref, u_ref, send_ref):
    cells = part_ref.shape[1]
    clusters = cells // 64
    rank2 = 2 * p_ref.shape[1]

    def tail(u, off, sl, q):
        pw = _weighted_proj(u, c_ref[:, sl], p_ref[0, :, sl], p_ref[1, :, sl])
        return q + _proj_chunk(pw, off, clusters, 64)

    body = _far_common(part_ref, qs_ref, cpl_ref, e_ref, u_ref, tail)
    q = lax.fori_loop(0, cells // CHUNK, body, jnp.zeros((rank2, clusters), F32))
    send_ref[...] = _pack(q, _rr_groups(rr_ref[...], send_ref.shape[1] // rank2))


def _far_grad_kernel(part_ref, qs_ref, cpl_ref, e_ref, bg_ref, u_ref, t_ref):
    cells = part_ref.shape[1]

    def tail(u, off, sl, acc):
        bg = bg_ref[:, sl]
        t_ref[:, sl] = bg[0:1] * u[0:1] + bg[1:2] * u[1:2]
        return acc

    body = _far_common(part_ref, qs_ref, cpl_ref, e_ref, u_ref, tail)
    lax.fori_loop(0, cells // CHUNK, body, 0)


def _call(kernel, outs, args, flops, name):
    leaves = outs if isinstance(outs, tuple) else (outs,)
    nbytes = sum(a.size * a.dtype.itemsize for a in args) + sum(
        o.size * jnp.dtype(o.dtype).itemsize for o in leaves
    )
    return pl.pallas_call(
        kernel,
        out_shape=outs,
        compiler_params=pltpu.CompilerParams(vmem_limit_bytes=VMEM_LIMIT),
        cost_estimate=pl.CostEstimate(flops=flops, bytes_accessed=nbytes, transcendentals=0),
        name=name,
    )(*args)


def _exchange(send, idx, devices, cap):
    total = send.size
    got = lax.all_to_all(send.reshape(devices, total // devices), "cells", 0, 0)
    got = got.reshape(devices * cap, total // (devices * cap))
    return got[idx].T


def _exchange_all(send, devices, clusters, rank2, cap, groups, src_index):
    total = send.size
    got = lax.all_to_all(send.reshape(devices, total // devices), "cells", 0, 0)
    lanes = send.shape[1]
    got = got.reshape(devices, total // (devices * lanes), lanes)
    rr = got[:, -1, :cap]
    table = got[:, :-1, :].reshape(devices, rank2, clusters).transpose(1, 0, 2)
    return table.reshape(rank2, devices * clusters)[:, src_index], rr


def per_device(
    adj_source,
    contrast,
    background,
    near_blocks,
    near_list,
    proj_basis,
    expand_basis,
    coupling,
    far_owner,
    far_slot,
):
    devices = lax.axis_size("cells")
    clusters = near_list.shape[0]
    cells = contrast.shape[1]
    width = cells // clusters
    npairs = far_slot.shape[0]
    cap = 32

    src = adj_source[0]
    cst = contrast
    nb = near_blocks[0]
    pb = proj_basis[0]
    eb = expand_basis[0]
    cp = coupling[0]
    bg = background[0]

    me = lax.axis_index("cells")
    local_list = near_list - me * clusters
    nlc = jnp.repeat(local_list.T, width, axis=1)

    groups = 4
    src_index = far_owner[:, 0] * clusters + far_slot

    nsend = devices * cap
    rank2 = 2 * pb.shape[1]
    q_shape = jax.ShapeDtypeStruct((rank2, clusters), F32)
    field_shape = jax.ShapeDtypeStruct((2, cells), F32)

    first_shape = jax.ShapeDtypeStruct((devices * (clusters // groups + 1), groups * rank2), F32)
    idx, send = _call(
        _proj_pack_kernel,
        (jax.ShapeDtypeStruct((1, npairs), jnp.int32), first_shape),
        (src, cst, pb, far_owner.reshape(1, npairs), far_slot.reshape(1, npairs)),
        4 * rank2 * cells + 2 * devices * npairs * npairs,
        "proj_pack",
    )
    idx = idx.reshape(npairs)
    send_shape = jax.ShapeDtypeStruct((devices * cap // groups, groups * rank2), F32)
    field = src
    for step in range(ITERS):
        if step == 0:
            qs, rr = _exchange_all(send, devices, clusters, rank2, cap, groups, src_index)
        else:
            qs = _exchange(send, idx, devices, cap)
        part = _call(
            _near_kernel, field_shape, (field, cst, nb, nlc, src), 8 * nb.shape[1] * cells, "near"
        )
        if step < ITERS - 1:
            field, send = _call(
                _far_proj_kernel,
                (field_shape, send_shape),
                (part, qs, cp, eb, cst, pb, rr),
                8 * cp.size,
                "far_proj",
            )
        else:
            field, terms = _call(
                _far_grad_kernel,
                (field_shape, jax.ShapeDtypeStruct((1, cells), F32)),
                (part, qs, cp, eb, bg),
                8 * cp.size,
                "far_grad",
            )
    freqs = lax.axis_size("freq")
    mine = terms[0]
    got = [mine] + [
        lax.ppermute(mine, "freq", [(i, (i + k) % freqs) for i in range(freqs)])
        for k in range(1, freqs)
    ]
    stacked = jnp.stack(got)
    f = lax.axis_index("freq")
    total = stacked[(f - 0) % freqs]
    for src in range(1, freqs):
        total = total + stacked[(f - src) % freqs]
    return (field[None], total)


def solution(mesh):
    return jax.shard_map(
        per_device,
        mesh=mesh,
        in_specs=(
            P("freq", None, "cells"),
            P("freq", "cells"),
            P("freq", None, "cells"),
            P("freq", None, None, "cells"),
            P("cells", None),
            P("freq", None, None, "cells"),
            P("freq", None, None, "cells"),
            P("freq", None, None, None, "cells"),
            P("cells", None),
            P("cells"),
        ),
        out_specs=(P("freq", None, "cells"), P("cells")),
        check_vma=False,
    )
```

```python
import jax
import jax.numpy as jnp
from jax import lax
from jax.experimental import pallas as pl
from jax.experimental.pallas import tpu as pltpu
from jax.sharding import PartitionSpec as P

ITERS = 2
F32 = jnp.float32
BF16 = jnp.bfloat16
CHUNK = 2048
PAIR_CHUNK = 512
VMEM_LIMIT = 56 * 1024 * 1024


def _split3(a):
    hi = a.astype(BF16)
    r = a - hi.astype(F32)
    mid = r.astype(BF16)
    lo = (r - mid.astype(F32)).astype(BF16)
    return jnp.concatenate([hi, mid, lo], axis=0)


def _sdot(split, onehot):
    m = split.shape[0] // 3
    r = jnp.dot(split, onehot, preferred_element_type=F32)
    return r[:m] + r[m : 2 * m] + r[2 * m :]


def _xdot(a, onehot):
    return _sdot(_split3(a), onehot)


def _iota(shape, dim):
    return lax.broadcasted_iota(jnp.int32, shape, dim)


def _div(x, d):
    return x >> (d.bit_length() - 1) if d & (d - 1) == 0 else x // d


def _mod(x, d):
    return x & (d - 1) if d & (d - 1) == 0 else x % d


def _weighted_proj(u, c, pre, pim):
    wre = u[0:1] * c
    wim = u[1:2] * c
    return jnp.concatenate([pre * wre - pim * wim, pre * wim + pim * wre], axis=0)


def _proj_chunk(pw, off, clusters, width):
    n = pw.shape[1]
    seg = _div(_iota((n, clusters), 0) + off, width) == _iota((n, clusters), 1)
    return _xdot(pw, seg.astype(BF16))


def _pack(q, rr):
    rank2, clusters = q.shape
    rows, groups = rr.shape
    wide = groups * clusters
    lane = _iota((rows, wide), 1)
    grp = _div(lane, clusters)
    want = rr[:, 0:1]
    for g in range(1, groups):
        want = jnp.where(grp == g, rr[:, g : g + 1], want)
    oh = (_mod(lane, clusters).astype(F32) == want).astype(BF16)
    tile = (_iota((clusters, wide), 0) == _mod(_iota((clusters, wide), 1), clusters)).astype(BF16)
    qw = _xdot(q, tile)
    qw = jnp.concatenate([qw] * groups, axis=0)
    keep = _div(_iota((groups * rank2, wide), 0), rank2) == _div(_iota((groups * rank2, wide), 1), clusters)
    qw = jnp.where(keep, qw, 0.0)
    r = lax.dot_general(oh, _split3(qw), (((1,), (1,)), ((), ())), preferred_element_type=F32)
    n = groups * rank2
    return r[:, :n] + r[:, n : 2 * n] + r[:, 2 * n :]


def _prep(or_ref, sr_ref, idx_ref, devices, cap):
    n = or_ref.shape[1]
    oht = _iota((devices, n), 0) == or_ref[...]
    upper = (_iota((n, n), 0) < _iota((n, n), 1)).astype(BF16)
    counts = jnp.dot(oht.astype(BF16), upper, preferred_element_type=F32)
    pos = jnp.sum(jnp.where(oht, counts, 0.0), axis=0, keepdims=True).astype(jnp.int32)
    idx_ref[...] = or_ref[...] * cap + pos
    pkt = (_iota((cap, n), 0) == pos).astype(BF16)
    ohs = jnp.where(oht, sr_ref[...].astype(F32), 0.0).astype(BF16)
    return lax.dot_general(ohs, pkt, (((1,), (1,)), ((), ())), preferred_element_type=F32)


def _proj_pack_kernel(u_ref, c_ref, p_ref, or_ref, sr_ref, idx_ref, send_ref):
    cells = u_ref.shape[1]
    clusters = cells // 64
    rank2 = 2 * p_ref.shape[1]
    lanes = send_ref.shape[1]
    nrow = rank2 * clusters // lanes
    block = nrow + 1
    devices = send_ref.shape[0] // block
    cap = 32
    req = _prep(or_ref, sr_ref, idx_ref, devices, cap)

    def body(ci, q):
        off = pl.multiple_of(ci * CHUNK, CHUNK)
        sl = pl.ds(off, CHUNK)
        pw = _weighted_proj(u_ref[:, sl], c_ref[:, sl], p_ref[0, :, sl], p_ref[1, :, sl])
        return q + _proj_chunk(pw, off, clusters, 64)

    q = lax.fori_loop(0, cells // CHUNK, body, jnp.zeros((rank2, clusters), F32))
    per = lanes // clusters
    hi = q.astype(BF16)
    r1 = q - hi.astype(F32)
    mid = r1.astype(BF16)
    lo = (r1 - mid.astype(F32)).astype(BF16)
    flat = jnp.zeros((nrow, lanes), F32)
    for h in range(per):
        sel = (_iota((nrow, rank2), 1) == _iota((nrow, rank2), 0) * per + h).astype(BF16)
        part = sum(jnp.dot(sel, x, preferred_element_type=F32) for x in (hi, mid, lo))
        place = (_iota((clusters, lanes), 1) == _iota((clusters, lanes), 0) + h * clusters)
        flat = flat + _xdot(part, place.astype(BF16))
    place = (_iota((cap, lanes), 0) == _iota((cap, lanes), 1)).astype(BF16)
    reqrow = jnp.dot(req.astype(BF16), place, preferred_element_type=F32)
    for e in range(devices):
        send_ref[pl.ds(e * block, nrow), :] = flat
        send_ref[pl.ds(e * block + nrow, 1), :] = reqrow[e : e + 1]


def _rr_groups(rr, groups):
    devices, cap = rr.shape
    per = cap // groups
    rows = devices * per
    rep = (_div(_iota((rows, devices), 0), per) == _iota((rows, devices), 1)).astype(BF16)
    wide = jnp.dot(rep, rr.astype(BF16), preferred_element_type=F32)
    keep = _div(_iota((rows, cap), 1), groups) == _mod(_iota((rows, cap), 0), per)
    fold = (_mod(_iota((cap, groups), 0), groups) == _iota((cap, groups), 1)).astype(BF16)
    return jnp.dot(jnp.where(keep, wide, 0.0).astype(BF16), fold, preferred_element_type=F32)


def _near_kernel(u_ref, c_ref, nb_ref, nlc_ref, base_ref, out_ref):
    cells = u_ref.shape[1]
    width = 64
    clusters = cells // width
    near = nlc_ref.shape[0]

    def wt_body(ci, acc):
        off = pl.multiple_of(ci * CHUNK, CHUNK)
        sl = pl.ds(off, CHUNK)
        w = u_ref[:, sl] * c_ref[:, sl]
        sel = _iota((width, CHUNK), 0) == _mod(_iota((width, CHUNK), 1) + off, width)
        wm = jnp.concatenate(
            [jnp.where(sel, w[0:1], 0.0), jnp.where(sel, w[1:2], 0.0)], axis=0
        )
        seg = _div(_iota((CHUNK, clusters), 0) + off, width) == _iota((CHUNK, clusters), 1)
        return acc + _xdot(wm, seg.astype(BF16))

    wt = lax.fori_loop(0, cells // CHUNK, wt_body, jnp.zeros((2 * width, clusters), F32))
    wt_split = _split3(wt)

    def near_body(ci, carry):
        off = pl.multiple_of(ci * CHUNK, CHUNK)
        sl = pl.ds(off, CHUNK)
        crow = _iota((clusters, CHUNK), 0)
        acc_re = jnp.zeros((1, CHUNK), F32)
        acc_im = jnp.zeros((1, CHUNK), F32)
        for k in range(near):
            m = (crow == nlc_ref[k : k + 1, sl]).astype(BF16)
            wk = _sdot(wt_split, m)
            wre = wk[:width]
            wim = wk[width:]
            nre = nb_ref[0, pl.ds(k * width, width), sl]
            nim = nb_ref[1, pl.ds(k * width, width), sl]
            acc_re = acc_re + jnp.sum(nre * wre - nim * wim, axis=0, keepdims=True)
            acc_im = acc_im + jnp.sum(nre * wim + nim * wre, axis=0, keepdims=True)
        out_ref[:, sl] = base_ref[:, sl] + jnp.concatenate([acc_re, acc_im], axis=0)
        return carry

    lax.fori_loop(0, cells // CHUNK, near_body, 0)


def _far_common(part_ref, qs_ref, cpl_ref, e_ref, u_ref, chunk_tail):
    cells = part_ref.shape[1]
    width = 64
    clusters = cells // width
    rank = cpl_ref.shape[1]
    npairs = qs_ref.shape[1]
    far = npairs // clusters

    def pair_body(pj, z):
        off = pl.multiple_of(pj * PAIR_CHUNK, PAIR_CHUNK)
        sl = pl.ds(off, PAIR_CHUNK)
        qs = qs_ref[:, sl]
        qre = qs[:rank][None]
        qim = qs[rank:][None]
        cre = cpl_ref[0, :, :, sl]
        cim = cpl_ref[1, :, :, sl]
        zre = jnp.sum(cre * qre - cim * qim, axis=1)
        zim = jnp.sum(cre * qim + cim * qre, axis=1)
        seg = _div(_iota((PAIR_CHUNK, clusters), 0) + off, far) == _iota((PAIR_CHUNK, clusters), 1)
        return z + _xdot(jnp.concatenate([zre, zim], axis=0), seg.astype(BF16))

    z = lax.fori_loop(0, npairs // PAIR_CHUNK, pair_body, jnp.zeros((2 * rank, clusters), F32))
    z_split = _split3(z)

    def cell_body(ci, acc):
        off = pl.multiple_of(ci * CHUNK, CHUNK)
        sl = pl.ds(off, CHUNK)
        spread = _iota((clusters, CHUNK), 0) == _div(_iota((clusters, CHUNK), 1) + off, width)
        zz = _sdot(z_split, spread.astype(BF16))
        zre = zz[:rank]
        zim = zz[rank:]
        ere = e_ref[0, :, sl]
        eim = e_ref[1, :, sl]
        far_re = jnp.sum(ere * zre - eim * zim, axis=0, keepdims=True)
        far_im = jnp.sum(ere * zim + eim * zre, axis=0, keepdims=True)
        u = part_ref[:, sl] + jnp.concatenate([far_re, far_im], axis=0)
        u_ref[:, sl] = u
        return chunk_tail(u, off, sl, acc)

    return cell_body


def _far_proj_kernel(part_ref, qs_ref, cpl_ref, e_ref, c_ref, p_ref, rr_ref, u_ref, send_ref):
    cells = part_ref.shape[1]
    clusters = cells // 64
    rank2 = 2 * p_ref.shape[1]

    def tail(u, off, sl, q):
        pw = _weighted_proj(u, c_ref[:, sl], p_ref[0, :, sl], p_ref[1, :, sl])
        return q + _proj_chunk(pw, off, clusters, 64)

    body = _far_common(part_ref, qs_ref, cpl_ref, e_ref, u_ref, tail)
    q = lax.fori_loop(0, cells // CHUNK, body, jnp.zeros((rank2, clusters), F32))
    send_ref[...] = _pack(q, _rr_groups(rr_ref[...], send_ref.shape[1] // rank2))


def _far_grad_kernel(part_ref, qs_ref, cpl_ref, e_ref, bg_ref, u_ref, t_ref):
    cells = part_ref.shape[1]

    def tail(u, off, sl, acc):
        bg = bg_ref[:, sl]
        t_ref[:, sl] = bg[0:1] * u[0:1] + bg[1:2] * u[1:2]
        return acc

    body = _far_common(part_ref, qs_ref, cpl_ref, e_ref, u_ref, tail)
    lax.fori_loop(0, cells // CHUNK, body, 0)


def _call(kernel, outs, args, flops, name):
    leaves = outs if isinstance(outs, tuple) else (outs,)
    nbytes = sum(a.size * a.dtype.itemsize for a in args) + sum(
        o.size * jnp.dtype(o.dtype).itemsize for o in leaves
    )
    return pl.pallas_call(
        kernel,
        out_shape=outs,
        compiler_params=pltpu.CompilerParams(vmem_limit_bytes=VMEM_LIMIT),
        cost_estimate=pl.CostEstimate(flops=flops, bytes_accessed=nbytes, transcendentals=0),
        name=name,
    )(*args)


def _exchange(send, idx, devices, cap):
    total = send.size
    got = lax.all_to_all(send.reshape(devices, total // devices), "cells", 0, 0)
    got = got.reshape(devices * cap, total // (devices * cap))
    return got[idx].T


def _exchange_all(send, devices, clusters, rank2, cap, groups, src_index):
    total = send.size
    got = lax.all_to_all(send.reshape(devices, total // devices), "cells", 0, 0)
    lanes = send.shape[1]
    got = got.reshape(devices, total // (devices * lanes), lanes)
    rr = got[:, -1, :cap]
    table = got[:, :-1, :].reshape(devices, rank2, clusters).transpose(1, 0, 2)
    return table.reshape(rank2, devices * clusters)[:, src_index], rr


def per_device(
    adj_source,
    contrast,
    background,
    near_blocks,
    near_list,
    proj_basis,
    expand_basis,
    coupling,
    far_owner,
    far_slot,
):
    devices = lax.axis_size("cells")
    clusters = near_list.shape[0]
    cells = contrast.shape[1]
    width = cells // clusters
    npairs = far_slot.shape[0]
    cap = 32

    src = adj_source[0]
    cst = contrast
    nb = near_blocks[0]
    pb = proj_basis[0]
    eb = expand_basis[0]
    cp = coupling[0]
    bg = background[0]

    me = lax.axis_index("cells")
    local_list = near_list - me * clusters
    nlc = jnp.repeat(local_list.T, width, axis=1)

    groups = 4
    src_index = far_owner[:, 0] * clusters + far_slot

    nsend = devices * cap
    rank2 = 2 * pb.shape[1]
    q_shape = jax.ShapeDtypeStruct((rank2, clusters), F32)
    field_shape = jax.ShapeDtypeStruct((2, cells), F32)

    first_shape = jax.ShapeDtypeStruct((devices * (clusters // groups + 1), groups * rank2), F32)
    idx, send = _call(
        _proj_pack_kernel,
        (jax.ShapeDtypeStruct((1, npairs), jnp.int32), first_shape),
        (src, cst, pb, far_owner.reshape(1, npairs), far_slot.reshape(1, npairs)),
        4 * rank2 * cells + 2 * devices * npairs * npairs,
        "proj_pack",
    )
    idx = idx.reshape(npairs)
    send_shape = jax.ShapeDtypeStruct((devices * cap // groups, groups * rank2), F32)
    field = src
    for step in range(ITERS):
        if step == 0:
            qs, rr = _exchange_all(send, devices, clusters, rank2, cap, groups, src_index)
        else:
            qs = _exchange(send, idx, devices, cap)
        part = _call(
            _near_kernel, field_shape, (field, cst, nb, nlc, src), 8 * nb.shape[1] * cells, "near"
        )
        if step < ITERS - 1:
            field, send = _call(
                _far_proj_kernel,
                (field_shape, send_shape),
                (part, qs, cp, eb, cst, pb, rr),
                8 * cp.size,
                "far_proj",
            )
        else:
            field, terms = _call(
                _far_grad_kernel,
                (field_shape, jax.ShapeDtypeStruct((1, cells), F32)),
                (part, qs, cp, eb, bg),
                8 * cp.size,
                "far_grad",
            )
    freqs = lax.axis_size("freq")
    mine = terms[0]
    got = [mine] + [
        lax.ppermute(mine, "freq", [(i, (i + k) % freqs) for i in range(freqs)])
        for k in range(1, freqs)
    ]
    stacked = jnp.stack(got)
    f = lax.axis_index("freq")
    total = stacked[(f - 0) % freqs]
    for src in range(1, freqs):
        total = total + stacked[(f - src) % freqs]
    return (field[None], total)


def solution(mesh):
    return jax.shard_map(
        per_device,
        mesh=mesh,
        in_specs=(
            P("freq", None, "cells"),
            P("freq", "cells"),
            P("freq", None, "cells"),
            P("freq", None, None, "cells"),
            P("cells", None),
            P("freq", None, None, "cells"),
            P("freq", None, None, "cells"),
            P("freq", None, None, None, "cells"),
            P("cells", None),
            P("cells"),
        ),
        out_specs=(P("freq", None, "cells"), P("cells")),
        check_vma=False,
    )
```

```python
import jax
import jax.numpy as jnp
from jax import lax
from jax.experimental import pallas as pl
from jax.experimental.pallas import tpu as pltpu
from jax.sharding import PartitionSpec as P

ITERS = 2
F32 = jnp.float32
BF16 = jnp.bfloat16
CHUNK = 4096
PAIR_CHUNK = 1024
VMEM_LIMIT = 56 * 1024 * 1024


def _split3(a):
    hi = a.astype(BF16)
    r = a - hi.astype(F32)
    mid = r.astype(BF16)
    lo = (r - mid.astype(F32)).astype(BF16)
    return jnp.concatenate([hi, mid, lo], axis=0)


def _sdot(split, onehot):
    m = split.shape[0] // 3
    r = jnp.dot(split, onehot, preferred_element_type=F32)
    return r[:m] + r[m : 2 * m] + r[2 * m :]


def _xdot(a, onehot):
    return _sdot(_split3(a), onehot)


def _iota(shape, dim):
    return lax.broadcasted_iota(jnp.int32, shape, dim)


def _div(x, d):
    return x >> (d.bit_length() - 1) if d & (d - 1) == 0 else x // d


def _mod(x, d):
    return x & (d - 1) if d & (d - 1) == 0 else x % d


def _weighted_proj(u, c, pre, pim):
    wre = u[0:1] * c
    wim = u[1:2] * c
    return jnp.concatenate([pre * wre - pim * wim, pre * wim + pim * wre], axis=0)


def _proj_chunk(pw, off, clusters, width):
    n = pw.shape[1]
    seg = _div(_iota((n, clusters), 0) + off, width) == _iota((n, clusters), 1)
    return _xdot(pw, seg.astype(BF16))


def _pack(q, rr):
    rank2, clusters = q.shape
    rows, groups = rr.shape
    wide = groups * clusters
    lane = _iota((rows, wide), 1)
    grp = _div(lane, clusters)
    want = rr[:, 0:1]
    for g in range(1, groups):
        want = jnp.where(grp == g, rr[:, g : g + 1], want)
    oh = (_mod(lane, clusters).astype(F32) == want).astype(BF16)
    tile = (_iota((clusters, wide), 0) == _mod(_iota((clusters, wide), 1), clusters)).astype(BF16)
    qw = _xdot(q, tile)
    qw = jnp.concatenate([qw] * groups, axis=0)
    keep = _div(_iota((groups * rank2, wide), 0), rank2) == _div(_iota((groups * rank2, wide), 1), clusters)
    qw = jnp.where(keep, qw, 0.0)
    r = lax.dot_general(oh, _split3(qw), (((1,), (1,)), ((), ())), preferred_element_type=F32)
    n = groups * rank2
    return r[:, :n] + r[:, n : 2 * n] + r[:, 2 * n :]


def _prep(or_ref, sr_ref, idx_ref, devices, cap):
    n = or_ref.shape[1]
    oht = _iota((devices, n), 0) == or_ref[...]
    upper = (_iota((n, n), 0) < _iota((n, n), 1)).astype(BF16)
    counts = jnp.dot(oht.astype(BF16), upper, preferred_element_type=F32)
    pos = jnp.sum(jnp.where(oht, counts, 0.0), axis=0, keepdims=True).astype(jnp.int32)
    idx_ref[...] = or_ref[...] * cap + pos
    pkt = (_iota((cap, n), 0) == pos).astype(BF16)
    ohs = jnp.where(oht, sr_ref[...].astype(F32), 0.0).astype(BF16)
    return lax.dot_general(ohs, pkt, (((1,), (1,)), ((), ())), preferred_element_type=F32)


def _proj_pack_kernel(u_ref, c_ref, p_ref, or_ref, sr_ref, idx_ref, send_ref):
    cells = u_ref.shape[1]
    clusters = cells // 64
    rank2 = 2 * p_ref.shape[1]
    lanes = send_ref.shape[1]
    nrow = rank2 * clusters // lanes
    block = nrow + 1
    devices = send_ref.shape[0] // block
    cap = 32
    req = _prep(or_ref, sr_ref, idx_ref, devices, cap)

    def body(ci, q):
        off = pl.multiple_of(ci * CHUNK, CHUNK)
        sl = pl.ds(off, CHUNK)
        pw = _weighted_proj(u_ref[:, sl], c_ref[:, sl], p_ref[0, :, sl], p_ref[1, :, sl])
        return q + _proj_chunk(pw, off, clusters, 64)

    q = lax.fori_loop(0, cells // CHUNK, body, jnp.zeros((rank2, clusters), F32))
    per = lanes // clusters
    hi = q.astype(BF16)
    r1 = q - hi.astype(F32)
    mid = r1.astype(BF16)
    lo = (r1 - mid.astype(F32)).astype(BF16)
    flat = jnp.zeros((nrow, lanes), F32)
    for h in range(per):
        sel = (_iota((nrow, rank2), 1) == _iota((nrow, rank2), 0) * per + h).astype(BF16)
        part = sum(jnp.dot(sel, x, preferred_element_type=F32) for x in (hi, mid, lo))
        place = (_iota((clusters, lanes), 1) == _iota((clusters, lanes), 0) + h * clusters)
        flat = flat + _xdot(part, place.astype(BF16))
    place = (_iota((cap, lanes), 0) == _iota((cap, lanes), 1)).astype(BF16)
    reqrow = jnp.dot(req.astype(BF16), place, preferred_element_type=F32)
    for e in range(devices):
        send_ref[pl.ds(e * block, nrow), :] = flat
        send_ref[pl.ds(e * block + nrow, 1), :] = reqrow[e : e + 1]


def _rr_groups(rr, groups):
    devices, cap = rr.shape
    per = cap // groups
    rows = devices * per
    rep = (_div(_iota((rows, devices), 0), per) == _iota((rows, devices), 1)).astype(BF16)
    wide = jnp.dot(rep, rr.astype(BF16), preferred_element_type=F32)
    keep = _div(_iota((rows, cap), 1), groups) == _mod(_iota((rows, cap), 0), per)
    fold = (_mod(_iota((cap, groups), 0), groups) == _iota((cap, groups), 1)).astype(BF16)
    return jnp.dot(jnp.where(keep, wide, 0.0).astype(BF16), fold, preferred_element_type=F32)


def _near_kernel(u_ref, c_ref, nb_ref, nlc_ref, base_ref, out_ref):
    cells = u_ref.shape[1]
    width = 64
    clusters = cells // width
    near = nlc_ref.shape[0]

    def wt_body(ci, acc):
        off = pl.multiple_of(ci * CHUNK, CHUNK)
        sl = pl.ds(off, CHUNK)
        w = u_ref[:, sl] * c_ref[:, sl]
        sel = _iota((width, CHUNK), 0) == _mod(_iota((width, CHUNK), 1) + off, width)
        wm = jnp.concatenate(
            [jnp.where(sel, w[0:1], 0.0), jnp.where(sel, w[1:2], 0.0)], axis=0
        )
        seg = _div(_iota((CHUNK, clusters), 0) + off, width) == _iota((CHUNK, clusters), 1)
        return acc + _xdot(wm, seg.astype(BF16))

    wt = lax.fori_loop(0, cells // CHUNK, wt_body, jnp.zeros((2 * width, clusters), F32))
    wt_split = _split3(wt)

    def near_body(ci, carry):
        off = pl.multiple_of(ci * CHUNK, CHUNK)
        sl = pl.ds(off, CHUNK)
        crow = _iota((clusters, CHUNK), 0)
        acc_re = jnp.zeros((1, CHUNK), F32)
        acc_im = jnp.zeros((1, CHUNK), F32)
        for k in range(near):
            m = (crow == nlc_ref[k : k + 1, sl]).astype(BF16)
            wk = _sdot(wt_split, m)
            wre = wk[:width]
            wim = wk[width:]
            nre = nb_ref[0, pl.ds(k * width, width), sl]
            nim = nb_ref[1, pl.ds(k * width, width), sl]
            acc_re = acc_re + jnp.sum(nre * wre - nim * wim, axis=0, keepdims=True)
            acc_im = acc_im + jnp.sum(nre * wim + nim * wre, axis=0, keepdims=True)
        out_ref[:, sl] = base_ref[:, sl] + jnp.concatenate([acc_re, acc_im], axis=0)
        return carry

    lax.fori_loop(0, cells // CHUNK, near_body, 0)


def _far_common(part_ref, qs_ref, cpl_ref, e_ref, u_ref, chunk_tail):
    cells = part_ref.shape[1]
    width = 64
    clusters = cells // width
    rank = cpl_ref.shape[1]
    npairs = qs_ref.shape[1]
    far = npairs // clusters

    def pair_body(pj, z):
        off = pl.multiple_of(pj * PAIR_CHUNK, PAIR_CHUNK)
        sl = pl.ds(off, PAIR_CHUNK)
        qs = qs_ref[:, sl]
        qre = qs[:rank][None]
        qim = qs[rank:][None]
        cre = cpl_ref[0, :, :, sl]
        cim = cpl_ref[1, :, :, sl]
        zre = jnp.sum(cre * qre - cim * qim, axis=1)
        zim = jnp.sum(cre * qim + cim * qre, axis=1)
        seg = _div(_iota((PAIR_CHUNK, clusters), 0) + off, far) == _iota((PAIR_CHUNK, clusters), 1)
        return z + _xdot(jnp.concatenate([zre, zim], axis=0), seg.astype(BF16))

    z = lax.fori_loop(0, npairs // PAIR_CHUNK, pair_body, jnp.zeros((2 * rank, clusters), F32))
    z_split = _split3(z)

    def cell_body(ci, acc):
        off = pl.multiple_of(ci * CHUNK, CHUNK)
        sl = pl.ds(off, CHUNK)
        spread = _iota((clusters, CHUNK), 0) == _div(_iota((clusters, CHUNK), 1) + off, width)
        zz = _sdot(z_split, spread.astype(BF16))
        zre = zz[:rank]
        zim = zz[rank:]
        ere = e_ref[0, :, sl]
        eim = e_ref[1, :, sl]
        far_re = jnp.sum(ere * zre - eim * zim, axis=0, keepdims=True)
        far_im = jnp.sum(ere * zim + eim * zre, axis=0, keepdims=True)
        u = part_ref[:, sl] + jnp.concatenate([far_re, far_im], axis=0)
        u_ref[:, sl] = u
        return chunk_tail(u, off, sl, acc)

    return cell_body


def _far_proj_kernel(part_ref, qs_ref, cpl_ref, e_ref, c_ref, p_ref, rr_ref, u_ref, send_ref):
    cells = part_ref.shape[1]
    clusters = cells // 64
    rank2 = 2 * p_ref.shape[1]

    def tail(u, off, sl, q):
        pw = _weighted_proj(u, c_ref[:, sl], p_ref[0, :, sl], p_ref[1, :, sl])
        return q + _proj_chunk(pw, off, clusters, 64)

    body = _far_common(part_ref, qs_ref, cpl_ref, e_ref, u_ref, tail)
    q = lax.fori_loop(0, cells // CHUNK, body, jnp.zeros((rank2, clusters), F32))
    send_ref[...] = _pack(q, _rr_groups(rr_ref[...], send_ref.shape[1] // rank2))


def _far_grad_kernel(part_ref, qs_ref, cpl_ref, e_ref, bg_ref, u_ref, t_ref):
    cells = part_ref.shape[1]

    def tail(u, off, sl, acc):
        bg = bg_ref[:, sl]
        t_ref[:, sl] = bg[0:1] * u[0:1] + bg[1:2] * u[1:2]
        return acc

    body = _far_common(part_ref, qs_ref, cpl_ref, e_ref, u_ref, tail)
    lax.fori_loop(0, cells // CHUNK, body, 0)


def _call(kernel, outs, args, flops, name):
    leaves = outs if isinstance(outs, tuple) else (outs,)
    nbytes = sum(a.size * a.dtype.itemsize for a in args) + sum(
        o.size * jnp.dtype(o.dtype).itemsize for o in leaves
    )
    return pl.pallas_call(
        kernel,
        out_shape=outs,
        compiler_params=pltpu.CompilerParams(vmem_limit_bytes=VMEM_LIMIT),
        cost_estimate=pl.CostEstimate(flops=flops, bytes_accessed=nbytes, transcendentals=0),
        name=name,
    )(*args)


def _exchange(send, idx, devices, cap):
    total = send.size
    got = lax.all_to_all(send.reshape(devices, total // devices), "cells", 0, 0)
    got = got.reshape(devices * cap, total // (devices * cap))
    return got[idx].T


def _exchange_all(send, devices, clusters, rank2, cap, groups, src_index):
    total = send.size
    got = lax.all_to_all(send.reshape(devices, total // devices), "cells", 0, 0)
    lanes = send.shape[1]
    got = got.reshape(devices, total // (devices * lanes), lanes)
    rr = got[:, -1, :cap]
    table = got[:, :-1, :].reshape(devices, rank2, clusters).transpose(1, 0, 2)
    return table.reshape(rank2, devices * clusters)[:, src_index], rr


def per_device(
    adj_source,
    contrast,
    background,
    near_blocks,
    near_list,
    proj_basis,
    expand_basis,
    coupling,
    far_owner,
    far_slot,
):
    devices = lax.axis_size("cells")
    clusters = near_list.shape[0]
    cells = contrast.shape[1]
    width = cells // clusters
    npairs = far_slot.shape[0]
    cap = 32

    src = adj_source[0]
    cst = contrast
    nb = near_blocks[0]
    pb = proj_basis[0]
    eb = expand_basis[0]
    cp = coupling[0]
    bg = background[0]

    me = lax.axis_index("cells")
    local_list = near_list - me * clusters
    nlc = jnp.repeat(local_list.T, width, axis=1)

    groups = 4
    src_index = far_owner[:, 0] * clusters + far_slot

    nsend = devices * cap
    rank2 = 2 * pb.shape[1]
    q_shape = jax.ShapeDtypeStruct((rank2, clusters), F32)
    field_shape = jax.ShapeDtypeStruct((2, cells), F32)

    first_shape = jax.ShapeDtypeStruct((devices * (clusters // groups + 1), groups * rank2), F32)
    idx, send = _call(
        _proj_pack_kernel,
        (jax.ShapeDtypeStruct((1, npairs), jnp.int32), first_shape),
        (src, cst, pb, far_owner.reshape(1, npairs), far_slot.reshape(1, npairs)),
        4 * rank2 * cells + 2 * devices * npairs * npairs,
        "proj_pack",
    )
    idx = idx.reshape(npairs)
    send_shape = jax.ShapeDtypeStruct((devices * cap // groups, groups * rank2), F32)
    field = src
    for step in range(ITERS):
        if step == 0:
            qs, rr = _exchange_all(send, devices, clusters, rank2, cap, groups, src_index)
        else:
            qs = _exchange(send, idx, devices, cap)
        part = _call(
            _near_kernel, field_shape, (field, cst, nb, nlc, src), 8 * nb.shape[1] * cells, "near"
        )
        if step < ITERS - 1:
            field, send = _call(
                _far_proj_kernel,
                (field_shape, send_shape),
                (part, qs, cp, eb, cst, pb, rr),
                8 * cp.size,
                "far_proj",
            )
        else:
            field, terms = _call(
                _far_grad_kernel,
                (field_shape, jax.ShapeDtypeStruct((1, cells), F32)),
                (part, qs, cp, eb, bg),
                8 * cp.size,
                "far_grad",
            )
    freqs = lax.axis_size("freq")
    mine = terms[0]
    got = [mine] + [
        lax.ppermute(mine, "freq", [(i, (i + k) % freqs) for i in range(freqs)])
        for k in range(1, freqs)
    ]
    stacked = jnp.stack(got)
    f = lax.axis_index("freq")
    total = stacked[(f - 0) % freqs]
    for src in range(1, freqs):
        total = total + stacked[(f - src) % freqs]
    return (field[None], total)


def solution(mesh):
    return jax.shard_map(
        per_device,
        mesh=mesh,
        in_specs=(
            P("freq", None, "cells"),
            P("freq", "cells"),
            P("freq", None, "cells"),
            P("freq", None, None, "cells"),
            P("cells", None),
            P("freq", None, None, "cells"),
            P("freq", None, None, "cells"),
            P("freq", None, None, None, "cells"),
            P("cells", None),
            P("cells"),
        ),
        out_specs=(P("freq", None, "cells"), P("cells")),
        check_vma=False,
    )
```

```python
import jax
import jax.numpy as jnp
from jax import lax
from jax.experimental import pallas as pl
from jax.experimental.pallas import tpu as pltpu
from jax.sharding import PartitionSpec as P

ITERS = 2
F32 = jnp.float32
BF16 = jnp.bfloat16
CHUNK = 4096
PAIR_CHUNK = 1024
VMEM_LIMIT = 56 * 1024 * 1024


def _split3(a):
    hi = a.astype(BF16)
    r = a - hi.astype(F32)
    mid = r.astype(BF16)
    lo = (r - mid.astype(F32)).astype(BF16)
    return jnp.concatenate([hi, mid, lo], axis=0)


def _sdot(split, onehot):
    m = split.shape[0] // 3
    r = jnp.dot(split, onehot, preferred_element_type=F32)
    return r[:m] + r[m : 2 * m] + r[2 * m :]


def _xdot(a, onehot):
    return _sdot(_split3(a), onehot)


def _iota(shape, dim):
    return lax.broadcasted_iota(jnp.int32, shape, dim)


def _div(x, d):
    return x >> (d.bit_length() - 1) if d & (d - 1) == 0 else x // d


def _mod(x, d):
    return x & (d - 1) if d & (d - 1) == 0 else x % d


def _weighted_proj(u, c, pre, pim):
    wre = u[0:1] * c
    wim = u[1:2] * c
    return jnp.concatenate([pre * wre - pim * wim, pre * wim + pim * wre], axis=0)


def _proj_chunk(pw, off, clusters, width):
    n = pw.shape[1]
    seg = _div(_iota((n, clusters), 0) + off, width) == _iota((n, clusters), 1)
    return _xdot(pw, seg.astype(BF16))


def _pack(q, rr):
    rank2, clusters = q.shape
    rows, groups = rr.shape
    wide = groups * clusters
    lane = _iota((rows, wide), 1)
    grp = _div(lane, clusters)
    want = rr[:, 0:1]
    for g in range(1, groups):
        want = jnp.where(grp == g, rr[:, g : g + 1], want)
    oh = (_mod(lane, clusters).astype(F32) == want).astype(BF16)
    tile = (_iota((clusters, wide), 0) == _mod(_iota((clusters, wide), 1), clusters)).astype(BF16)
    qw = _xdot(q, tile)
    qw = jnp.concatenate([qw] * groups, axis=0)
    keep = _div(_iota((groups * rank2, wide), 0), rank2) == _div(_iota((groups * rank2, wide), 1), clusters)
    qw = jnp.where(keep, qw, 0.0)
    r = lax.dot_general(oh, _split3(qw), (((1,), (1,)), ((), ())), preferred_element_type=F32)
    n = groups * rank2
    return r[:, :n] + r[:, n : 2 * n] + r[:, 2 * n :]


def _prep(or_ref, sr_ref, idx_ref, devices, cap):
    n = or_ref.shape[1]
    oht = _iota((devices, n), 0) == or_ref[...]
    upper = (_iota((n, n), 0) < _iota((n, n), 1)).astype(BF16)
    counts = jnp.dot(oht.astype(BF16), upper, preferred_element_type=F32)
    pos = jnp.sum(jnp.where(oht, counts, 0.0), axis=0, keepdims=True).astype(jnp.int32)
    idx_ref[...] = or_ref[...] * cap + pos
    pkt = (_iota((cap, n), 0) == pos).astype(BF16)
    ohs = jnp.where(oht, sr_ref[...].astype(F32), 0.0).astype(BF16)
    return lax.dot_general(ohs, pkt, (((1,), (1,)), ((), ())), preferred_element_type=F32)


def _proj_pack_kernel(u_ref, c_ref, p_ref, or_ref, sr_ref, idx_ref, send_ref):
    cells = u_ref.shape[1]
    clusters = cells // 64
    rank2 = 2 * p_ref.shape[1]
    lanes = send_ref.shape[1]
    nrow = rank2 * clusters // lanes
    block = nrow + 1
    devices = send_ref.shape[0] // block
    cap = 32
    req = _prep(or_ref, sr_ref, idx_ref, devices, cap)

    def body(ci, q):
        off = pl.multiple_of(ci * CHUNK, CHUNK)
        sl = pl.ds(off, CHUNK)
        pw = _weighted_proj(u_ref[:, sl], c_ref[:, sl], p_ref[0, :, sl], p_ref[1, :, sl])
        return q + _proj_chunk(pw, off, clusters, 64)

    q = lax.fori_loop(0, cells // CHUNK, body, jnp.zeros((rank2, clusters), F32))
    per = lanes // clusters
    hi = q.astype(BF16)
    r1 = q - hi.astype(F32)
    mid = r1.astype(BF16)
    lo = (r1 - mid.astype(F32)).astype(BF16)
    flat = jnp.zeros((nrow, lanes), F32)
    for h in range(per):
        sel = (_iota((nrow, rank2), 1) == _iota((nrow, rank2), 0) * per + h).astype(BF16)
        part = sum(jnp.dot(sel, x, preferred_element_type=F32) for x in (hi, mid, lo))
        place = (_iota((clusters, lanes), 1) == _iota((clusters, lanes), 0) + h * clusters)
        flat = flat + _xdot(part, place.astype(BF16))
    place = (_iota((cap, lanes), 0) == _iota((cap, lanes), 1)).astype(BF16)
    reqrow = jnp.dot(req.astype(BF16), place, preferred_element_type=F32)
    for e in range(devices):
        send_ref[pl.ds(e * block, nrow), :] = flat
        send_ref[pl.ds(e * block + nrow, 1), :] = reqrow[e : e + 1]


def _rr_groups(rr, groups):
    devices, cap = rr.shape
    per = cap // groups
    rows = devices * per
    rep = (_div(_iota((rows, devices), 0), per) == _iota((rows, devices), 1)).astype(BF16)
    wide = jnp.dot(rep, rr.astype(BF16), preferred_element_type=F32)
    keep = _div(_iota((rows, cap), 1), groups) == _mod(_iota((rows, cap), 0), per)
    fold = (_mod(_iota((cap, groups), 0), groups) == _iota((cap, groups), 1)).astype(BF16)
    return jnp.dot(jnp.where(keep, wide, 0.0).astype(BF16), fold, preferred_element_type=F32)


def _near_kernel(u_ref, c_ref, nb_ref, nlc_ref, base_ref, out_ref):
    cells = u_ref.shape[1]
    width = 64
    clusters = cells // width
    near = nlc_ref.shape[0]

    def wt_body(ci, acc):
        off = pl.multiple_of(ci * CHUNK, CHUNK)
        sl = pl.ds(off, CHUNK)
        w = u_ref[:, sl] * c_ref[:, sl]
        sel = _iota((width, CHUNK), 0) == _mod(_iota((width, CHUNK), 1) + off, width)
        wm = jnp.concatenate(
            [jnp.where(sel, w[0:1], 0.0), jnp.where(sel, w[1:2], 0.0)], axis=0
        )
        seg = _div(_iota((CHUNK, clusters), 0) + off, width) == _iota((CHUNK, clusters), 1)
        return acc + _xdot(wm, seg.astype(BF16))

    wt = lax.fori_loop(0, cells // CHUNK, wt_body, jnp.zeros((2 * width, clusters), F32))
    wt_split = _split3(wt)

    def near_body(ci, carry):
        off = pl.multiple_of(ci * CHUNK, CHUNK)
        sl = pl.ds(off, CHUNK)
        crow = _iota((clusters, CHUNK), 0)
        acc_re = jnp.zeros((1, CHUNK), F32)
        acc_im = jnp.zeros((1, CHUNK), F32)
        for k in range(near):
            m = (crow == nlc_ref[k : k + 1, sl]).astype(BF16)
            wk = _sdot(wt_split, m)
            wre = wk[:width]
            wim = wk[width:]
            nre = nb_ref[0, pl.ds(k * width, width), sl]
            nim = nb_ref[1, pl.ds(k * width, width), sl]
            acc_re = acc_re + jnp.sum(nre * wre - nim * wim, axis=0, keepdims=True)
            acc_im = acc_im + jnp.sum(nre * wim + nim * wre, axis=0, keepdims=True)
        out_ref[:, sl] = base_ref[:, sl] + jnp.concatenate([acc_re, acc_im], axis=0)
        return carry

    lax.fori_loop(0, cells // CHUNK, near_body, 0)


def _far_common(part_ref, qs_ref, cpl_ref, e_ref, u_ref, chunk_tail):
    cells = part_ref.shape[1]
    width = 64
    clusters = cells // width
    rank = cpl_ref.shape[1]
    npairs = qs_ref.shape[0]
    far = npairs // clusters

    def pair_body(pj, z):
        off = pl.multiple_of(pj * PAIR_CHUNK, PAIR_CHUNK)
        sl = pl.ds(off, PAIR_CHUNK)
        qs = qs_ref[sl, :].T
        qre = qs[:rank][None]
        qim = qs[rank:][None]
        cre = cpl_ref[0, :, :, sl]
        cim = cpl_ref[1, :, :, sl]
        zre = jnp.sum(cre * qre - cim * qim, axis=1)
        zim = jnp.sum(cre * qim + cim * qre, axis=1)
        seg = _div(_iota((PAIR_CHUNK, clusters), 0) + off, far) == _iota((PAIR_CHUNK, clusters), 1)
        return z + _xdot(jnp.concatenate([zre, zim], axis=0), seg.astype(BF16))

    z = lax.fori_loop(0, npairs // PAIR_CHUNK, pair_body, jnp.zeros((2 * rank, clusters), F32))
    z_split = _split3(z)

    def cell_body(ci, acc):
        off = pl.multiple_of(ci * CHUNK, CHUNK)
        sl = pl.ds(off, CHUNK)
        spread = _iota((clusters, CHUNK), 0) == _div(_iota((clusters, CHUNK), 1) + off, width)
        zz = _sdot(z_split, spread.astype(BF16))
        zre = zz[:rank]
        zim = zz[rank:]
        ere = e_ref[0, :, sl]
        eim = e_ref[1, :, sl]
        far_re = jnp.sum(ere * zre - eim * zim, axis=0, keepdims=True)
        far_im = jnp.sum(ere * zim + eim * zre, axis=0, keepdims=True)
        u = part_ref[:, sl] + jnp.concatenate([far_re, far_im], axis=0)
        u_ref[:, sl] = u
        return chunk_tail(u, off, sl, acc)

    return cell_body


def _far_proj_kernel(part_ref, qs_ref, cpl_ref, e_ref, c_ref, p_ref, rr_ref, u_ref, send_ref):
    cells = part_ref.shape[1]
    clusters = cells // 64
    rank2 = 2 * p_ref.shape[1]

    def tail(u, off, sl, q):
        pw = _weighted_proj(u, c_ref[:, sl], p_ref[0, :, sl], p_ref[1, :, sl])
        return q + _proj_chunk(pw, off, clusters, 64)

    body = _far_common(part_ref, qs_ref, cpl_ref, e_ref, u_ref, tail)
    q = lax.fori_loop(0, cells // CHUNK, body, jnp.zeros((rank2, clusters), F32))
    send_ref[...] = _pack(q, _rr_groups(rr_ref[...], send_ref.shape[1] // rank2))


def _far_grad_kernel(part_ref, qs_ref, cpl_ref, e_ref, bg_ref, u_ref, t_ref):
    cells = part_ref.shape[1]

    def tail(u, off, sl, acc):
        bg = bg_ref[:, sl]
        t_ref[:, sl] = bg[0:1] * u[0:1] + bg[1:2] * u[1:2]
        return acc

    body = _far_common(part_ref, qs_ref, cpl_ref, e_ref, u_ref, tail)
    lax.fori_loop(0, cells // CHUNK, body, 0)


def _call(kernel, outs, args, flops, name):
    leaves = outs if isinstance(outs, tuple) else (outs,)
    nbytes = sum(a.size * a.dtype.itemsize for a in args) + sum(
        o.size * jnp.dtype(o.dtype).itemsize for o in leaves
    )
    return pl.pallas_call(
        kernel,
        out_shape=outs,
        compiler_params=pltpu.CompilerParams(vmem_limit_bytes=VMEM_LIMIT),
        cost_estimate=pl.CostEstimate(flops=flops, bytes_accessed=nbytes, transcendentals=0),
        name=name,
    )(*args)


def _exchange(send, idx, devices, cap):
    total = send.size
    got = lax.all_to_all(send.reshape(devices, total // devices), "cells", 0, 0)
    got = got.reshape(devices * cap, total // (devices * cap))
    return got[idx]


def _exchange_all(send, devices, clusters, rank2, cap, groups, src_index):
    total = send.size
    got = lax.all_to_all(send.reshape(devices, total // devices), "cells", 0, 0)
    lanes = send.shape[1]
    got = got.reshape(devices, total // (devices * lanes), lanes)
    rr = got[:, -1, :cap]
    table = got[:, :-1, :].reshape(devices, rank2, clusters).transpose(1, 0, 2)
    return table.reshape(rank2, devices * clusters)[:, src_index].T, rr


def per_device(
    adj_source,
    contrast,
    background,
    near_blocks,
    near_list,
    proj_basis,
    expand_basis,
    coupling,
    far_owner,
    far_slot,
):
    devices = lax.axis_size("cells")
    clusters = near_list.shape[0]
    cells = contrast.shape[1]
    width = cells // clusters
    npairs = far_slot.shape[0]
    cap = 32

    src = adj_source[0]
    cst = contrast
    nb = near_blocks[0]
    pb = proj_basis[0]
    eb = expand_basis[0]
    cp = coupling[0]
    bg = background[0]

    me = lax.axis_index("cells")
    local_list = near_list - me * clusters
    nlc = jnp.repeat(local_list.T, width, axis=1)

    groups = 4
    src_index = far_owner[:, 0] * clusters + far_slot

    nsend = devices * cap
    rank2 = 2 * pb.shape[1]
    q_shape = jax.ShapeDtypeStruct((rank2, clusters), F32)
    field_shape = jax.ShapeDtypeStruct((2, cells), F32)

    first_shape = jax.ShapeDtypeStruct((devices * (clusters // groups + 1), groups * rank2), F32)
    idx, send = _call(
        _proj_pack_kernel,
        (jax.ShapeDtypeStruct((1, npairs), jnp.int32), first_shape),
        (src, cst, pb, far_owner.reshape(1, npairs), far_slot.reshape(1, npairs)),
        4 * rank2 * cells + 2 * devices * npairs * npairs,
        "proj_pack",
    )
    idx = idx.reshape(npairs)
    send_shape = jax.ShapeDtypeStruct((devices * cap // groups, groups * rank2), F32)
    field = src
    for step in range(ITERS):
        if step == 0:
            qs, rr = _exchange_all(send, devices, clusters, rank2, cap, groups, src_index)
        else:
            qs = _exchange(send, idx, devices, cap)
        part = _call(
            _near_kernel, field_shape, (field, cst, nb, nlc, src), 8 * nb.shape[1] * cells, "near"
        )
        if step < ITERS - 1:
            field, send = _call(
                _far_proj_kernel,
                (field_shape, send_shape),
                (part, qs, cp, eb, cst, pb, rr),
                8 * cp.size,
                "far_proj",
            )
        else:
            field, terms = _call(
                _far_grad_kernel,
                (field_shape, jax.ShapeDtypeStruct((1, cells), F32)),
                (part, qs, cp, eb, bg),
                8 * cp.size,
                "far_grad",
            )
    freqs = lax.axis_size("freq")
    mine = terms[0]
    got = [mine] + [
        lax.ppermute(mine, "freq", [(i, (i + k) % freqs) for i in range(freqs)])
        for k in range(1, freqs)
    ]
    stacked = jnp.stack(got)
    f = lax.axis_index("freq")
    total = stacked[(f - 0) % freqs]
    for src in range(1, freqs):
        total = total + stacked[(f - src) % freqs]
    return (field[None], total)


def solution(mesh):
    return jax.shard_map(
        per_device,
        mesh=mesh,
        in_specs=(
            P("freq", None, "cells"),
            P("freq", "cells"),
            P("freq", None, "cells"),
            P("freq", None, None, "cells"),
            P("cells", None),
            P("freq", None, None, "cells"),
            P("freq", None, None, "cells"),
            P("freq", None, None, None, "cells"),
            P("cells", None),
            P("cells"),
        ),
        out_specs=(P("freq", None, "cells"), P("cells")),
        check_vma=False,
    )
```

```python
import jax
import jax.numpy as jnp
from jax import lax
from jax.experimental import pallas as pl
from jax.experimental.pallas import tpu as pltpu
from jax.sharding import PartitionSpec as P

ITERS = 2
F32 = jnp.float32
BF16 = jnp.bfloat16
CHUNK = 4096
PAIR_CHUNK = 1024
VMEM_LIMIT = 56 * 1024 * 1024


def _split3(a):
    hi = a.astype(BF16)
    r = a - hi.astype(F32)
    mid = r.astype(BF16)
    lo = (r - mid.astype(F32)).astype(BF16)
    return jnp.concatenate([hi, mid, lo], axis=0)


def _sdot(split, onehot):
    m = split.shape[0] // 3
    r = jnp.dot(split, onehot, preferred_element_type=F32)
    return r[:m] + r[m : 2 * m] + r[2 * m :]


def _xdot(a, onehot):
    return _sdot(_split3(a), onehot)


def _iota(shape, dim):
    return lax.broadcasted_iota(jnp.int32, shape, dim)


def _div(x, d):
    return x >> (d.bit_length() - 1) if d & (d - 1) == 0 else x // d


def _mod(x, d):
    return x & (d - 1) if d & (d - 1) == 0 else x % d


def _weighted_proj(u, c, pre, pim):
    wre = u[0:1] * c
    wim = u[1:2] * c
    return jnp.concatenate([pre * wre - pim * wim, pre * wim + pim * wre], axis=0)


def _proj_chunk(pw, off, clusters, width):
    n = pw.shape[1]
    seg = _div(_iota((n, clusters), 0) + off, width) == _iota((n, clusters), 1)
    return _xdot(pw, seg.astype(BF16))


def _pack(q, rr):
    rank2, clusters = q.shape
    rows, groups = rr.shape
    wide = groups * clusters
    lane = _iota((rows, wide), 1)
    grp = _div(lane, clusters)
    want = rr[:, 0:1]
    for g in range(1, groups):
        want = jnp.where(grp == g, rr[:, g : g + 1], want)
    oh = (_mod(lane, clusters).astype(F32) == want).astype(BF16)
    tile = (_iota((clusters, wide), 0) == _mod(_iota((clusters, wide), 1), clusters)).astype(BF16)
    qw = _xdot(q, tile)
    qw = jnp.concatenate([qw] * groups, axis=0)
    keep = _div(_iota((groups * rank2, wide), 0), rank2) == _div(_iota((groups * rank2, wide), 1), clusters)
    qw = jnp.where(keep, qw, 0.0)
    r = lax.dot_general(oh, _split3(qw), (((1,), (1,)), ((), ())), preferred_element_type=F32)
    n = groups * rank2
    return r[:, :n] + r[:, n : 2 * n] + r[:, 2 * n :]


def _prep(or_ref, sr_ref, idx_ref, devices, cap):
    n = or_ref.shape[1]
    oht = _iota((devices, n), 0) == or_ref[...]
    upper = (_iota((n, n), 0) < _iota((n, n), 1)).astype(BF16)
    counts = jnp.dot(oht.astype(BF16), upper, preferred_element_type=F32)
    pos = jnp.sum(jnp.where(oht, counts, 0.0), axis=0, keepdims=True).astype(jnp.int32)
    idx_ref[...] = or_ref[...] * cap + pos
    pkt = (_iota((cap, n), 0) == pos).astype(BF16)
    ohs = jnp.where(oht, sr_ref[...].astype(F32), 0.0).astype(BF16)
    return lax.dot_general(ohs, pkt, (((1,), (1,)), ((), ())), preferred_element_type=F32)


def _proj_pack_kernel(u_ref, c_ref, p_ref, or_ref, sr_ref, idx_ref, send_ref):
    cells = u_ref.shape[1]
    clusters = cells // 64
    rank2 = 2 * p_ref.shape[1]
    lanes = send_ref.shape[1]
    nrow = rank2 * clusters // lanes
    block = nrow + 1
    devices = send_ref.shape[0] // block
    cap = 32
    req = _prep(or_ref, sr_ref, idx_ref, devices, cap)

    def body(ci, q):
        off = pl.multiple_of(ci * CHUNK, CHUNK)
        sl = pl.ds(off, CHUNK)
        pw = _weighted_proj(u_ref[:, sl], c_ref[:, sl], p_ref[0, :, sl], p_ref[1, :, sl])
        return q + _proj_chunk(pw, off, clusters, 64)

    q = lax.fori_loop(0, cells // CHUNK, body, jnp.zeros((rank2, clusters), F32))
    per = lanes // clusters
    hi = q.astype(BF16)
    r1 = q - hi.astype(F32)
    mid = r1.astype(BF16)
    lo = (r1 - mid.astype(F32)).astype(BF16)
    flat = jnp.zeros((nrow, lanes), F32)
    for h in range(per):
        sel = (_iota((nrow, rank2), 1) == _iota((nrow, rank2), 0) * per + h).astype(BF16)
        part = sum(jnp.dot(sel, x, preferred_element_type=F32) for x in (hi, mid, lo))
        place = (_iota((clusters, lanes), 1) == _iota((clusters, lanes), 0) + h * clusters)
        flat = flat + _xdot(part, place.astype(BF16))
    place = (_iota((cap, lanes), 0) == _iota((cap, lanes), 1)).astype(BF16)
    reqrow = jnp.dot(req.astype(BF16), place, preferred_element_type=F32)
    for e in range(devices):
        send_ref[pl.ds(e * block, nrow), :] = flat
        send_ref[pl.ds(e * block + nrow, 1), :] = reqrow[e : e + 1]


def _rr_groups(rr, groups):
    devices, cap = rr.shape
    per = cap // groups
    rows = devices * per
    rep = (_div(_iota((rows, devices), 0), per) == _iota((rows, devices), 1)).astype(BF16)
    wide = jnp.dot(rep, rr.astype(BF16), preferred_element_type=F32)
    keep = _div(_iota((rows, cap), 1), groups) == _mod(_iota((rows, cap), 0), per)
    fold = (_mod(_iota((cap, groups), 0), groups) == _iota((cap, groups), 1)).astype(BF16)
    return jnp.dot(jnp.where(keep, wide, 0.0).astype(BF16), fold, preferred_element_type=F32)


def _near_kernel(u_ref, c_ref, nb_ref, nlc_ref, base_ref, out_ref):
    cells = u_ref.shape[1]
    width = 64
    clusters = cells // width
    near = nlc_ref.shape[0]

    def wt_body(ci, acc):
        off = pl.multiple_of(ci * CHUNK, CHUNK)
        sl = pl.ds(off, CHUNK)
        w = u_ref[:, sl] * c_ref[:, sl]
        sel = _iota((width, CHUNK), 0) == _mod(_iota((width, CHUNK), 1) + off, width)
        wm = jnp.concatenate(
            [jnp.where(sel, w[0:1], 0.0), jnp.where(sel, w[1:2], 0.0)], axis=0
        )
        seg = _div(_iota((CHUNK, clusters), 0) + off, width) == _iota((CHUNK, clusters), 1)
        return acc + _xdot(wm, seg.astype(BF16))

    wt = lax.fori_loop(0, cells // CHUNK, wt_body, jnp.zeros((2 * width, clusters), F32))
    wt_split = _split3(wt)

    def near_body(ci, carry):
        off = pl.multiple_of(ci * CHUNK, CHUNK)
        sl = pl.ds(off, CHUNK)
        crow = _iota((clusters, CHUNK), 0)
        acc_re = jnp.zeros((1, CHUNK), F32)
        acc_im = jnp.zeros((1, CHUNK), F32)
        for k in range(near):
            m = (crow == nlc_ref[k : k + 1, sl]).astype(BF16)
            wk = _sdot(wt_split, m)
            wre = wk[:width]
            wim = wk[width:]
            nre = nb_ref[0, pl.ds(k * width, width), sl]
            nim = nb_ref[1, pl.ds(k * width, width), sl]
            acc_re = acc_re + jnp.sum(nre * wre - nim * wim, axis=0, keepdims=True)
            acc_im = acc_im + jnp.sum(nre * wim + nim * wre, axis=0, keepdims=True)
        out_ref[:, sl] = base_ref[:, sl] + jnp.concatenate([acc_re, acc_im], axis=0)
        return carry

    lax.fori_loop(0, cells // CHUNK, near_body, 0)


def _far_common(part_ref, qs_ref, cpl_ref, e_ref, u_ref, chunk_tail):
    cells = part_ref.shape[1]
    width = 64
    clusters = cells // width
    rank = cpl_ref.shape[1]
    npairs = qs_ref.shape[1]
    far = npairs // clusters

    def pair_body(pj, z):
        off = pl.multiple_of(pj * PAIR_CHUNK, PAIR_CHUNK)
        sl = pl.ds(off, PAIR_CHUNK)
        qs = qs_ref[:, sl]
        zre = jnp.zeros((rank, PAIR_CHUNK), F32)
        zim = jnp.zeros((rank, PAIR_CHUNK), F32)
        for i in range(rank):
            cre = cpl_ref[0, i, :, sl]
            cim = cpl_ref[1, i, :, sl]
            qre = qs[i : i + 1]
            qim = qs[rank + i : rank + i + 1]
            zre = zre + (cre * qre - cim * qim)
            zim = zim + (cre * qim + cim * qre)
        seg = _div(_iota((PAIR_CHUNK, clusters), 0) + off, far) == _iota((PAIR_CHUNK, clusters), 1)
        return z + _xdot(jnp.concatenate([zre, zim], axis=0), seg.astype(BF16))

    z = lax.fori_loop(0, npairs // PAIR_CHUNK, pair_body, jnp.zeros((2 * rank, clusters), F32))
    z_split = _split3(z)

    def cell_body(ci, acc):
        off = pl.multiple_of(ci * CHUNK, CHUNK)
        sl = pl.ds(off, CHUNK)
        spread = _iota((clusters, CHUNK), 0) == _div(_iota((clusters, CHUNK), 1) + off, width)
        zz = _sdot(z_split, spread.astype(BF16))
        zre = zz[:rank]
        zim = zz[rank:]
        ere = e_ref[0, :, sl]
        eim = e_ref[1, :, sl]
        far_re = jnp.sum(ere * zre - eim * zim, axis=0, keepdims=True)
        far_im = jnp.sum(ere * zim + eim * zre, axis=0, keepdims=True)
        u = part_ref[:, sl] + jnp.concatenate([far_re, far_im], axis=0)
        u_ref[:, sl] = u
        return chunk_tail(u, off, sl, acc)

    return cell_body


def _far_proj_kernel(part_ref, qs_ref, cpl_ref, e_ref, c_ref, p_ref, rr_ref, u_ref, send_ref):
    cells = part_ref.shape[1]
    clusters = cells // 64
    rank2 = 2 * p_ref.shape[1]

    def tail(u, off, sl, q):
        pw = _weighted_proj(u, c_ref[:, sl], p_ref[0, :, sl], p_ref[1, :, sl])
        return q + _proj_chunk(pw, off, clusters, 64)

    body = _far_common(part_ref, qs_ref, cpl_ref, e_ref, u_ref, tail)
    q = lax.fori_loop(0, cells // CHUNK, body, jnp.zeros((rank2, clusters), F32))
    send_ref[...] = _pack(q, _rr_groups(rr_ref[...], send_ref.shape[1] // rank2))


def _far_grad_kernel(part_ref, qs_ref, cpl_ref, e_ref, bg_ref, u_ref, t_ref):
    cells = part_ref.shape[1]

    def tail(u, off, sl, acc):
        bg = bg_ref[:, sl]
        t_ref[:, sl] = bg[0:1] * u[0:1] + bg[1:2] * u[1:2]
        return acc

    body = _far_common(part_ref, qs_ref, cpl_ref, e_ref, u_ref, tail)
    lax.fori_loop(0, cells // CHUNK, body, 0)


def _call(kernel, outs, args, flops, name):
    leaves = outs if isinstance(outs, tuple) else (outs,)
    nbytes = sum(a.size * a.dtype.itemsize for a in args) + sum(
        o.size * jnp.dtype(o.dtype).itemsize for o in leaves
    )
    return pl.pallas_call(
        kernel,
        out_shape=outs,
        compiler_params=pltpu.CompilerParams(vmem_limit_bytes=VMEM_LIMIT),
        cost_estimate=pl.CostEstimate(flops=flops, bytes_accessed=nbytes, transcendentals=0),
        name=name,
    )(*args)


def _exchange(send, idx, devices, cap):
    total = send.size
    got = lax.all_to_all(send.reshape(devices, total // devices), "cells", 0, 0)
    got = got.reshape(devices * cap, total // (devices * cap))
    return got[idx].T


def _exchange_all(send, devices, clusters, rank2, cap, groups, src_index):
    total = send.size
    got = lax.all_to_all(send.reshape(devices, total // devices), "cells", 0, 0)
    lanes = send.shape[1]
    got = got.reshape(devices, total // (devices * lanes), lanes)
    rr = got[:, -1, :cap]
    table = got[:, :-1, :].reshape(devices, rank2, clusters).transpose(1, 0, 2)
    return table.reshape(rank2, devices * clusters)[:, src_index], rr


def per_device(
    adj_source,
    contrast,
    background,
    near_blocks,
    near_list,
    proj_basis,
    expand_basis,
    coupling,
    far_owner,
    far_slot,
):
    devices = lax.axis_size("cells")
    clusters = near_list.shape[0]
    cells = contrast.shape[1]
    width = cells // clusters
    npairs = far_slot.shape[0]
    cap = 32

    src = adj_source[0]
    cst = contrast
    nb = near_blocks[0]
    pb = proj_basis[0]
    eb = expand_basis[0]
    cp = jnp.transpose(coupling[0], (0, 2, 1, 3))
    bg = background[0]

    me = lax.axis_index("cells")
    local_list = near_list - me * clusters
    nlc = jnp.repeat(local_list.T, width, axis=1)

    groups = 4
    src_index = far_owner[:, 0] * clusters + far_slot

    nsend = devices * cap
    rank2 = 2 * pb.shape[1]
    q_shape = jax.ShapeDtypeStruct((rank2, clusters), F32)
    field_shape = jax.ShapeDtypeStruct((2, cells), F32)

    first_shape = jax.ShapeDtypeStruct((devices * (clusters // groups + 1), groups * rank2), F32)
    idx, send = _call(
        _proj_pack_kernel,
        (jax.ShapeDtypeStruct((1, npairs), jnp.int32), first_shape),
        (src, cst, pb, far_owner.reshape(1, npairs), far_slot.reshape(1, npairs)),
        4 * rank2 * cells + 2 * devices * npairs * npairs,
        "proj_pack",
    )
    idx = idx.reshape(npairs)
    send_shape = jax.ShapeDtypeStruct((devices * cap // groups, groups * rank2), F32)
    field = src
    for step in range(ITERS):
        if step == 0:
            qs, rr = _exchange_all(send, devices, clusters, rank2, cap, groups, src_index)
        else:
            qs = _exchange(send, idx, devices, cap)
        part = _call(
            _near_kernel, field_shape, (field, cst, nb, nlc, src), 8 * nb.shape[1] * cells, "near"
        )
        if step < ITERS - 1:
            field, send = _call(
                _far_proj_kernel,
                (field_shape, send_shape),
                (part, qs, cp, eb, cst, pb, rr),
                8 * cp.size,
                "far_proj",
            )
        else:
            field, terms = _call(
                _far_grad_kernel,
                (field_shape, jax.ShapeDtypeStruct((1, cells), F32)),
                (part, qs, cp, eb, bg),
                8 * cp.size,
                "far_grad",
            )
    freqs = lax.axis_size("freq")
    mine = terms[0]
    got = [mine] + [
        lax.ppermute(mine, "freq", [(i, (i + k) % freqs) for i in range(freqs)])
        for k in range(1, freqs)
    ]
    stacked = jnp.stack(got)
    f = lax.axis_index("freq")
    total = stacked[(f - 0) % freqs]
    for src in range(1, freqs):
        total = total + stacked[(f - src) % freqs]
    return (field[None], total)


def solution(mesh):
    return jax.shard_map(
        per_device,
        mesh=mesh,
        in_specs=(
            P("freq", None, "cells"),
            P("freq", "cells"),
            P("freq", None, "cells"),
            P("freq", None, None, "cells"),
            P("cells", None),
            P("freq", None, None, "cells"),
            P("freq", None, None, "cells"),
            P("freq", None, None, None, "cells"),
            P("cells", None),
            P("cells"),
        ),
        out_specs=(P("freq", None, "cells"), P("cells")),
        check_vma=False,
    )
```

```python
import jax
import jax.numpy as jnp
from jax import lax
from jax.experimental import pallas as pl
from jax.experimental.pallas import tpu as pltpu
from jax.sharding import PartitionSpec as P

ITERS = 2
F32 = jnp.float32
BF16 = jnp.bfloat16
CHUNK = 4096
PAIR_CHUNK = 1024
VMEM_LIMIT = 56 * 1024 * 1024


def _split3(a):
    hi = a.astype(BF16)
    r = a - hi.astype(F32)
    mid = r.astype(BF16)
    lo = (r - mid.astype(F32)).astype(BF16)
    return jnp.concatenate([hi, mid, lo], axis=0)


def _sdot(split, onehot):
    m = split.shape[0] // 3
    r = jnp.dot(split, onehot, preferred_element_type=F32)
    return r[:m] + r[m : 2 * m] + r[2 * m :]


def _xdot(a, onehot):
    return _sdot(_split3(a), onehot)


def _iota(shape, dim):
    return lax.broadcasted_iota(jnp.int32, shape, dim)


def _div(x, d):
    return x >> (d.bit_length() - 1) if d & (d - 1) == 0 else x // d


def _mod(x, d):
    return x & (d - 1) if d & (d - 1) == 0 else x % d


def _weighted_proj(u, c, pre, pim):
    wre = u[0:1] * c
    wim = u[1:2] * c
    return jnp.concatenate([pre * wre - pim * wim, pre * wim + pim * wre], axis=0)


def _proj_chunk(pw, off, clusters, width):
    n = pw.shape[1]
    seg = _div(_iota((n, clusters), 0) + off, width) == _iota((n, clusters), 1)
    return _xdot(pw, seg.astype(BF16))


def _pack(q, rr):
    rank2, clusters = q.shape
    rows, groups = rr.shape
    wide = groups * clusters
    lane = _iota((rows, wide), 1)
    grp = _div(lane, clusters)
    want = rr[:, 0:1]
    for g in range(1, groups):
        want = jnp.where(grp == g, rr[:, g : g + 1], want)
    oh = (_mod(lane, clusters).astype(F32) == want).astype(BF16)
    tile = (_iota((clusters, wide), 0) == _mod(_iota((clusters, wide), 1), clusters)).astype(BF16)
    qw = _xdot(q, tile)
    qw = jnp.concatenate([qw] * groups, axis=0)
    keep = _div(_iota((groups * rank2, wide), 0), rank2) == _div(_iota((groups * rank2, wide), 1), clusters)
    qw = jnp.where(keep, qw, 0.0)
    r = lax.dot_general(oh, _split3(qw), (((1,), (1,)), ((), ())), preferred_element_type=F32)
    n = groups * rank2
    return r[:, :n] + r[:, n : 2 * n] + r[:, 2 * n :]


def _prep(or_ref, sr_ref, idx_ref, devices, cap):
    n = or_ref.shape[1]
    oht = _iota((devices, n), 0) == or_ref[...]
    upper = (_iota((n, n), 0) < _iota((n, n), 1)).astype(BF16)
    counts = jnp.dot(oht.astype(BF16), upper, preferred_element_type=F32)
    pos = jnp.sum(jnp.where(oht, counts, 0.0), axis=0, keepdims=True).astype(jnp.int32)
    idx_ref[...] = or_ref[...] * cap + pos
    pkt = (_iota((cap, n), 0) == pos).astype(BF16)
    ohs = jnp.where(oht, sr_ref[...].astype(F32), 0.0).astype(BF16)
    return lax.dot_general(ohs, pkt, (((1,), (1,)), ((), ())), preferred_element_type=F32)


def _proj_pack_kernel(u_ref, c_ref, p_ref, or_ref, sr_ref, idx_ref, send_ref):
    cells = u_ref.shape[1]
    clusters = cells // 64
    rank2 = 2 * p_ref.shape[1]
    lanes = send_ref.shape[1]
    nrow = rank2 * clusters // lanes
    block = nrow + 1
    devices = send_ref.shape[0] // block
    cap = 32
    req = _prep(or_ref, sr_ref, idx_ref, devices, cap)

    def body(ci, q):
        off = pl.multiple_of(ci * CHUNK, CHUNK)
        sl = pl.ds(off, CHUNK)
        pw = _weighted_proj(u_ref[:, sl], c_ref[:, sl], p_ref[0, :, sl], p_ref[1, :, sl])
        return q + _proj_chunk(pw, off, clusters, 64)

    q = lax.fori_loop(0, cells // CHUNK, body, jnp.zeros((rank2, clusters), F32))
    per = lanes // clusters
    hi = q.astype(BF16)
    r1 = q - hi.astype(F32)
    mid = r1.astype(BF16)
    lo = (r1 - mid.astype(F32)).astype(BF16)
    flat = jnp.zeros((nrow, lanes), F32)
    for h in range(per):
        sel = (_iota((nrow, rank2), 1) == _iota((nrow, rank2), 0) * per + h).astype(BF16)
        part = sum(jnp.dot(sel, x, preferred_element_type=F32) for x in (hi, mid, lo))
        place = (_iota((clusters, lanes), 1) == _iota((clusters, lanes), 0) + h * clusters)
        flat = flat + _xdot(part, place.astype(BF16))
    place = (_iota((cap, lanes), 0) == _iota((cap, lanes), 1)).astype(BF16)
    reqrow = jnp.dot(req.astype(BF16), place, preferred_element_type=F32)
    for e in range(devices):
        send_ref[pl.ds(e * block, nrow), :] = flat
        send_ref[pl.ds(e * block + nrow, 1), :] = reqrow[e : e + 1]


def _rr_groups(rr, groups):
    devices, cap = rr.shape
    per = cap // groups
    rows = devices * per
    rep = (_div(_iota((rows, devices), 0), per) == _iota((rows, devices), 1)).astype(BF16)
    wide = jnp.dot(rep, rr.astype(BF16), preferred_element_type=F32)
    keep = _div(_iota((rows, cap), 1), groups) == _mod(_iota((rows, cap), 0), per)
    fold = (_mod(_iota((cap, groups), 0), groups) == _iota((cap, groups), 1)).astype(BF16)
    return jnp.dot(jnp.where(keep, wide, 0.0).astype(BF16), fold, preferred_element_type=F32)


def _near_kernel(u_ref, c_ref, nb_ref, nlc_ref, base_ref, out_ref):
    cells = u_ref.shape[1]
    width = 64
    clusters = cells // width
    near = nlc_ref.shape[0]

    def wt_body(ci, acc):
        off = pl.multiple_of(ci * CHUNK, CHUNK)
        sl = pl.ds(off, CHUNK)
        w = u_ref[:, sl] * c_ref[:, sl]
        sel = _iota((width, CHUNK), 0) == _mod(_iota((width, CHUNK), 1) + off, width)
        wm = jnp.concatenate(
            [jnp.where(sel, w[0:1], 0.0), jnp.where(sel, w[1:2], 0.0)], axis=0
        )
        seg = _div(_iota((CHUNK, clusters), 0) + off, width) == _iota((CHUNK, clusters), 1)
        return acc + _xdot(wm, seg.astype(BF16))

    wt = lax.fori_loop(0, cells // CHUNK, wt_body, jnp.zeros((2 * width, clusters), F32))
    wt_split = _split3(wt)

    def near_body(ci, carry):
        off = pl.multiple_of(ci * CHUNK, CHUNK)
        sl = pl.ds(off, CHUNK)
        crow = _iota((clusters, CHUNK), 0)
        acc_re = jnp.zeros((1, CHUNK), F32)
        acc_im = jnp.zeros((1, CHUNK), F32)
        for k in range(near):
            m = (crow == nlc_ref[k : k + 1, sl]).astype(BF16)
            wk = _sdot(wt_split, m)
            wre = wk[:width]
            wim = wk[width:]
            nre = nb_ref[0, pl.ds(k * width, width), sl]
            nim = nb_ref[1, pl.ds(k * width, width), sl]
            acc_re = acc_re + jnp.sum(nre * wre - nim * wim, axis=0, keepdims=True)
            acc_im = acc_im + jnp.sum(nre * wim + nim * wre, axis=0, keepdims=True)
        out_ref[:, sl] = base_ref[:, sl] + jnp.concatenate([acc_re, acc_im], axis=0)
        return carry

    lax.fori_loop(0, cells // CHUNK, near_body, 0)


def _far_common(part_ref, qs_ref, cpl_ref, e_ref, u_ref, chunk_tail):
    cells = part_ref.shape[1]
    width = 64
    clusters = cells // width
    rank = cpl_ref.shape[1]
    npairs = qs_ref.shape[1]
    far = npairs // clusters

    def pair_body(pj, z):
        off = pl.multiple_of(pj * PAIR_CHUNK, PAIR_CHUNK)
        sl = pl.ds(off, PAIR_CHUNK)
        qs = qs_ref[:, sl]
        qre = qs[:rank][None]
        qim = qs[rank:][None]
        cre = cpl_ref[0, :, :, sl]
        cim = cpl_ref[1, :, :, sl]
        zre = jnp.sum(cre * qre - cim * qim, axis=1)
        zim = jnp.sum(cre * qim + cim * qre, axis=1)
        seg = _div(_iota((PAIR_CHUNK, clusters), 0) + off, far) == _iota((PAIR_CHUNK, clusters), 1)
        return z + _xdot(jnp.concatenate([zre, zim], axis=0), seg.astype(BF16))

    z = lax.fori_loop(0, npairs // PAIR_CHUNK, pair_body, jnp.zeros((2 * rank, clusters), F32))
    z_split = _split3(z)

    def cell_body(ci, acc):
        off = pl.multiple_of(ci * CHUNK, CHUNK)
        sl = pl.ds(off, CHUNK)
        spread = _iota((clusters, CHUNK), 0) == _div(_iota((clusters, CHUNK), 1) + off, width)
        zz = _sdot(z_split, spread.astype(BF16))
        zre = zz[:rank]
        zim = zz[rank:]
        ere = e_ref[0, :, sl]
        eim = e_ref[1, :, sl]
        far_re = jnp.sum(ere * zre - eim * zim, axis=0, keepdims=True)
        far_im = jnp.sum(ere * zim + eim * zre, axis=0, keepdims=True)
        u = part_ref[:, sl] + jnp.concatenate([far_re, far_im], axis=0)
        u_ref[:, sl] = u
        return chunk_tail(u, off, sl, acc)

    return cell_body


def _far_proj_kernel(part_ref, qs_ref, cpl_ref, e_ref, c_ref, p_ref, rr_ref, u_ref, send_ref):
    cells = part_ref.shape[1]
    clusters = cells // 64
    rank2 = 2 * p_ref.shape[1]

    def tail(u, off, sl, q):
        pw = _weighted_proj(u, c_ref[:, sl], p_ref[0, :, sl], p_ref[1, :, sl])
        return q + _proj_chunk(pw, off, clusters, 64)

    body = _far_common(part_ref, qs_ref, cpl_ref, e_ref, u_ref, tail)
    q = lax.fori_loop(0, cells // CHUNK, body, jnp.zeros((rank2, clusters), F32))
    send_ref[...] = _pack(q, _rr_groups(rr_ref[...], send_ref.shape[1] // rank2))


def _far_grad_kernel(part_ref, qs_ref, cpl_ref, e_ref, bg_ref, u_ref, t_ref):
    cells = part_ref.shape[1]

    def tail(u, off, sl, acc):
        bg = bg_ref[:, sl]
        t_ref[:, sl] = bg[0:1] * u[0:1] + bg[1:2] * u[1:2]
        return acc

    body = _far_common(part_ref, qs_ref, cpl_ref, e_ref, u_ref, tail)
    lax.fori_loop(0, cells // CHUNK, body, 0)


def _call(kernel, outs, args, flops, name):
    leaves = outs if isinstance(outs, tuple) else (outs,)
    nbytes = sum(a.size * a.dtype.itemsize for a in args) + sum(
        o.size * jnp.dtype(o.dtype).itemsize for o in leaves
    )
    return pl.pallas_call(
        kernel,
        out_shape=outs,
        compiler_params=pltpu.CompilerParams(vmem_limit_bytes=VMEM_LIMIT),
        cost_estimate=pl.CostEstimate(flops=flops, bytes_accessed=nbytes, transcendentals=0),
        name=name,
    )(*args)


def _exchange(send, idx, devices, cap):
    total = send.size
    got = lax.all_to_all(send.reshape(devices, total // devices), "cells", 0, 0)
    got = got.reshape(devices * cap, total // (devices * cap))
    return got[idx].T


def _exchange_all(send, devices, clusters, rank2, cap, groups, src_index):
    total = send.size
    got = lax.all_to_all(send.reshape(devices, total // devices), "cells", 0, 0)
    lanes = send.shape[1]
    got = got.reshape(devices, total // (devices * lanes), lanes)
    rr = got[:, -1, :cap]
    table = got[:, :-1, :].reshape(devices, rank2, clusters).transpose(1, 0, 2)
    return table.reshape(rank2, devices * clusters)[:, src_index], rr


def per_device(
    adj_source,
    contrast,
    background,
    near_blocks,
    near_list,
    proj_basis,
    expand_basis,
    coupling,
    far_owner,
    far_slot,
):
    devices = lax.axis_size("cells")
    clusters = near_list.shape[0]
    cells = contrast.shape[1]
    width = cells // clusters
    npairs = far_slot.shape[0]
    cap = 32

    src = adj_source[0]
    cst = contrast
    nb = near_blocks[0]
    pb = proj_basis[0]
    eb = expand_basis[0]
    cp = coupling[0]
    bg = background[0]

    me = lax.axis_index("cells")
    local_list = near_list - me * clusters
    nlc = jnp.repeat(local_list.T, width, axis=1)

    groups = 4
    src_index = far_owner[:, 0] * clusters + far_slot

    nsend = devices * cap
    rank2 = 2 * pb.shape[1]
    q_shape = jax.ShapeDtypeStruct((rank2, clusters), F32)
    field_shape = jax.ShapeDtypeStruct((2, cells), F32)

    first_shape = jax.ShapeDtypeStruct((devices * (clusters // groups + 1), groups * rank2), F32)
    idx, send = _call(
        _proj_pack_kernel,
        (jax.ShapeDtypeStruct((1, npairs), jnp.int32), first_shape),
        (src, cst, pb, far_owner.reshape(1, npairs), far_slot.reshape(1, npairs)),
        4 * rank2 * cells + 2 * devices * npairs * npairs,
        "proj_pack",
    )
    idx = idx.reshape(npairs)
    send_shape = jax.ShapeDtypeStruct((devices * cap // groups, groups * rank2), F32)
    field = src
    for step in range(ITERS):
        if step == 0:
            qs, rr = _exchange_all(send, devices, clusters, rank2, cap, groups, src_index)
        else:
            qs = _exchange(send, idx, devices, cap)
        part = _call(
            _near_kernel, field_shape, (field, cst, nb, nlc, src), 8 * nb.shape[1] * cells, "near"
        )
        if step < ITERS - 1:
            field, send = _call(
                _far_proj_kernel,
                (field_shape, send_shape),
                (part, qs, cp, eb, cst, pb, rr),
                8 * cp.size,
                "far_proj",
            )
        else:
            field, terms = _call(
                _far_grad_kernel,
                (field_shape, jax.ShapeDtypeStruct((1, cells), F32)),
                (part, qs, cp, eb, bg),
                8 * cp.size,
                "far_grad",
            )
    freqs = lax.axis_size("freq")
    mine = terms[0]
    got = [lax.ppermute(mine, "freq", [(i, i ^ k) for i in range(freqs)]) for k in range(1, freqs)]
    total = (mine + got[0]) + (got[1] + got[2])
    return (field[None], total)


def solution(mesh):
    return jax.shard_map(
        per_device,
        mesh=mesh,
        in_specs=(
            P("freq", None, "cells"),
            P("freq", "cells"),
            P("freq", None, "cells"),
            P("freq", None, None, "cells"),
            P("cells", None),
            P("freq", None, None, "cells"),
            P("freq", None, None, "cells"),
            P("freq", None, None, None, "cells"),
            P("cells", None),
            P("cells"),
        ),
        out_specs=(P("freq", None, "cells"), P("cells")),
        check_vma=False,
    )
```
